32 devices in a mesh: half: 2 (over x), row: 4 (over z), col: 4 (over y, core).
Axes of the slice: x: 2, y: 2, z: 4, core: 2. Of those that a mesh axis runs over, the one named last changes fastest.
Arguments:
- child_fronts: float32 [2, 6144, 6144], P('half', 'row', 'col'), may hold values from -1 to 40, as said below
- child_maps: int32 [2, 40], replicated, may hold values from 0 to 63, as said below
- parent_own: float32 [8192, 8192], P(('half', 'row'), 'col'), may hold values from -1 to 40, as said below
Outputs:
- child_factored: float32 [2, 6144, 6144], P('half', 'row', 'col')
- parent_factored: float32 [8192, 8192], P(('half', 'row'), 'col')
The draws below stay inside these ranges and needn't reach their ends.
Inputs may be any that keep to these rules, and one draw needn't show every extreme that they name: child_fronts[h] is symmetric and positive definite. parent_own in logical order is symmetric and positive definite. child_maps[h, u] equals u + 1024 / 128 modulo 16; among the update tiles of one child with the same residue it increases with u.
All inputs are finite; a program needn't handle non-finite values.
Results may differ from the reference program's by a relative error of at most 0.0001.
Values sent between devices are 32-bit elements; how exact they have to be, the bound alone decides.
No kernel may reach another device: no remote copies, remote signals or barrier semaphores. Data moves between devices by JAX's collectives and lax.ppermute only.
A program may use at most 192 MiB of HBM per device.

```python
import math
import jax
import jax.numpy as jnp
from jax import lax

TILE = 128
CHILD_ORDER = 6144
CHILD_PIVOTS = 1024
CYCLE = 16
PARENT_ORDER = 8192
PARENT_PIVOTS = 128
GRID = 4
UPD_TILES = 40


def symmetric_draw(key, count, matrix_order):
    entry_key, diag_key, place_key, scale_key = jax.random.split(key, 4)
    raw_values = jax.random.truncated_normal(entry_key, -4.0, 4.0, (count, matrix_order, matrix_order), jnp.float32)
    place_span = matrix_order / 2.0
    row_scales = jnp.exp(jax.random.uniform(scale_key, (count, matrix_order), jnp.float32, 0.0, 0.0))
    mixed = (raw_values + jnp.swapaxes(raw_values, 1, 2)) * math.sqrt(0.5) / math.sqrt(matrix_order)
    places = jax.random.uniform(place_key, (count, matrix_order), jnp.float32, 0.0, place_span)
    coupling = 3.0 * jnp.exp(-jnp.abs(places[:, :, None] - places[:, None, :]))
    diag_values = jnp.exp(jax.random.uniform(diag_key, (count, matrix_order), jnp.float32, math.log(2.5), math.log(5.5)))
    row_ids = lax.broadcasted_iota(jnp.int32, (matrix_order, matrix_order), 0)
    col_ids = lax.broadcasted_iota(jnp.int32, (matrix_order, matrix_order), 1)
    core = coupling + mixed + jnp.where((row_ids == col_ids)[None], diag_values[:, :, None], 0.0)
    return row_scales[:, :, None] * core * row_scales[:, None, :]


def stored_index_drawn(matrix_order, groups):
    positions = jnp.arange(matrix_order, dtype=jnp.int32)
    per_group = matrix_order // TILE // groups
    stored_tile = positions // TILE
    logical_tile = stored_tile % per_group * groups + stored_tile // per_group
    return logical_tile * TILE + positions % TILE


def draw_child_fronts(key, part):
    return symmetric_draw(jax.random.fold_in(key, 11), 2, CHILD_ORDER)


def draw_parent_own(key, part):
    logical = symmetric_draw(jax.random.fold_in(key, 23), 1, PARENT_ORDER)[0]
    row_index = stored_index_drawn(PARENT_ORDER, 2 * GRID)
    col_index = stored_index_drawn(PARENT_ORDER, GRID)
    return jnp.take(jnp.take(logical, row_index, axis=0), col_index, axis=1)


def draw_child_maps(key, part):
    base_key = jax.random.fold_in(key, 37)
    pivot_tiles = CHILD_PIVOTS // TILE
    slot_total = PARENT_ORDER // TILE // CYCLE
    class_ids = jnp.arange(CYCLE, dtype=jnp.int32)
    class_count = (UPD_TILES - class_ids + CYCLE - 1) // CYCLE
    skip_slots = jax.random.randint(base_key, (2, CYCLE), 0, class_count[None, :] + 1)
    first_class = (CYCLE - pivot_tiles % CYCLE) % CYCLE
    last_class = (2 * CYCLE - 1 - pivot_tiles % CYCLE) % CYCLE
    skip_slots = skip_slots.at[0, first_class].set(class_count[first_class]).at[1, last_class].set(0)
    update_tiles = jnp.arange(UPD_TILES, dtype=jnp.int32)
    base_class = update_tiles % CYCLE
    residue = (base_class + pivot_tiles) % CYCLE
    rank_index = update_tiles // CYCLE
    chosen = skip_slots[:, base_class]
    spare = (slot_total - class_count[base_class])[None, :]
    slot_index = rank_index[None, :] + (rank_index[None, :] >= chosen).astype(jnp.int32) * spare
    return residue[None, :] + CYCLE * slot_index


def setup_inputs(seed: int = 0) -> dict:
    arg_keys = jax.random.split(jax.random.key(seed), 4)
    child_fronts = draw_child_fronts(jax.random.fold_in(arg_keys[3], 71), 0)
    child_maps = draw_child_maps(jax.random.fold_in(arg_keys[3], 71), 0)
    parent_own = draw_parent_own(jax.random.fold_in(arg_keys[3], 71), 0)
    return {"child_fronts": child_fronts, "child_maps": child_maps, "parent_own": parent_own}


def stored_index(matrix_order, groups):
    positions = jnp.arange(matrix_order, dtype=jnp.int32)
    per_group = matrix_order // TILE // groups
    stored_tile = positions // TILE
    logical_tile = stored_tile % per_group * groups + stored_tile // per_group
    return logical_tile * TILE + positions % TILE

def logical_position(matrix_order, groups):
    indices = jnp.arange(matrix_order, dtype=jnp.int32)
    per_group = matrix_order // TILE // groups
    logical_tile = indices // TILE
    stored_tile = logical_tile % groups * per_group + logical_tile // groups
    return stored_tile * TILE + indices % TILE

def reorder(matrix, row_index, col_index):
    return jnp.take(jnp.take(matrix, row_index, axis=0), col_index, axis=1)

def partial_factor(matrix, pivots):
    matrix_order = matrix.shape[0]
    for pivot_tile in range(pivots // TILE):
        start_row = pivot_tile * TILE
        finish = start_row + TILE
        diag_factor = jnp.linalg.cholesky(matrix[start_row:finish, start_row:finish])
        below_block = matrix[finish:, start_row:finish]
        solved = jax.scipy.linalg.solve_triangular(diag_factor, below_block.T, lower=True).T
        update = jnp.dot(solved.astype(jnp.float32), solved.T.astype(jnp.float32), precision=lax.Precision.HIGHEST, preferred_element_type=jnp.float32)
        matrix = matrix.at[finish:, finish:].add(-update)
        matrix = matrix.at[start_row:finish, start_row:finish].set(jnp.tril(diag_factor))
        matrix = matrix.at[finish:, start_row:finish].set(solved)
        matrix = matrix.at[start_row:finish, finish:].set(jnp.zeros((TILE, matrix_order - finish), jnp.float32))
    return matrix

def reference(child_fronts, child_maps, parent_own):
    child_pos = logical_position(CHILD_ORDER, GRID)
    child_store = stored_index(CHILD_ORDER, GRID)
    parent_total = reorder(parent_own, logical_position(PARENT_ORDER, 2 * GRID), logical_position(PARENT_ORDER, GRID))
    within = jnp.arange(TILE, dtype=jnp.int32)
    outputs = []
    for child_index in range(2):
        factored = partial_factor(reorder(child_fronts[child_index], child_pos, child_pos), CHILD_PIVOTS)
        outputs.append(reorder(factored, child_store, child_store))
        targets = (child_maps[child_index][:, None] * TILE + within[None, :]).reshape(-1)
        parent_total = parent_total.at[targets[:, None], targets[None, :]].add(factored[CHILD_PIVOTS:, CHILD_PIVOTS:])
    parent_done = partial_factor(parent_total, PARENT_PIVOTS)
    parent_out = reorder(parent_done, stored_index(PARENT_ORDER, 2 * GRID), stored_index(PARENT_ORDER, GRID))
    return (jnp.stack(outputs), parent_out)
```

```python
import jax
import jax.numpy as jnp
from jax import lax
from jax.sharding import PartitionSpec as P

TILE = 128
CHILD_PIVOTS = 1024
PARENT_PIVOTS = 128


def spread(shard, axis, root):
    mine = lax.axis_index(axis) == root
    return lax.psum(jnp.where(mine, shard, jnp.zeros_like(shard)), axis)


def from_partner(shard, axis, distance):
    return lax.ppermute(shard, axis, [(i, i ^ 1 << distance) for i in range(lax.axis_size(axis))])


def factor_front(
    front_work,
    pivot_count,
    row_groups,
    col_groups,
    my_row,
    my_col,
    fetch_panel,
    fetch_diag,
    fetch_across,
):
    row_count, col_count = front_work.shape
    row_tiles = jnp.arange(row_count, dtype=jnp.int32) // TILE * row_groups + my_row
    col_tiles = jnp.arange(col_count, dtype=jnp.int32) // TILE * col_groups + my_col

    def one_step(pivot_tile, current):
        row_slot = pivot_tile // row_groups
        col_slot = pivot_tile // col_groups
        column = lax.dynamic_slice_in_dim(current, col_slot * TILE, TILE, 1)
        col_panel = fetch_panel(column, pivot_tile)
        diag_block = fetch_diag(current, col_panel, pivot_tile, row_slot, col_slot)
        diag_factor = jnp.linalg.cholesky(diag_block)
        solved_panel = jax.scipy.linalg.solve_triangular(diag_factor, col_panel.T, lower=True).T
        across_panel = fetch_across(solved_panel)
        rows_after = (row_tiles > pivot_tile)[:, None]
        cols_after = (col_tiles > pivot_tile)[:, None]
        left_factor = jnp.where(rows_after, solved_panel, 0.0)
        right_factor = jnp.where(cols_after, across_panel, 0.0)
        current = current - jnp.dot(
            left_factor,
            right_factor.T,
            precision=lax.Precision.HIGHEST,
            preferred_element_type=jnp.float32,
        )
        pivot_rows = lax.dynamic_slice_in_dim(current, row_slot * TILE, TILE, 0)
        row_owner = my_row == pivot_tile % row_groups
        pivot_rows = jnp.where(row_owner & (col_tiles > pivot_tile)[None, :], 0.0, pivot_rows)
        current = lax.dynamic_update_slice_in_dim(current, pivot_rows, row_slot * TILE, 0)
        diag_rows = jnp.tile(jnp.tril(diag_factor), (row_count // TILE, 1))
        new_column = jnp.where(
            rows_after, solved_panel, jnp.where((row_tiles == pivot_tile)[:, None], diag_rows, 0.0)
        )
        old_column = lax.dynamic_slice_in_dim(current, col_slot * TILE, TILE, 1)
        new_column = jnp.where(my_col == pivot_tile % col_groups, new_column, old_column)
        return lax.dynamic_update_slice_in_dim(current, new_column, col_slot * TILE, 1)

    return lax.fori_loop(0, pivot_count // TILE, one_step, front_work)


def pivot_order(pieces, slot_count, tile_count):
    group_count, rest = pieces.shape[0], pieces.shape[2:]
    shaped = pieces.reshape((group_count, slot_count, TILE) + rest)
    shaped = jnp.moveaxis(shaped, 0, 1).reshape((slot_count * group_count * TILE,) + rest)
    return shaped[: tile_count * TILE]


def factor_child(front_work, pivot_count, grid_size, my_row, my_col):
    local_count = front_work.shape[0]
    tile_count = pivot_count // TILE
    slot_count = -(-tile_count // grid_size)
    width = slot_count * TILE
    col_pieces = lax.all_gather(front_work[:, :width].T, "col", axis=0)
    panel_rows = pivot_order(col_pieces, slot_count, tile_count)
    row_pieces = lax.all_gather(front_work[:width, :], "row", axis=0)
    panel_cols = pivot_order(row_pieces, slot_count, tile_count)
    diag_pieces = lax.all_gather(panel_rows[:, :width].T, "row", axis=0)
    diag_block = pivot_order(diag_pieces, slot_count, tile_count)
    diag_factor = jnp.tril(jnp.linalg.cholesky(diag_block))
    both = jnp.concatenate([panel_rows, panel_cols], axis=1)
    solved = jax.scipy.linalg.solve_triangular(diag_factor, both, lower=True)
    solved_rows = solved[:, :local_count].T
    solved_cols = solved[:, local_count:].T
    within = jnp.arange(local_count, dtype=jnp.int32)
    row_index = within // TILE * grid_size * TILE + my_row * TILE + within % TILE
    col_index = within // TILE * grid_size * TILE + my_col * TILE + within % TILE
    rows_after = (row_index >= pivot_count)[:, None]
    cols_after = (col_index >= pivot_count)[None, :]
    update = jnp.dot(
        jnp.where(rows_after, solved_rows, 0.0),
        jnp.where(cols_after.T, solved_cols, 0.0).T,
        precision=lax.Precision.HIGHEST,
        preferred_element_type=jnp.float32,
    )
    diag_rows = jnp.take(diag_factor, jnp.minimum(row_index, pivot_count - 1), axis=0)
    full_rows = jnp.where(rows_after, solved_rows, diag_rows)
    pivot_cols = jnp.take(full_rows, jnp.minimum(col_index[:width], pivot_count - 1), axis=1)
    trailing = jnp.where(rows_after & cols_after, front_work - update, 0.0)
    head = jnp.where(cols_after[:, :width], trailing[:, :width], pivot_cols)
    return jnp.concatenate([head, trailing[:, width:]], axis=1)


def local(child_fronts, child_maps, parent_own):
    grid_size = lax.axis_size("row")
    half_index = lax.axis_index("half")
    my_row = lax.axis_index("row")
    my_col = lax.axis_index("col")

    child_done = factor_child(child_fronts[0], CHILD_PIVOTS, grid_size, my_row, my_col)
    local_tiles = child_done.shape[0] // TILE
    pivot_tiles = CHILD_PIVOTS // TILE
    own_map = lax.dynamic_index_in_dim(child_maps, half_index, 0, keepdims=False)
    update_count = child_maps.shape[1]
    slot_ids = jnp.arange(local_tiles, dtype=jnp.int32)
    update_range = jnp.arange(update_count, dtype=jnp.int32)

    def parent_tile(offset):
        update_ids = slot_ids * grid_size + offset - pivot_tiles
        matches = update_ids[:, None] == update_range[None, :]
        return (jnp.sum(jnp.where(matches, own_map[None, :], 0), axis=1), update_ids >= 0)

    row_target, row_valid = parent_tile(my_row)
    col_target, col_valid = parent_tile(my_col)
    parent_row_tiles = parent_own.shape[0] // TILE
    parent_col_tiles = parent_own.shape[1] // TILE
    row_dest = (
        jnp.arange(parent_row_tiles, dtype=jnp.int32)[None, :] * (2 * grid_size)
        + jnp.arange(2, dtype=jnp.int32)[:, None] * grid_size
        + my_row
    )
    row_place = (
        (row_dest[:, :, None] == row_target[None, None, :]) & row_valid[None, None, :]
    ).astype(jnp.float32)
    col_dest = jnp.arange(parent_col_tiles, dtype=jnp.int32) * grid_size + my_col
    col_place = ((col_dest[:, None] == col_target[None, :]) & col_valid[None, :]).astype(
        jnp.float32
    )
    blocks = child_done.reshape(local_tiles, TILE, local_tiles, TILE)
    rows_moved = jnp.einsum("hak,kilj->hailj", row_place, blocks, precision=lax.Precision.HIGHEST)
    both_moved = jnp.einsum(
        "hailj,bl->haibj", rows_moved, col_place, precision=lax.Precision.HIGHEST
    )
    both_moved = both_moved.reshape(2, parent_own.shape[0], parent_own.shape[1])
    kept_part = lax.dynamic_index_in_dim(both_moved, half_index, 0, keepdims=False)
    sent_part = lax.dynamic_index_in_dim(both_moved, 1 - half_index, 0, keepdims=False)
    received = from_partner(sent_part, "half", 0)
    parent_start = parent_own + kept_part + received

    def send_parent_column(column, pivot_tile):
        return spread(column, "col", pivot_tile % grid_size)

    def send_parent_block(current, col_panel, pivot_tile, row_slot, col_slot):
        own_block = lax.dynamic_slice_in_dim(col_panel, row_slot * TILE, TILE, 0)
        result_block = spread(own_block, ("half", "row"), pivot_tile % (2 * grid_size))
        return result_block

    def send_parent_rows(solved_panel):
        pieces = [
            spread(solved_panel, ("half", "row"), which_half * grid_size + my_col)
            for which_half in range(2)
        ]
        even_tiles = pieces[0]
        odd_tiles = pieces[1]
        tile_count = solved_panel.shape[0] // TILE
        stacked = jnp.stack(
            [even_tiles.reshape(tile_count, TILE, TILE), odd_tiles.reshape(tile_count, TILE, TILE)],
            axis=1,
        )
        return stacked.reshape(2 * tile_count * TILE, TILE)

    parent_row = half_index * grid_size + my_row
    parent_done = factor_front(
        parent_start,
        PARENT_PIVOTS,
        2 * grid_size,
        grid_size,
        parent_row,
        my_col,
        send_parent_column,
        send_parent_block,
        send_parent_rows,
    )
    return (child_done[None], parent_done)


def solution(mesh):
    in_specs = (P("half", "row", "col"), P(), P(("half", "row"), "col"))
    out_specs = (P("half", "row", "col"), P(("half", "row"), "col"))
    return jax.shard_map(local, mesh=mesh, in_specs=in_specs, out_specs=out_specs, check_vma=False)
```

```python
import jax
import jax.numpy as jnp
from jax import lax
from jax.sharding import PartitionSpec as P

TILE = 128
CHILD_PIVOTS = 1024
PARENT_PIVOTS = 128
CYCLE_TILES = 16


def spread(shard, axis, root):
    mine = lax.axis_index(axis) == root
    return lax.psum(jnp.where(mine, shard, jnp.zeros_like(shard)), axis)


def from_partner(shard, axis, distance):
    return lax.ppermute(shard, axis, [(i, i ^ 1 << distance) for i in range(lax.axis_size(axis))])


def factor_front(
    front_work,
    pivot_count,
    row_groups,
    col_groups,
    my_row,
    my_col,
    fetch_panel,
    fetch_diag,
    fetch_across,
):
    row_count, col_count = front_work.shape
    row_tiles = jnp.arange(row_count, dtype=jnp.int32) // TILE * row_groups + my_row
    col_tiles = jnp.arange(col_count, dtype=jnp.int32) // TILE * col_groups + my_col

    def one_step(pivot_tile, current):
        row_slot = pivot_tile // row_groups
        col_slot = pivot_tile // col_groups
        column = lax.dynamic_slice_in_dim(current, col_slot * TILE, TILE, 1)
        col_panel = fetch_panel(column, pivot_tile)
        diag_block = fetch_diag(current, col_panel, pivot_tile, row_slot, col_slot)
        diag_factor = jnp.linalg.cholesky(diag_block)
        solved_panel = jax.scipy.linalg.solve_triangular(diag_factor, col_panel.T, lower=True).T
        across_panel = fetch_across(solved_panel)
        rows_after = (row_tiles > pivot_tile)[:, None]
        cols_after = (col_tiles > pivot_tile)[:, None]
        left_factor = jnp.where(rows_after, solved_panel, 0.0)
        right_factor = jnp.where(cols_after, across_panel, 0.0)
        current = current - jnp.dot(
            left_factor,
            right_factor.T,
            precision=lax.Precision.HIGHEST,
            preferred_element_type=jnp.float32,
        )
        pivot_rows = lax.dynamic_slice_in_dim(current, row_slot * TILE, TILE, 0)
        row_owner = my_row == pivot_tile % row_groups
        pivot_rows = jnp.where(row_owner & (col_tiles > pivot_tile)[None, :], 0.0, pivot_rows)
        current = lax.dynamic_update_slice_in_dim(current, pivot_rows, row_slot * TILE, 0)
        diag_rows = jnp.tile(jnp.tril(diag_factor), (row_count // TILE, 1))
        new_column = jnp.where(
            rows_after, solved_panel, jnp.where((row_tiles == pivot_tile)[:, None], diag_rows, 0.0)
        )
        old_column = lax.dynamic_slice_in_dim(current, col_slot * TILE, TILE, 1)
        new_column = jnp.where(my_col == pivot_tile % col_groups, new_column, old_column)
        return lax.dynamic_update_slice_in_dim(current, new_column, col_slot * TILE, 1)

    return lax.fori_loop(0, pivot_count // TILE, one_step, front_work)


def pivot_order(pieces, slot_count, tile_count):
    group_count, rest = pieces.shape[0], pieces.shape[2:]
    shaped = pieces.reshape((group_count, slot_count, TILE) + rest)
    shaped = jnp.moveaxis(shaped, 0, 1).reshape((slot_count * group_count * TILE,) + rest)
    return shaped[: tile_count * TILE]


def factor_child(front_work, pivot_count, grid_size, my_row, my_col):
    local_count = front_work.shape[0]
    tile_count = pivot_count // TILE
    slot_count = -(-tile_count // grid_size)
    width = slot_count * TILE
    col_pieces = lax.all_gather(front_work[:, :width].T, "col", axis=0)
    panel_rows = pivot_order(col_pieces, slot_count, tile_count)
    row_pieces = lax.all_gather(front_work[:width, :], "row", axis=0)
    panel_cols = pivot_order(row_pieces, slot_count, tile_count)
    diag_pieces = lax.all_gather(panel_rows[:, :width].T, "row", axis=0)
    diag_block = pivot_order(diag_pieces, slot_count, tile_count)
    diag_factor = jnp.tril(jnp.linalg.cholesky(diag_block))
    both = jnp.concatenate([panel_rows, panel_cols], axis=1)
    solved = jax.scipy.linalg.solve_triangular(diag_factor, both, lower=True)
    solved_rows = solved[:, :local_count].T
    solved_cols = solved[:, local_count:].T
    within = jnp.arange(local_count, dtype=jnp.int32)
    row_index = within // TILE * grid_size * TILE + my_row * TILE + within % TILE
    col_index = within // TILE * grid_size * TILE + my_col * TILE + within % TILE
    rows_after = (row_index >= pivot_count)[:, None]
    cols_after = (col_index >= pivot_count)[None, :]
    update = jnp.dot(
        jnp.where(rows_after, solved_rows, 0.0),
        jnp.where(cols_after.T, solved_cols, 0.0).T,
        precision=lax.Precision.HIGHEST,
        preferred_element_type=jnp.float32,
    )
    diag_rows = jnp.take(diag_factor, jnp.minimum(row_index, pivot_count - 1), axis=0)
    full_rows = jnp.where(rows_after, solved_rows, diag_rows)
    pivot_cols = jnp.take(full_rows, jnp.minimum(col_index[:width], pivot_count - 1), axis=1)
    trailing = jnp.where(rows_after & cols_after, front_work - update, 0.0)
    head = jnp.where(cols_after[:, :width], trailing[:, :width], pivot_cols)
    return jnp.concatenate([head, trailing[:, width:]], axis=1)


def assemble_by_einsum(child_done, child_maps, parent_own, grid_size, half_index, my_row, my_col):
    local_tiles = child_done.shape[0] // TILE
    pivot_tiles = CHILD_PIVOTS // TILE
    own_map = lax.dynamic_index_in_dim(child_maps, half_index, 0, keepdims=False)
    update_count = child_maps.shape[1]
    slot_ids = jnp.arange(local_tiles, dtype=jnp.int32)
    update_range = jnp.arange(update_count, dtype=jnp.int32)

    def parent_tile(offset):
        update_ids = slot_ids * grid_size + offset - pivot_tiles
        matches = update_ids[:, None] == update_range[None, :]
        return (jnp.sum(jnp.where(matches, own_map[None, :], 0), axis=1), update_ids >= 0)

    row_target, row_valid = parent_tile(my_row)
    col_target, col_valid = parent_tile(my_col)
    parent_row_tiles = parent_own.shape[0] // TILE
    parent_col_tiles = parent_own.shape[1] // TILE
    row_dest = (
        jnp.arange(parent_row_tiles, dtype=jnp.int32)[None, :] * (2 * grid_size)
        + jnp.arange(2, dtype=jnp.int32)[:, None] * grid_size
        + my_row
    )
    row_place = (
        (row_dest[:, :, None] == row_target[None, None, :]) & row_valid[None, None, :]
    ).astype(jnp.float32)
    col_dest = jnp.arange(parent_col_tiles, dtype=jnp.int32) * grid_size + my_col
    col_place = ((col_dest[:, None] == col_target[None, :]) & col_valid[None, :]).astype(
        jnp.float32
    )
    blocks = child_done.reshape(local_tiles, TILE, local_tiles, TILE)
    rows_moved = jnp.einsum("hak,kilj->hailj", row_place, blocks, precision=lax.Precision.HIGHEST)
    both_moved = jnp.einsum(
        "hailj,bl->haibj", rows_moved, col_place, precision=lax.Precision.HIGHEST
    )
    both_moved = both_moved.reshape(2, parent_own.shape[0], parent_own.shape[1])
    kept_part = lax.dynamic_index_in_dim(both_moved, half_index, 0, keepdims=False)
    sent_part = lax.dynamic_index_in_dim(both_moved, 1 - half_index, 0, keepdims=False)
    received = from_partner(sent_part, "half", 0)
    return parent_own + kept_part + received


def tile_source(targets, slot_total):
    slots = jnp.arange(slot_total, dtype=jnp.int32)
    matches = targets[None, :] == slots[:, None]
    source = jnp.sum(jnp.where(matches, jnp.arange(targets.shape[0], dtype=jnp.int32)[None, :], 0), axis=1)
    return source, jnp.any(matches, axis=1)


def place_tiles(block, child_map, row_source, parent_shape, grid_size, row_groups, my_col):
    col_count = block.shape[2] // TILE
    col_ids = jnp.arange(col_count, dtype=jnp.int32) * grid_size + my_col
    col_targets = jnp.take(child_map, col_ids, axis=0) // grid_size
    col_source, col_valid = tile_source(col_targets, parent_shape[1] // TILE)
    row_ids = row_source
    row_targets = jnp.take(child_map, row_ids, axis=0) // row_groups
    row_from, row_valid = tile_source(row_targets, parent_shape[0] // TILE)
    tiles = block.reshape(block.shape[0], TILE, col_count, TILE)
    tiles = jnp.take(tiles, row_from, axis=0)
    tiles = jnp.take(tiles, col_source, axis=2)
    valid = row_valid[:, None, None, None] & col_valid[None, None, :, None]
    return jnp.where(valid, tiles, 0.0).reshape(parent_shape)


def assemble_by_parity(child_done, child_maps, parent_own, grid_size, half_index, my_row, my_col):
    pivot_tiles = CHILD_PIVOTS // TILE
    first_slot = pivot_tiles // grid_size
    update = child_done[first_slot * TILE :, first_slot * TILE :]
    pair_count = update.shape[0] // (2 * TILE)
    by_parity = update.reshape(pair_count, 2, TILE, update.shape[1])
    kept = lax.dynamic_index_in_dim(by_parity, half_index, 1, keepdims=False)
    sent = lax.dynamic_index_in_dim(by_parity, 1 - half_index, 1, keepdims=False)
    received = from_partner(sent, "half", 0)
    pair_ids = jnp.arange(pair_count, dtype=jnp.int32)
    row_update_ids = (2 * pair_ids + half_index) * grid_size + my_row
    own_map = lax.dynamic_index_in_dim(child_maps, half_index, 0, keepdims=False)
    other_map = lax.dynamic_index_in_dim(child_maps, 1 - half_index, 0, keepdims=False)
    row_groups = 2 * grid_size
    kept_part = place_tiles(kept, own_map, row_update_ids, parent_own.shape, grid_size, row_groups, my_col)
    got_part = place_tiles(received, other_map, row_update_ids, parent_own.shape, grid_size, row_groups, my_col)
    return parent_own + kept_part + got_part


def local(child_fronts, child_maps, parent_own):
    grid_size = lax.axis_size("row")
    half_index = lax.axis_index("half")
    my_row = lax.axis_index("row")
    my_col = lax.axis_index("col")

    child_done = factor_child(child_fronts[0], CHILD_PIVOTS, grid_size, my_row, my_col)
    pivot_tiles = CHILD_PIVOTS // TILE
    first_slot = pivot_tiles // grid_size
    update_slots = child_done.shape[0] // TILE - first_slot
    parity_fits = CYCLE_TILES % (2 * grid_size) == 0 and pivot_tiles % grid_size == 0
    parity_fits = parity_fits and first_slot % 2 == 0 and update_slots % 2 == 0
    if not parity_fits:
        parent_start = assemble_by_einsum(
            child_done, child_maps, parent_own, grid_size, half_index, my_row, my_col
        )
    else:
        parent_start = assemble_by_parity(
            child_done, child_maps, parent_own, grid_size, half_index, my_row, my_col
        )

    def send_parent_column(column, pivot_tile):
        return spread(column, "col", pivot_tile % grid_size)

    def send_parent_block(current, col_panel, pivot_tile, row_slot, col_slot):
        own_block = lax.dynamic_slice_in_dim(col_panel, row_slot * TILE, TILE, 0)
        result_block = spread(own_block, ("half", "row"), pivot_tile % (2 * grid_size))
        return result_block

    def send_parent_rows(solved_panel):
        pieces = [
            spread(solved_panel, ("half", "row"), which_half * grid_size + my_col)
            for which_half in range(2)
        ]
        even_tiles = pieces[0]
        odd_tiles = pieces[1]
        tile_count = solved_panel.shape[0] // TILE
        stacked = jnp.stack(
            [even_tiles.reshape(tile_count, TILE, TILE), odd_tiles.reshape(tile_count, TILE, TILE)],
            axis=1,
        )
        return stacked.reshape(2 * tile_count * TILE, TILE)

    parent_row = half_index * grid_size + my_row
    parent_done = factor_front(
        parent_start,
        PARENT_PIVOTS,
        2 * grid_size,
        grid_size,
        parent_row,
        my_col,
        send_parent_column,
        send_parent_block,
        send_parent_rows,
    )
    return (child_done[None], parent_done)


def solution(mesh):
    in_specs = (P("half", "row", "col"), P(), P(("half", "row"), "col"))
    out_specs = (P("half", "row", "col"), P(("half", "row"), "col"))
    return jax.shard_map(local, mesh=mesh, in_specs=in_specs, out_specs=out_specs, check_vma=False)
```

```python
import jax
import jax.numpy as jnp
from jax import lax
from jax.sharding import PartitionSpec as P

TILE = 128
CHILD_PIVOTS = 1024
PARENT_PIVOTS = 128
CYCLE_TILES = 16


def spread(shard, axis, root):
    mine = lax.axis_index(axis) == root
    return lax.psum(jnp.where(mine, shard, jnp.zeros_like(shard)), axis)


def from_partner(shard, axis, distance):
    return lax.ppermute(shard, axis, [(i, i ^ 1 << distance) for i in range(lax.axis_size(axis))])


def factor_front(
    front_work,
    pivot_count,
    row_groups,
    col_groups,
    my_row,
    my_col,
    fetch_panel,
    fetch_diag,
    fetch_across,
):
    row_count, col_count = front_work.shape
    row_tiles = jnp.arange(row_count, dtype=jnp.int32) // TILE * row_groups + my_row
    col_tiles = jnp.arange(col_count, dtype=jnp.int32) // TILE * col_groups + my_col

    def one_step(pivot_tile, current):
        row_slot = pivot_tile // row_groups
        col_slot = pivot_tile // col_groups
        column = lax.dynamic_slice_in_dim(current, col_slot * TILE, TILE, 1)
        col_panel = fetch_panel(column, pivot_tile)
        diag_block = fetch_diag(current, col_panel, pivot_tile, row_slot, col_slot)
        diag_factor = jnp.linalg.cholesky(diag_block)
        solved_panel = jax.scipy.linalg.solve_triangular(diag_factor, col_panel.T, lower=True).T
        across_panel = fetch_across(solved_panel)
        rows_after = (row_tiles > pivot_tile)[:, None]
        cols_after = (col_tiles > pivot_tile)[:, None]
        left_factor = jnp.where(rows_after, solved_panel, 0.0)
        right_factor = jnp.where(cols_after, across_panel, 0.0)
        current = current - jnp.dot(
            left_factor,
            right_factor.T,
            precision=lax.Precision.HIGHEST,
            preferred_element_type=jnp.float32,
        )
        pivot_rows = lax.dynamic_slice_in_dim(current, row_slot * TILE, TILE, 0)
        row_owner = my_row == pivot_tile % row_groups
        pivot_rows = jnp.where(row_owner & (col_tiles > pivot_tile)[None, :], 0.0, pivot_rows)
        current = lax.dynamic_update_slice_in_dim(current, pivot_rows, row_slot * TILE, 0)
        diag_rows = jnp.tile(jnp.tril(diag_factor), (row_count // TILE, 1))
        new_column = jnp.where(
            rows_after, solved_panel, jnp.where((row_tiles == pivot_tile)[:, None], diag_rows, 0.0)
        )
        old_column = lax.dynamic_slice_in_dim(current, col_slot * TILE, TILE, 1)
        new_column = jnp.where(my_col == pivot_tile % col_groups, new_column, old_column)
        return lax.dynamic_update_slice_in_dim(current, new_column, col_slot * TILE, 1)

    return lax.fori_loop(0, pivot_count // TILE, one_step, front_work)


def pivot_order(pieces, slot_count, tile_count):
    group_count, rest = pieces.shape[0], pieces.shape[2:]
    shaped = pieces.reshape((group_count, slot_count, TILE) + rest)
    shaped = jnp.moveaxis(shaped, 0, 1).reshape((slot_count * group_count * TILE,) + rest)
    return shaped[: tile_count * TILE]


def factor_child(front_work, pivot_count, grid_size, my_row, my_col):
    local_count = front_work.shape[0]
    tile_count = pivot_count // TILE
    slot_count = -(-tile_count // grid_size)
    width = slot_count * TILE
    diag_pieces = lax.all_gather(front_work[:width, :width], ("row", "col"), axis=0)
    diag_block = diag_pieces.reshape(grid_size, grid_size, slot_count, TILE, slot_count, TILE)
    diag_block = diag_block.transpose(2, 0, 3, 4, 1, 5).reshape(slot_count * grid_size * TILE, -1)
    diag_block = diag_block[:pivot_count, :pivot_count]
    diag_factor = jnp.tril(jnp.linalg.cholesky(diag_block))
    eye = jnp.eye(pivot_count, dtype=jnp.float32)
    diag_inverse = jnp.tril(jax.scipy.linalg.solve_triangular(diag_factor, eye, lower=True))
    col_pieces = lax.all_gather(front_work[:, :width].T, "col", axis=0)
    panel_rows = pivot_order(col_pieces, slot_count, tile_count)
    row_pieces = lax.all_gather(front_work[:width, :], "row", axis=0)
    panel_cols = pivot_order(row_pieces, slot_count, tile_count)
    both = jnp.concatenate([panel_rows, panel_cols], axis=1)
    solved = jnp.dot(
        diag_inverse, both, precision=lax.Precision.HIGHEST, preferred_element_type=jnp.float32
    )
    solved_rows = solved[:, :local_count].T
    solved_cols = solved[:, local_count:].T
    within = jnp.arange(local_count, dtype=jnp.int32)
    row_index = within // TILE * grid_size * TILE + my_row * TILE + within % TILE
    col_index = within // TILE * grid_size * TILE + my_col * TILE + within % TILE
    rows_after = (row_index >= pivot_count)[:, None]
    cols_after = (col_index >= pivot_count)[None, :]
    update = jnp.dot(
        jnp.where(rows_after, solved_rows, 0.0),
        jnp.where(cols_after.T, solved_cols, 0.0).T,
        precision=lax.Precision.HIGHEST,
        preferred_element_type=jnp.float32,
    )
    diag_rows = jnp.take(diag_factor, jnp.minimum(row_index, pivot_count - 1), axis=0)
    full_rows = jnp.where(rows_after, solved_rows, diag_rows)
    pivot_cols = jnp.take(full_rows, jnp.minimum(col_index[:width], pivot_count - 1), axis=1)
    trailing = jnp.where(rows_after & cols_after, front_work - update, 0.0)
    head = jnp.where(cols_after[:, :width], trailing[:, :width], pivot_cols)
    return jnp.concatenate([head, trailing[:, width:]], axis=1)


def assemble_by_einsum(child_done, child_maps, parent_own, grid_size, half_index, my_row, my_col):
    local_tiles = child_done.shape[0] // TILE
    pivot_tiles = CHILD_PIVOTS // TILE
    own_map = lax.dynamic_index_in_dim(child_maps, half_index, 0, keepdims=False)
    update_count = child_maps.shape[1]
    slot_ids = jnp.arange(local_tiles, dtype=jnp.int32)
    update_range = jnp.arange(update_count, dtype=jnp.int32)

    def parent_tile(offset):
        update_ids = slot_ids * grid_size + offset - pivot_tiles
        matches = update_ids[:, None] == update_range[None, :]
        return (jnp.sum(jnp.where(matches, own_map[None, :], 0), axis=1), update_ids >= 0)

    row_target, row_valid = parent_tile(my_row)
    col_target, col_valid = parent_tile(my_col)
    parent_row_tiles = parent_own.shape[0] // TILE
    parent_col_tiles = parent_own.shape[1] // TILE
    row_dest = (
        jnp.arange(parent_row_tiles, dtype=jnp.int32)[None, :] * (2 * grid_size)
        + jnp.arange(2, dtype=jnp.int32)[:, None] * grid_size
        + my_row
    )
    row_place = (
        (row_dest[:, :, None] == row_target[None, None, :]) & row_valid[None, None, :]
    ).astype(jnp.float32)
    col_dest = jnp.arange(parent_col_tiles, dtype=jnp.int32) * grid_size + my_col
    col_place = ((col_dest[:, None] == col_target[None, :]) & col_valid[None, :]).astype(
        jnp.float32
    )
    blocks = child_done.reshape(local_tiles, TILE, local_tiles, TILE)
    rows_moved = jnp.einsum("hak,kilj->hailj", row_place, blocks, precision=lax.Precision.HIGHEST)
    both_moved = jnp.einsum(
        "hailj,bl->haibj", rows_moved, col_place, precision=lax.Precision.HIGHEST
    )
    both_moved = both_moved.reshape(2, parent_own.shape[0], parent_own.shape[1])
    kept_part = lax.dynamic_index_in_dim(both_moved, half_index, 0, keepdims=False)
    sent_part = lax.dynamic_index_in_dim(both_moved, 1 - half_index, 0, keepdims=False)
    received = from_partner(sent_part, "half", 0)
    return parent_own + kept_part + received


def tile_source(targets, slot_total):
    slots = jnp.arange(slot_total, dtype=jnp.int32)
    matches = targets[None, :] == slots[:, None]
    source = jnp.sum(jnp.where(matches, jnp.arange(targets.shape[0], dtype=jnp.int32)[None, :], 0), axis=1)
    return source, jnp.any(matches, axis=1)


def place_tiles(block, child_map, row_source, parent_shape, grid_size, row_groups, my_col):
    col_count = block.shape[2] // TILE
    col_ids = jnp.arange(col_count, dtype=jnp.int32) * grid_size + my_col
    col_targets = jnp.take(child_map, col_ids, axis=0) // grid_size
    col_source, col_valid = tile_source(col_targets, parent_shape[1] // TILE)
    row_ids = row_source
    row_targets = jnp.take(child_map, row_ids, axis=0) // row_groups
    row_from, row_valid = tile_source(row_targets, parent_shape[0] // TILE)
    tiles = block.reshape(block.shape[0], TILE, col_count, TILE)
    tiles = jnp.take(tiles, row_from, axis=0)
    tiles = jnp.take(tiles, col_source, axis=2)
    valid = row_valid[:, None, None, None] & col_valid[None, None, :, None]
    return jnp.where(valid, tiles, 0.0).reshape(parent_shape)


def assemble_by_parity(child_done, child_maps, parent_own, grid_size, half_index, my_row, my_col):
    pivot_tiles = CHILD_PIVOTS // TILE
    first_slot = pivot_tiles // grid_size
    update = child_done[first_slot * TILE :, first_slot * TILE :]
    pair_count = update.shape[0] // (2 * TILE)
    by_parity = update.reshape(pair_count, 2, TILE, update.shape[1])
    kept = lax.dynamic_index_in_dim(by_parity, half_index, 1, keepdims=False)
    sent = lax.dynamic_index_in_dim(by_parity, 1 - half_index, 1, keepdims=False)
    received = from_partner(sent, "half", 0)
    pair_ids = jnp.arange(pair_count, dtype=jnp.int32)
    row_update_ids = (2 * pair_ids + half_index) * grid_size + my_row
    own_map = lax.dynamic_index_in_dim(child_maps, half_index, 0, keepdims=False)
    other_map = lax.dynamic_index_in_dim(child_maps, 1 - half_index, 0, keepdims=False)
    row_groups = 2 * grid_size
    kept_part = place_tiles(kept, own_map, row_update_ids, parent_own.shape, grid_size, row_groups, my_col)
    got_part = place_tiles(received, other_map, row_update_ids, parent_own.shape, grid_size, row_groups, my_col)
    return parent_own + kept_part + got_part


def local(child_fronts, child_maps, parent_own):
    grid_size = lax.axis_size("row")
    half_index = lax.axis_index("half")
    my_row = lax.axis_index("row")
    my_col = lax.axis_index("col")

    child_done = factor_child(child_fronts[0], CHILD_PIVOTS, grid_size, my_row, my_col)
    pivot_tiles = CHILD_PIVOTS // TILE
    first_slot = pivot_tiles // grid_size
    update_slots = child_done.shape[0] // TILE - first_slot
    parity_fits = CYCLE_TILES % (2 * grid_size) == 0 and pivot_tiles % grid_size == 0
    parity_fits = parity_fits and first_slot % 2 == 0 and update_slots % 2 == 0
    if not parity_fits:
        parent_start = assemble_by_einsum(
            child_done, child_maps, parent_own, grid_size, half_index, my_row, my_col
        )
    else:
        parent_start = assemble_by_parity(
            child_done, child_maps, parent_own, grid_size, half_index, my_row, my_col
        )

    def send_parent_column(column, pivot_tile):
        return spread(column, "col", pivot_tile % grid_size)

    def send_parent_block(current, col_panel, pivot_tile, row_slot, col_slot):
        own_block = lax.dynamic_slice_in_dim(col_panel, row_slot * TILE, TILE, 0)
        result_block = spread(own_block, ("half", "row"), pivot_tile % (2 * grid_size))
        return result_block

    def send_parent_rows(solved_panel):
        pieces = [
            spread(solved_panel, ("half", "row"), which_half * grid_size + my_col)
            for which_half in range(2)
        ]
        even_tiles = pieces[0]
        odd_tiles = pieces[1]
        tile_count = solved_panel.shape[0] // TILE
        stacked = jnp.stack(
            [even_tiles.reshape(tile_count, TILE, TILE), odd_tiles.reshape(tile_count, TILE, TILE)],
            axis=1,
        )
        return stacked.reshape(2 * tile_count * TILE, TILE)

    parent_row = half_index * grid_size + my_row
    parent_done = factor_front(
        parent_start,
        PARENT_PIVOTS,
        2 * grid_size,
        grid_size,
        parent_row,
        my_col,
        send_parent_column,
        send_parent_block,
        send_parent_rows,
    )
    return (child_done[None], parent_done)


def solution(mesh):
    in_specs = (P("half", "row", "col"), P(), P(("half", "row"), "col"))
    out_specs = (P("half", "row", "col"), P(("half", "row"), "col"))
    return jax.shard_map(local, mesh=mesh, in_specs=in_specs, out_specs=out_specs, check_vma=False)
```

```python
import jax
import jax.numpy as jnp
from jax import lax
from jax.sharding import PartitionSpec as P

TILE = 128
CHILD_PIVOTS = 1024
PARENT_PIVOTS = 128
CYCLE_TILES = 16


def spread(shard, axis, root):
    mine = lax.axis_index(axis) == root
    return lax.psum(jnp.where(mine, shard, jnp.zeros_like(shard)), axis)


def from_partner(shard, axis, distance):
    return lax.ppermute(shard, axis, [(i, i ^ 1 << distance) for i in range(lax.axis_size(axis))])


def factor_front(
    front_work,
    pivot_count,
    row_groups,
    col_groups,
    my_row,
    my_col,
    fetch_panel,
    fetch_diag,
    fetch_across,
):
    row_count, col_count = front_work.shape
    row_tiles = jnp.arange(row_count, dtype=jnp.int32) // TILE * row_groups + my_row
    col_tiles = jnp.arange(col_count, dtype=jnp.int32) // TILE * col_groups + my_col

    def one_step(pivot_tile, current):
        row_slot = pivot_tile // row_groups
        col_slot = pivot_tile // col_groups
        column = lax.dynamic_slice_in_dim(current, col_slot * TILE, TILE, 1)
        col_panel = fetch_panel(column, pivot_tile)
        diag_block = fetch_diag(current, col_panel, pivot_tile, row_slot, col_slot)
        diag_factor = jnp.linalg.cholesky(diag_block)
        solved_panel = jax.scipy.linalg.solve_triangular(diag_factor, col_panel.T, lower=True).T
        across_panel = fetch_across(solved_panel)
        rows_after = (row_tiles > pivot_tile)[:, None]
        cols_after = (col_tiles > pivot_tile)[:, None]
        left_factor = jnp.where(rows_after, solved_panel, 0.0)
        right_factor = jnp.where(cols_after, across_panel, 0.0)
        current = current - jnp.dot(
            left_factor,
            right_factor.T,
            precision=lax.Precision.HIGHEST,
            preferred_element_type=jnp.float32,
        )
        pivot_rows = lax.dynamic_slice_in_dim(current, row_slot * TILE, TILE, 0)
        row_owner = my_row == pivot_tile % row_groups
        pivot_rows = jnp.where(row_owner & (col_tiles > pivot_tile)[None, :], 0.0, pivot_rows)
        current = lax.dynamic_update_slice_in_dim(current, pivot_rows, row_slot * TILE, 0)
        diag_rows = jnp.tile(jnp.tril(diag_factor), (row_count // TILE, 1))
        new_column = jnp.where(
            rows_after, solved_panel, jnp.where((row_tiles == pivot_tile)[:, None], diag_rows, 0.0)
        )
        old_column = lax.dynamic_slice_in_dim(current, col_slot * TILE, TILE, 1)
        new_column = jnp.where(my_col == pivot_tile % col_groups, new_column, old_column)
        return lax.dynamic_update_slice_in_dim(current, new_column, col_slot * TILE, 1)

    return lax.fori_loop(0, pivot_count // TILE, one_step, front_work)


def pivot_order(pieces, slot_count, tile_count):
    group_count, rest = pieces.shape[0], pieces.shape[2:]
    shaped = pieces.reshape((group_count, slot_count, TILE) + rest)
    shaped = jnp.moveaxis(shaped, 0, 1).reshape((slot_count * group_count * TILE,) + rest)
    return shaped[: tile_count * TILE]


def lower_inverse(factor):
    order = factor.shape[0]
    count = order // TILE
    if count & (count - 1):
        eye = jnp.eye(order, dtype=jnp.float32)
        return jnp.tril(jax.scipy.linalg.solve_triangular(factor, eye, lower=True))
    picks = jnp.arange(count)
    diag = factor.reshape(count, TILE, count, TILE)[picks, :, picks, :]
    eye = jnp.broadcast_to(jnp.eye(TILE, dtype=jnp.float32), diag.shape)
    inverse = jnp.tril(jax.scipy.linalg.solve_triangular(diag, eye, lower=True))
    size = TILE
    while size < order:
        pairs = order // size // 2
        halves = inverse.reshape(pairs, 2, size, size)
        first, second = halves[:, 0], halves[:, 1]
        picks = jnp.arange(pairs)
        lower = factor.reshape(pairs, 2, size, pairs, 2, size)[picks, 1, :, picks, 0, :]
        mixed = jnp.einsum("kab,kbc->kac", second, lower, precision=lax.Precision.HIGHEST)
        mixed = -jnp.einsum("kab,kbc->kac", mixed, first, precision=lax.Precision.HIGHEST)
        top = jnp.concatenate([first, jnp.zeros_like(first)], axis=2)
        bottom = jnp.concatenate([mixed, second], axis=2)
        inverse = jnp.concatenate([top, bottom], axis=1)
        size *= 2
    return inverse[0]


def factor_child(front_work, pivot_count, grid_size, my_row, my_col):
    local_count = front_work.shape[0]
    tile_count = pivot_count // TILE
    slot_count = -(-tile_count // grid_size)
    width = slot_count * TILE
    diag_pieces = lax.all_gather(front_work[:width, :width], ("row", "col"), axis=0)
    diag_block = diag_pieces.reshape(grid_size, grid_size, slot_count, TILE, slot_count, TILE)
    diag_block = diag_block.transpose(2, 0, 3, 4, 1, 5).reshape(slot_count * grid_size * TILE, -1)
    diag_block = diag_block[:pivot_count, :pivot_count]
    diag_factor = jnp.tril(jnp.linalg.cholesky(diag_block))
    diag_inverse = lower_inverse(diag_factor)
    col_pieces = lax.all_gather(front_work[:, :width].T, "col", axis=0)
    panel_rows = pivot_order(col_pieces, slot_count, tile_count)
    row_pieces = lax.all_gather(front_work[:width, :], "row", axis=0)
    panel_cols = pivot_order(row_pieces, slot_count, tile_count)
    both = jnp.concatenate([panel_rows, panel_cols], axis=1)
    solved = jnp.dot(
        diag_inverse, both, precision=lax.Precision.HIGHEST, preferred_element_type=jnp.float32
    )
    solved_rows = solved[:, :local_count].T
    solved_cols = solved[:, local_count:].T
    within = jnp.arange(local_count, dtype=jnp.int32)
    row_index = within // TILE * grid_size * TILE + my_row * TILE + within % TILE
    col_index = within // TILE * grid_size * TILE + my_col * TILE + within % TILE
    rows_after = (row_index >= pivot_count)[:, None]
    cols_after = (col_index >= pivot_count)[None, :]
    update = jnp.dot(
        jnp.where(rows_after, solved_rows, 0.0),
        jnp.where(cols_after.T, solved_cols, 0.0).T,
        precision=lax.Precision.HIGHEST,
        preferred_element_type=jnp.float32,
    )
    diag_rows = jnp.take(diag_factor, jnp.minimum(row_index, pivot_count - 1), axis=0)
    full_rows = jnp.where(rows_after, solved_rows, diag_rows)
    pivot_cols = jnp.take(full_rows, jnp.minimum(col_index[:width], pivot_count - 1), axis=1)
    trailing = jnp.where(rows_after & cols_after, front_work - update, 0.0)
    head = jnp.where(cols_after[:, :width], trailing[:, :width], pivot_cols)
    return jnp.concatenate([head, trailing[:, width:]], axis=1)


def assemble_by_einsum(child_done, child_maps, parent_own, grid_size, half_index, my_row, my_col):
    local_tiles = child_done.shape[0] // TILE
    pivot_tiles = CHILD_PIVOTS // TILE
    own_map = lax.dynamic_index_in_dim(child_maps, half_index, 0, keepdims=False)
    update_count = child_maps.shape[1]
    slot_ids = jnp.arange(local_tiles, dtype=jnp.int32)
    update_range = jnp.arange(update_count, dtype=jnp.int32)

    def parent_tile(offset):
        update_ids = slot_ids * grid_size + offset - pivot_tiles
        matches = update_ids[:, None] == update_range[None, :]
        return (jnp.sum(jnp.where(matches, own_map[None, :], 0), axis=1), update_ids >= 0)

    row_target, row_valid = parent_tile(my_row)
    col_target, col_valid = parent_tile(my_col)
    parent_row_tiles = parent_own.shape[0] // TILE
    parent_col_tiles = parent_own.shape[1] // TILE
    row_dest = (
        jnp.arange(parent_row_tiles, dtype=jnp.int32)[None, :] * (2 * grid_size)
        + jnp.arange(2, dtype=jnp.int32)[:, None] * grid_size
        + my_row
    )
    row_place = (
        (row_dest[:, :, None] == row_target[None, None, :]) & row_valid[None, None, :]
    ).astype(jnp.float32)
    col_dest = jnp.arange(parent_col_tiles, dtype=jnp.int32) * grid_size + my_col
    col_place = ((col_dest[:, None] == col_target[None, :]) & col_valid[None, :]).astype(
        jnp.float32
    )
    blocks = child_done.reshape(local_tiles, TILE, local_tiles, TILE)
    rows_moved = jnp.einsum("hak,kilj->hailj", row_place, blocks, precision=lax.Precision.HIGHEST)
    both_moved = jnp.einsum(
        "hailj,bl->haibj", rows_moved, col_place, precision=lax.Precision.HIGHEST
    )
    both_moved = both_moved.reshape(2, parent_own.shape[0], parent_own.shape[1])
    kept_part = lax.dynamic_index_in_dim(both_moved, half_index, 0, keepdims=False)
    sent_part = lax.dynamic_index_in_dim(both_moved, 1 - half_index, 0, keepdims=False)
    received = from_partner(sent_part, "half", 0)
    return parent_own + kept_part + received


def tile_source(targets, slot_total):
    slots = jnp.arange(slot_total, dtype=jnp.int32)
    matches = targets[None, :] == slots[:, None]
    source = jnp.sum(jnp.where(matches, jnp.arange(targets.shape[0], dtype=jnp.int32)[None, :], 0), axis=1)
    return source, jnp.any(matches, axis=1)


def place_tiles(block, child_map, row_source, parent_shape, grid_size, row_groups, my_col):
    col_count = block.shape[2] // TILE
    col_ids = jnp.arange(col_count, dtype=jnp.int32) * grid_size + my_col
    col_targets = jnp.take(child_map, col_ids, axis=0) // grid_size
    col_source, col_valid = tile_source(col_targets, parent_shape[1] // TILE)
    row_ids = row_source
    row_targets = jnp.take(child_map, row_ids, axis=0) // row_groups
    row_from, row_valid = tile_source(row_targets, parent_shape[0] // TILE)
    tiles = block.reshape(block.shape[0], TILE, col_count, TILE)
    tiles = jnp.take(tiles, row_from, axis=0)
    tiles = jnp.take(tiles, col_source, axis=2)
    valid = row_valid[:, None, None, None] & col_valid[None, None, :, None]
    return jnp.where(valid, tiles, 0.0).reshape(parent_shape)


def assemble_by_parity(child_done, child_maps, parent_own, grid_size, half_index, my_row, my_col):
    pivot_tiles = CHILD_PIVOTS // TILE
    first_slot = pivot_tiles // grid_size
    update = child_done[first_slot * TILE :, first_slot * TILE :]
    pair_count = update.shape[0] // (2 * TILE)
    by_parity = update.reshape(pair_count, 2, TILE, update.shape[1])
    kept = lax.dynamic_index_in_dim(by_parity, half_index, 1, keepdims=False)
    sent = lax.dynamic_index_in_dim(by_parity, 1 - half_index, 1, keepdims=False)
    received = from_partner(sent, "half", 0)
    pair_ids = jnp.arange(pair_count, dtype=jnp.int32)
    row_update_ids = (2 * pair_ids + half_index) * grid_size + my_row
    own_map = lax.dynamic_index_in_dim(child_maps, half_index, 0, keepdims=False)
    other_map = lax.dynamic_index_in_dim(child_maps, 1 - half_index, 0, keepdims=False)
    row_groups = 2 * grid_size
    kept_part = place_tiles(kept, own_map, row_update_ids, parent_own.shape, grid_size, row_groups, my_col)
    got_part = place_tiles(received, other_map, row_update_ids, parent_own.shape, grid_size, row_groups, my_col)
    return parent_own + kept_part + got_part


def local(child_fronts, child_maps, parent_own):
    grid_size = lax.axis_size("row")
    half_index = lax.axis_index("half")
    my_row = lax.axis_index("row")
    my_col = lax.axis_index("col")

    child_done = factor_child(child_fronts[0], CHILD_PIVOTS, grid_size, my_row, my_col)
    pivot_tiles = CHILD_PIVOTS // TILE
    first_slot = pivot_tiles // grid_size
    update_slots = child_done.shape[0] // TILE - first_slot
    parity_fits = CYCLE_TILES % (2 * grid_size) == 0 and pivot_tiles % grid_size == 0
    parity_fits = parity_fits and first_slot % 2 == 0 and update_slots % 2 == 0
    if not parity_fits:
        parent_start = assemble_by_einsum(
            child_done, child_maps, parent_own, grid_size, half_index, my_row, my_col
        )
    else:
        parent_start = assemble_by_parity(
            child_done, child_maps, parent_own, grid_size, half_index, my_row, my_col
        )

    def send_parent_column(column, pivot_tile):
        return spread(column, "col", pivot_tile % grid_size)

    def send_parent_block(current, col_panel, pivot_tile, row_slot, col_slot):
        own_block = lax.dynamic_slice_in_dim(col_panel, row_slot * TILE, TILE, 0)
        result_block = spread(own_block, ("half", "row"), pivot_tile % (2 * grid_size))
        return result_block

    def send_parent_rows(solved_panel):
        pieces = [
            spread(solved_panel, ("half", "row"), which_half * grid_size + my_col)
            for which_half in range(2)
        ]
        even_tiles = pieces[0]
        odd_tiles = pieces[1]
        tile_count = solved_panel.shape[0] // TILE
        stacked = jnp.stack(
            [even_tiles.reshape(tile_count, TILE, TILE), odd_tiles.reshape(tile_count, TILE, TILE)],
            axis=1,
        )
        return stacked.reshape(2 * tile_count * TILE, TILE)

    parent_row = half_index * grid_size + my_row
    parent_done = factor_front(
        parent_start,
        PARENT_PIVOTS,
        2 * grid_size,
        grid_size,
        parent_row,
        my_col,
        send_parent_column,
        send_parent_block,
        send_parent_rows,
    )
    return (child_done[None], parent_done)


def solution(mesh):
    in_specs = (P("half", "row", "col"), P(), P(("half", "row"), "col"))
    out_specs = (P("half", "row", "col"), P(("half", "row"), "col"))
    return jax.shard_map(local, mesh=mesh, in_specs=in_specs, out_specs=out_specs, check_vma=False)
```

```python
import jax
import jax.numpy as jnp
from jax import lax
from jax.sharding import PartitionSpec as P

TILE = 128
CHILD_PIVOTS = 1024
PARENT_PIVOTS = 128
CYCLE_TILES = 16


def spread(shard, axis, root):
    mine = lax.axis_index(axis) == root
    return lax.psum(jnp.where(mine, shard, jnp.zeros_like(shard)), axis)


def from_partner(shard, axis, distance):
    return lax.ppermute(shard, axis, [(i, i ^ 1 << distance) for i in range(lax.axis_size(axis))])


def factor_front(
    front_work,
    pivot_count,
    row_groups,
    col_groups,
    my_row,
    my_col,
    fetch_panel,
    fetch_diag,
    fetch_across,
):
    row_count, col_count = front_work.shape
    row_tiles = jnp.arange(row_count, dtype=jnp.int32) // TILE * row_groups + my_row
    col_tiles = jnp.arange(col_count, dtype=jnp.int32) // TILE * col_groups + my_col

    def one_step(pivot_tile, current):
        row_slot = pivot_tile // row_groups
        col_slot = pivot_tile // col_groups
        column = lax.dynamic_slice_in_dim(current, col_slot * TILE, TILE, 1)
        col_panel = fetch_panel(column, pivot_tile)
        diag_block = fetch_diag(current, col_panel, pivot_tile, row_slot, col_slot)
        diag_factor = jnp.linalg.cholesky(diag_block)
        solved_panel = jax.scipy.linalg.solve_triangular(diag_factor, col_panel.T, lower=True).T
        across_panel = fetch_across(solved_panel)
        rows_after = (row_tiles > pivot_tile)[:, None]
        cols_after = (col_tiles > pivot_tile)[:, None]
        left_factor = jnp.where(rows_after, solved_panel, 0.0)
        right_factor = jnp.where(cols_after, across_panel, 0.0)
        current = current - jnp.dot(
            left_factor,
            right_factor.T,
            precision=lax.Precision.HIGHEST,
            preferred_element_type=jnp.float32,
        )
        pivot_rows = lax.dynamic_slice_in_dim(current, row_slot * TILE, TILE, 0)
        row_owner = my_row == pivot_tile % row_groups
        pivot_rows = jnp.where(row_owner & (col_tiles > pivot_tile)[None, :], 0.0, pivot_rows)
        current = lax.dynamic_update_slice_in_dim(current, pivot_rows, row_slot * TILE, 0)
        diag_rows = jnp.tile(jnp.tril(diag_factor), (row_count // TILE, 1))
        new_column = jnp.where(
            rows_after, solved_panel, jnp.where((row_tiles == pivot_tile)[:, None], diag_rows, 0.0)
        )
        old_column = lax.dynamic_slice_in_dim(current, col_slot * TILE, TILE, 1)
        new_column = jnp.where(my_col == pivot_tile % col_groups, new_column, old_column)
        return lax.dynamic_update_slice_in_dim(current, new_column, col_slot * TILE, 1)

    return lax.fori_loop(0, pivot_count // TILE, one_step, front_work)


def pivot_order(pieces, slot_count, tile_count):
    group_count, rest = pieces.shape[0], pieces.shape[2:]
    shaped = pieces.reshape((group_count, slot_count, TILE) + rest)
    shaped = jnp.moveaxis(shaped, 0, 1).reshape((slot_count * group_count * TILE,) + rest)
    return shaped[: tile_count * TILE]


def factor_pivots(block):
    order = block.shape[0]
    count = order // TILE
    eye = jnp.eye(TILE, dtype=jnp.float32)
    work = block
    columns = []
    inverses = []
    for step in range(count):
        factor = jnp.tril(jnp.linalg.cholesky(work[:TILE, :TILE]))
        inverse = jnp.tril(jax.scipy.linalg.solve_triangular(factor, eye, lower=True))
        panel = jnp.dot(
            work[TILE:, :TILE], inverse.T, precision=lax.Precision.HIGHEST,
            preferred_element_type=jnp.float32,
        )
        work = work[TILE:, TILE:] - jnp.dot(
            panel, panel.T, precision=lax.Precision.HIGHEST, preferred_element_type=jnp.float32
        )
        columns.append(jnp.concatenate([jnp.zeros((step * TILE, TILE), jnp.float32), factor, panel]))
        inverses.append(inverse)
    return jnp.concatenate(columns, axis=1), jnp.stack(inverses)


def lower_inverse(factor, inverse):
    order = factor.shape[0]
    size = TILE
    while size < order:
        pairs = order // size // 2
        halves = inverse.reshape(pairs, 2, size, size)
        first, second = halves[:, 0], halves[:, 1]
        picks = jnp.arange(pairs)
        lower = factor.reshape(pairs, 2, size, pairs, 2, size)[picks, 1, :, picks, 0, :]
        mixed = jnp.einsum("kab,kbc->kac", second, lower, precision=lax.Precision.HIGHEST)
        mixed = -jnp.einsum("kab,kbc->kac", mixed, first, precision=lax.Precision.HIGHEST)
        top = jnp.concatenate([first, jnp.zeros_like(first)], axis=2)
        bottom = jnp.concatenate([mixed, second], axis=2)
        inverse = jnp.concatenate([top, bottom], axis=1)
        size *= 2
    return inverse[0]


def factor_child(front_work, pivot_count, grid_size, my_row, my_col):
    local_count = front_work.shape[0]
    tile_count = pivot_count // TILE
    slot_count = -(-tile_count // grid_size)
    width = slot_count * TILE
    diag_pieces = lax.all_gather(front_work[:width, :width], ("row", "col"), axis=0)
    diag_block = diag_pieces.reshape(grid_size, grid_size, slot_count, TILE, slot_count, TILE)
    diag_block = diag_block.transpose(2, 0, 3, 4, 1, 5).reshape(slot_count * grid_size * TILE, -1)
    diag_block = diag_block[:pivot_count, :pivot_count]
    diag_factor, block_inverses = factor_pivots(diag_block)
    if tile_count & (tile_count - 1):
        eye = jnp.eye(pivot_count, dtype=jnp.float32)
        diag_inverse = jnp.tril(jax.scipy.linalg.solve_triangular(diag_factor, eye, lower=True))
    else:
        diag_inverse = lower_inverse(diag_factor, block_inverses)
    col_pieces = lax.all_gather(front_work[:, :width].T, "col", axis=0)
    panel_rows = pivot_order(col_pieces, slot_count, tile_count)
    row_pieces = lax.all_gather(front_work[:width, :], "row", axis=0)
    panel_cols = pivot_order(row_pieces, slot_count, tile_count)
    both = jnp.concatenate([panel_rows, panel_cols], axis=1)
    solved = jnp.dot(
        diag_inverse, both, precision=lax.Precision.HIGHEST, preferred_element_type=jnp.float32
    )
    solved_rows = solved[:, :local_count].T
    solved_cols = solved[:, local_count:].T
    within = jnp.arange(local_count, dtype=jnp.int32)
    row_index = within // TILE * grid_size * TILE + my_row * TILE + within % TILE
    col_index = within // TILE * grid_size * TILE + my_col * TILE + within % TILE
    rows_after = (row_index >= pivot_count)[:, None]
    cols_after = (col_index >= pivot_count)[None, :]
    update = jnp.dot(
        jnp.where(rows_after, solved_rows, 0.0),
        jnp.where(cols_after.T, solved_cols, 0.0).T,
        precision=lax.Precision.HIGHEST,
        preferred_element_type=jnp.float32,
    )
    diag_rows = jnp.take(diag_factor, jnp.minimum(row_index, pivot_count - 1), axis=0)
    full_rows = jnp.where(rows_after, solved_rows, diag_rows)
    pivot_cols = jnp.take(full_rows, jnp.minimum(col_index[:width], pivot_count - 1), axis=1)
    trailing = jnp.where(rows_after & cols_after, front_work - update, 0.0)
    head = jnp.where(cols_after[:, :width], trailing[:, :width], pivot_cols)
    return jnp.concatenate([head, trailing[:, width:]], axis=1)


def assemble_by_einsum(child_done, child_maps, parent_own, grid_size, half_index, my_row, my_col):
    local_tiles = child_done.shape[0] // TILE
    pivot_tiles = CHILD_PIVOTS // TILE
    own_map = lax.dynamic_index_in_dim(child_maps, half_index, 0, keepdims=False)
    update_count = child_maps.shape[1]
    slot_ids = jnp.arange(local_tiles, dtype=jnp.int32)
    update_range = jnp.arange(update_count, dtype=jnp.int32)

    def parent_tile(offset):
        update_ids = slot_ids * grid_size + offset - pivot_tiles
        matches = update_ids[:, None] == update_range[None, :]
        return (jnp.sum(jnp.where(matches, own_map[None, :], 0), axis=1), update_ids >= 0)

    row_target, row_valid = parent_tile(my_row)
    col_target, col_valid = parent_tile(my_col)
    parent_row_tiles = parent_own.shape[0] // TILE
    parent_col_tiles = parent_own.shape[1] // TILE
    row_dest = (
        jnp.arange(parent_row_tiles, dtype=jnp.int32)[None, :] * (2 * grid_size)
        + jnp.arange(2, dtype=jnp.int32)[:, None] * grid_size
        + my_row
    )
    row_place = (
        (row_dest[:, :, None] == row_target[None, None, :]) & row_valid[None, None, :]
    ).astype(jnp.float32)
    col_dest = jnp.arange(parent_col_tiles, dtype=jnp.int32) * grid_size + my_col
    col_place = ((col_dest[:, None] == col_target[None, :]) & col_valid[None, :]).astype(
        jnp.float32
    )
    blocks = child_done.reshape(local_tiles, TILE, local_tiles, TILE)
    rows_moved = jnp.einsum("hak,kilj->hailj", row_place, blocks, precision=lax.Precision.HIGHEST)
    both_moved = jnp.einsum(
        "hailj,bl->haibj", rows_moved, col_place, precision=lax.Precision.HIGHEST
    )
    both_moved = both_moved.reshape(2, parent_own.shape[0], parent_own.shape[1])
    kept_part = lax.dynamic_index_in_dim(both_moved, half_index, 0, keepdims=False)
    sent_part = lax.dynamic_index_in_dim(both_moved, 1 - half_index, 0, keepdims=False)
    received = from_partner(sent_part, "half", 0)
    return parent_own + kept_part + received


def tile_source(targets, slot_total):
    slots = jnp.arange(slot_total, dtype=jnp.int32)
    matches = targets[None, :] == slots[:, None]
    source = jnp.sum(jnp.where(matches, jnp.arange(targets.shape[0], dtype=jnp.int32)[None, :], 0), axis=1)
    return source, jnp.any(matches, axis=1)


def place_tiles(block, child_map, row_source, parent_shape, grid_size, row_groups, my_col):
    col_count = block.shape[2] // TILE
    col_ids = jnp.arange(col_count, dtype=jnp.int32) * grid_size + my_col
    col_targets = jnp.take(child_map, col_ids, axis=0) // grid_size
    col_source, col_valid = tile_source(col_targets, parent_shape[1] // TILE)
    row_ids = row_source
    row_targets = jnp.take(child_map, row_ids, axis=0) // row_groups
    row_from, row_valid = tile_source(row_targets, parent_shape[0] // TILE)
    tiles = block.reshape(block.shape[0], TILE, col_count, TILE)
    tiles = jnp.take(tiles, row_from, axis=0)
    tiles = jnp.take(tiles, col_source, axis=2)
    valid = row_valid[:, None, None, None] & col_valid[None, None, :, None]
    return jnp.where(valid, tiles, 0.0).reshape(parent_shape)


def assemble_by_parity(child_done, child_maps, parent_own, grid_size, half_index, my_row, my_col):
    pivot_tiles = CHILD_PIVOTS // TILE
    first_slot = pivot_tiles // grid_size
    update = child_done[first_slot * TILE :, first_slot * TILE :]
    pair_count = update.shape[0] // (2 * TILE)
    by_parity = update.reshape(pair_count, 2, TILE, update.shape[1])
    kept = lax.dynamic_index_in_dim(by_parity, half_index, 1, keepdims=False)
    sent = lax.dynamic_index_in_dim(by_parity, 1 - half_index, 1, keepdims=False)
    received = from_partner(sent, "half", 0)
    pair_ids = jnp.arange(pair_count, dtype=jnp.int32)
    row_update_ids = (2 * pair_ids + half_index) * grid_size + my_row
    own_map = lax.dynamic_index_in_dim(child_maps, half_index, 0, keepdims=False)
    other_map = lax.dynamic_index_in_dim(child_maps, 1 - half_index, 0, keepdims=False)
    row_groups = 2 * grid_size
    kept_part = place_tiles(kept, own_map, row_update_ids, parent_own.shape, grid_size, row_groups, my_col)
    got_part = place_tiles(received, other_map, row_update_ids, parent_own.shape, grid_size, row_groups, my_col)
    return parent_own + kept_part + got_part


def local(child_fronts, child_maps, parent_own):
    grid_size = lax.axis_size("row")
    half_index = lax.axis_index("half")
    my_row = lax.axis_index("row")
    my_col = lax.axis_index("col")

    child_done = factor_child(child_fronts[0], CHILD_PIVOTS, grid_size, my_row, my_col)
    pivot_tiles = CHILD_PIVOTS // TILE
    first_slot = pivot_tiles // grid_size
    update_slots = child_done.shape[0] // TILE - first_slot
    parity_fits = CYCLE_TILES % (2 * grid_size) == 0 and pivot_tiles % grid_size == 0
    parity_fits = parity_fits and first_slot % 2 == 0 and update_slots % 2 == 0
    if not parity_fits:
        parent_start = assemble_by_einsum(
            child_done, child_maps, parent_own, grid_size, half_index, my_row, my_col
        )
    else:
        parent_start = assemble_by_parity(
            child_done, child_maps, parent_own, grid_size, half_index, my_row, my_col
        )

    def send_parent_column(column, pivot_tile):
        return spread(column, "col", pivot_tile % grid_size)

    def send_parent_block(current, col_panel, pivot_tile, row_slot, col_slot):
        own_block = lax.dynamic_slice_in_dim(col_panel, row_slot * TILE, TILE, 0)
        result_block = spread(own_block, ("half", "row"), pivot_tile % (2 * grid_size))
        return result_block

    def send_parent_rows(solved_panel):
        pieces = [
            spread(solved_panel, ("half", "row"), which_half * grid_size + my_col)
            for which_half in range(2)
        ]
        even_tiles = pieces[0]
        odd_tiles = pieces[1]
        tile_count = solved_panel.shape[0] // TILE
        stacked = jnp.stack(
            [even_tiles.reshape(tile_count, TILE, TILE), odd_tiles.reshape(tile_count, TILE, TILE)],
            axis=1,
        )
        return stacked.reshape(2 * tile_count * TILE, TILE)

    parent_row = half_index * grid_size + my_row
    parent_done = factor_front(
        parent_start,
        PARENT_PIVOTS,
        2 * grid_size,
        grid_size,
        parent_row,
        my_col,
        send_parent_column,
        send_parent_block,
        send_parent_rows,
    )
    return (child_done[None], parent_done)


def solution(mesh):
    in_specs = (P("half", "row", "col"), P(), P(("half", "row"), "col"))
    out_specs = (P("half", "row", "col"), P(("half", "row"), "col"))
    return jax.shard_map(local, mesh=mesh, in_specs=in_specs, out_specs=out_specs, check_vma=False)
```

```python
import jax
import jax.numpy as jnp
from jax import lax
from jax.sharding import PartitionSpec as P

TILE = 128
CHILD_PIVOTS = 1024
PARENT_PIVOTS = 128
CYCLE_TILES = 16


def spread(shard, axis, root):
    mine = lax.axis_index(axis) == root
    return lax.psum(jnp.where(mine, shard, jnp.zeros_like(shard)), axis)


def from_partner(shard, axis, distance):
    return lax.ppermute(shard, axis, [(i, i ^ 1 << distance) for i in range(lax.axis_size(axis))])


def pivot_order(pieces, slot_count, tile_count):
    group_count, rest = pieces.shape[0], pieces.shape[2:]
    shaped = pieces.reshape((group_count, slot_count, TILE) + rest)
    shaped = jnp.moveaxis(shaped, 0, 1).reshape((slot_count * group_count * TILE,) + rest)
    return shaped[: tile_count * TILE]


def factor_pivots(block):
    order = block.shape[0]
    count = order // TILE
    eye = jnp.eye(TILE, dtype=jnp.float32)
    work = block
    columns = []
    inverses = []
    for step in range(count):
        factor = jnp.tril(jnp.linalg.cholesky(work[:TILE, :TILE]))
        inverse = jnp.tril(jax.scipy.linalg.solve_triangular(factor, eye, lower=True))
        panel = jnp.dot(
            work[TILE:, :TILE], inverse.T, precision=lax.Precision.HIGHEST,
            preferred_element_type=jnp.float32,
        )
        work = work[TILE:, TILE:] - jnp.dot(
            panel, panel.T, precision=lax.Precision.HIGHEST, preferred_element_type=jnp.float32
        )
        columns.append(jnp.concatenate([jnp.zeros((step * TILE, TILE), jnp.float32), factor, panel]))
        inverses.append(inverse)
    return jnp.concatenate(columns, axis=1), jnp.stack(inverses)


def lower_inverse(factor, inverse):
    order = factor.shape[0]
    size = TILE
    while size < order:
        pairs = order // size // 2
        halves = inverse.reshape(pairs, 2, size, size)
        first, second = halves[:, 0], halves[:, 1]
        picks = jnp.arange(pairs)
        lower = factor.reshape(pairs, 2, size, pairs, 2, size)[picks, 1, :, picks, 0, :]
        mixed = jnp.einsum("kab,kbc->kac", second, lower, precision=lax.Precision.HIGHEST)
        mixed = -jnp.einsum("kab,kbc->kac", mixed, first, precision=lax.Precision.HIGHEST)
        top = jnp.concatenate([first, jnp.zeros_like(first)], axis=2)
        bottom = jnp.concatenate([mixed, second], axis=2)
        inverse = jnp.concatenate([top, bottom], axis=1)
        size *= 2
    return inverse[0]


def factor_child(front_work, pivot_count, grid_size, my_row, my_col):
    local_count = front_work.shape[0]
    tile_count = pivot_count // TILE
    slot_count = -(-tile_count // grid_size)
    width = slot_count * TILE
    diag_pieces = lax.all_gather(front_work[:width, :width], ("row", "col"), axis=0)
    diag_block = diag_pieces.reshape(grid_size, grid_size, slot_count, TILE, slot_count, TILE)
    diag_block = diag_block.transpose(2, 0, 3, 4, 1, 5).reshape(slot_count * grid_size * TILE, -1)
    diag_block = diag_block[:pivot_count, :pivot_count]
    diag_factor, block_inverses = factor_pivots(diag_block)
    if tile_count & (tile_count - 1):
        eye = jnp.eye(pivot_count, dtype=jnp.float32)
        diag_inverse = jnp.tril(jax.scipy.linalg.solve_triangular(diag_factor, eye, lower=True))
    else:
        diag_inverse = lower_inverse(diag_factor, block_inverses)
    col_pieces = lax.all_gather(front_work[:, :width].T, "col", axis=0)
    panel_rows = pivot_order(col_pieces, slot_count, tile_count)
    row_pieces = lax.all_gather(front_work[:width, :], "row", axis=0)
    panel_cols = pivot_order(row_pieces, slot_count, tile_count)
    both = jnp.concatenate([panel_rows, panel_cols], axis=1)
    solved = jnp.dot(
        diag_inverse, both, precision=lax.Precision.HIGHEST, preferred_element_type=jnp.float32
    )
    solved_rows = solved[:, :local_count].T
    solved_cols = solved[:, local_count:].T
    within = jnp.arange(local_count, dtype=jnp.int32)
    row_index = within // TILE * grid_size * TILE + my_row * TILE + within % TILE
    col_index = within // TILE * grid_size * TILE + my_col * TILE + within % TILE
    rows_after = (row_index >= pivot_count)[:, None]
    cols_after = (col_index >= pivot_count)[None, :]
    update = jnp.dot(
        jnp.where(rows_after, solved_rows, 0.0),
        jnp.where(cols_after.T, solved_cols, 0.0).T,
        precision=lax.Precision.HIGHEST,
        preferred_element_type=jnp.float32,
    )
    diag_rows = jnp.take(diag_factor, jnp.minimum(row_index, pivot_count - 1), axis=0)
    full_rows = jnp.where(rows_after, solved_rows, diag_rows)
    pivot_cols = jnp.take(full_rows, jnp.minimum(col_index[:width], pivot_count - 1), axis=1)
    trailing = jnp.where(rows_after & cols_after, front_work - update, 0.0)
    head = jnp.where(cols_after[:, :width], trailing[:, :width], pivot_cols)
    return jnp.concatenate([head, trailing[:, width:]], axis=1)


def assemble_by_einsum(child_done, child_maps, parent_own, grid_size, half_index, my_row, my_col):
    local_tiles = child_done.shape[0] // TILE
    pivot_tiles = CHILD_PIVOTS // TILE
    own_map = lax.dynamic_index_in_dim(child_maps, half_index, 0, keepdims=False)
    update_count = child_maps.shape[1]
    slot_ids = jnp.arange(local_tiles, dtype=jnp.int32)
    update_range = jnp.arange(update_count, dtype=jnp.int32)

    def parent_tile(offset):
        update_ids = slot_ids * grid_size + offset - pivot_tiles
        matches = update_ids[:, None] == update_range[None, :]
        return (jnp.sum(jnp.where(matches, own_map[None, :], 0), axis=1), update_ids >= 0)

    row_target, row_valid = parent_tile(my_row)
    col_target, col_valid = parent_tile(my_col)
    parent_row_tiles = parent_own.shape[0] // TILE
    parent_col_tiles = parent_own.shape[1] // TILE
    row_dest = (
        jnp.arange(parent_row_tiles, dtype=jnp.int32)[None, :] * (2 * grid_size)
        + jnp.arange(2, dtype=jnp.int32)[:, None] * grid_size
        + my_row
    )
    row_place = (
        (row_dest[:, :, None] == row_target[None, None, :]) & row_valid[None, None, :]
    ).astype(jnp.float32)
    col_dest = jnp.arange(parent_col_tiles, dtype=jnp.int32) * grid_size + my_col
    col_place = ((col_dest[:, None] == col_target[None, :]) & col_valid[None, :]).astype(
        jnp.float32
    )
    blocks = child_done.reshape(local_tiles, TILE, local_tiles, TILE)
    rows_moved = jnp.einsum("hak,kilj->hailj", row_place, blocks, precision=lax.Precision.HIGHEST)
    both_moved = jnp.einsum(
        "hailj,bl->haibj", rows_moved, col_place, precision=lax.Precision.HIGHEST
    )
    both_moved = both_moved.reshape(2, parent_own.shape[0], parent_own.shape[1])
    kept_part = lax.dynamic_index_in_dim(both_moved, half_index, 0, keepdims=False)
    sent_part = lax.dynamic_index_in_dim(both_moved, 1 - half_index, 0, keepdims=False)
    received = from_partner(sent_part, "half", 0)
    return parent_own + kept_part + received


def tile_source(targets, slot_total):
    slots = jnp.arange(slot_total, dtype=jnp.int32)
    matches = targets[None, :] == slots[:, None]
    source = jnp.sum(jnp.where(matches, jnp.arange(targets.shape[0], dtype=jnp.int32)[None, :], 0), axis=1)
    return source, jnp.any(matches, axis=1)


def place_tiles(block, child_map, row_source, parent_shape, grid_size, row_groups, my_col):
    col_count = block.shape[2] // TILE
    col_ids = jnp.arange(col_count, dtype=jnp.int32) * grid_size + my_col
    col_targets = jnp.take(child_map, col_ids, axis=0) // grid_size
    col_source, col_valid = tile_source(col_targets, parent_shape[1] // TILE)
    row_ids = row_source
    row_targets = jnp.take(child_map, row_ids, axis=0) // row_groups
    row_from, row_valid = tile_source(row_targets, parent_shape[0] // TILE)
    tiles = block.reshape(block.shape[0], TILE, col_count, TILE)
    tiles = jnp.take(tiles, row_from, axis=0)
    tiles = jnp.take(tiles, col_source, axis=2)
    valid = row_valid[:, None, None, None] & col_valid[None, None, :, None]
    return jnp.where(valid, tiles, 0.0).reshape(parent_shape)


def assemble_by_parity(child_done, child_maps, parent_own, grid_size, half_index, my_row, my_col):
    pivot_tiles = CHILD_PIVOTS // TILE
    first_slot = pivot_tiles // grid_size
    update = child_done[first_slot * TILE :, first_slot * TILE :]
    pair_count = update.shape[0] // (2 * TILE)
    by_parity = update.reshape(pair_count, 2, TILE, update.shape[1])
    kept = lax.dynamic_index_in_dim(by_parity, half_index, 1, keepdims=False)
    sent = lax.dynamic_index_in_dim(by_parity, 1 - half_index, 1, keepdims=False)
    received = from_partner(sent, "half", 0)
    pair_ids = jnp.arange(pair_count, dtype=jnp.int32)
    row_update_ids = (2 * pair_ids + half_index) * grid_size + my_row
    own_map = lax.dynamic_index_in_dim(child_maps, half_index, 0, keepdims=False)
    other_map = lax.dynamic_index_in_dim(child_maps, 1 - half_index, 0, keepdims=False)
    row_groups = 2 * grid_size
    kept_part = place_tiles(kept, own_map, row_update_ids, parent_own.shape, grid_size, row_groups, my_col)
    got_part = place_tiles(received, other_map, row_update_ids, parent_own.shape, grid_size, row_groups, my_col)
    return parent_own + kept_part + got_part


def factor_parent(front_work, grid_size, half_index, my_row, my_col):
    row_groups = 2 * grid_size
    parent_row = half_index * grid_size + my_row
    row_count, col_count = front_work.shape
    column = spread(front_work[:, :TILE], "col", 0)
    halves = lax.all_gather(column, "half", axis=0)
    halves = halves.reshape(2, row_count // TILE, TILE, TILE)
    my_row_cols = jnp.swapaxes(halves, 0, 1).reshape(col_count, TILE)
    pairs = [
        (col * grid_size + row, row * grid_size + col)
        for row in range(grid_size)
        for col in range(grid_size)
    ]
    my_cols = lax.ppermute(my_row_cols, ("row", "col"), pairs)
    diag_block = spread(my_cols[:TILE], "col", 0)
    diag_factor = jnp.tril(jnp.linalg.cholesky(diag_block))
    eye = jnp.eye(TILE, dtype=jnp.float32)
    inverse = jnp.tril(jax.scipy.linalg.solve_triangular(diag_factor, eye, lower=True))
    solved_rows = jnp.dot(column, inverse.T, precision=lax.Precision.HIGHEST)
    solved_cols = jnp.dot(my_cols, inverse.T, precision=lax.Precision.HIGHEST)
    row_within = jnp.arange(row_count, dtype=jnp.int32)
    col_within = jnp.arange(col_count, dtype=jnp.int32)
    row_index = row_within // TILE * row_groups * TILE + parent_row * TILE + row_within % TILE
    col_index = col_within // TILE * grid_size * TILE + my_col * TILE + col_within % TILE
    return finish_front(front_work, solved_rows, solved_cols, diag_factor, row_index, col_index, TILE)


def finish_front(front_work, solved_rows, solved_cols, diag_factor, row_index, col_index, pivot_count):
    width = TILE * (-(-pivot_count // TILE))
    rows_after = (row_index >= pivot_count)[:, None]
    cols_after = (col_index >= pivot_count)[None, :]
    update = jnp.dot(
        jnp.where(rows_after, solved_rows, 0.0),
        jnp.where(cols_after.T, solved_cols, 0.0).T,
        precision=lax.Precision.HIGHEST,
        preferred_element_type=jnp.float32,
    )
    diag_rows = jnp.take(diag_factor, jnp.minimum(row_index, pivot_count - 1), axis=0)
    full_rows = jnp.where(rows_after, solved_rows, diag_rows)
    pivot_cols = jnp.take(full_rows, jnp.minimum(col_index[:width], pivot_count - 1), axis=1)
    trailing = jnp.where(rows_after & cols_after, front_work - update, 0.0)
    head = jnp.where(cols_after[:, :width], trailing[:, :width], pivot_cols)
    return jnp.concatenate([head, trailing[:, width:]], axis=1)


def local(child_fronts, child_maps, parent_own):
    grid_size = lax.axis_size("row")
    half_index = lax.axis_index("half")
    my_row = lax.axis_index("row")
    my_col = lax.axis_index("col")

    child_done = factor_child(child_fronts[0], CHILD_PIVOTS, grid_size, my_row, my_col)
    pivot_tiles = CHILD_PIVOTS // TILE
    first_slot = pivot_tiles // grid_size
    update_slots = child_done.shape[0] // TILE - first_slot
    parity_fits = CYCLE_TILES % (2 * grid_size) == 0 and pivot_tiles % grid_size == 0
    parity_fits = parity_fits and first_slot % 2 == 0 and update_slots % 2 == 0
    if not parity_fits:
        parent_start = assemble_by_einsum(
            child_done, child_maps, parent_own, grid_size, half_index, my_row, my_col
        )
    else:
        parent_start = assemble_by_parity(
            child_done, child_maps, parent_own, grid_size, half_index, my_row, my_col
        )

    parent_done = factor_parent(parent_start, grid_size, half_index, my_row, my_col)
    return (child_done[None], parent_done)


def solution(mesh):
    in_specs = (P("half", "row", "col"), P(), P(("half", "row"), "col"))
    out_specs = (P("half", "row", "col"), P(("half", "row"), "col"))
    return jax.shard_map(local, mesh=mesh, in_specs=in_specs, out_specs=out_specs, check_vma=False)
```

```python
import jax
import jax.numpy as jnp
from jax import lax
from jax.sharding import PartitionSpec as P

TILE = 128
CHILD_PIVOTS = 1024
PARENT_PIVOTS = 128
CYCLE_TILES = 16


def spread(shard, axis, root):
    mine = lax.axis_index(axis) == root
    return lax.psum(jnp.where(mine, shard, jnp.zeros_like(shard)), axis)


def copy_from(shard, axis, root):
    size = lax.axis_size(axis)
    mine = lax.axis_index(axis) == root
    total = jnp.where(mine, shard, jnp.zeros_like(shard))
    for target in range(size):
        if target != root:
            total = total + lax.ppermute(shard, axis, [(root, target)])
    return total


def from_partner(shard, axis, distance):
    return lax.ppermute(shard, axis, [(i, i ^ 1 << distance) for i in range(lax.axis_size(axis))])


def pivot_order(pieces, slot_count, tile_count):
    group_count, rest = pieces.shape[0], pieces.shape[2:]
    shaped = pieces.reshape((group_count, slot_count, TILE) + rest)
    shaped = jnp.moveaxis(shaped, 0, 1).reshape((slot_count * group_count * TILE,) + rest)
    return shaped[: tile_count * TILE]


def factor_pivots(block):
    order = block.shape[0]
    count = order // TILE
    eye = jnp.eye(TILE, dtype=jnp.float32)
    work = block
    columns = []
    inverses = []
    for step in range(count):
        factor = jnp.tril(jnp.linalg.cholesky(work[:TILE, :TILE]))
        inverse = jnp.tril(jax.scipy.linalg.solve_triangular(factor, eye, lower=True))
        panel = jnp.dot(
            work[TILE:, :TILE], inverse.T, precision=lax.Precision.HIGHEST,
            preferred_element_type=jnp.float32,
        )
        work = work[TILE:, TILE:] - jnp.dot(
            panel, panel.T, precision=lax.Precision.HIGHEST, preferred_element_type=jnp.float32
        )
        columns.append(jnp.concatenate([jnp.zeros((step * TILE, TILE), jnp.float32), factor, panel]))
        inverses.append(inverse)
    return jnp.concatenate(columns, axis=1), jnp.stack(inverses)


def lower_inverse(factor, inverse):
    order = factor.shape[0]
    size = TILE
    while size < order:
        pairs = order // size // 2
        halves = inverse.reshape(pairs, 2, size, size)
        first, second = halves[:, 0], halves[:, 1]
        picks = jnp.arange(pairs)
        lower = factor.reshape(pairs, 2, size, pairs, 2, size)[picks, 1, :, picks, 0, :]
        mixed = jnp.einsum("kab,kbc->kac", second, lower, precision=lax.Precision.HIGHEST)
        mixed = -jnp.einsum("kab,kbc->kac", mixed, first, precision=lax.Precision.HIGHEST)
        top = jnp.concatenate([first, jnp.zeros_like(first)], axis=2)
        bottom = jnp.concatenate([mixed, second], axis=2)
        inverse = jnp.concatenate([top, bottom], axis=1)
        size *= 2
    return inverse[0]


def factor_child(front_work, pivot_count, grid_size, my_row, my_col):
    local_count = front_work.shape[0]
    tile_count = pivot_count // TILE
    slot_count = -(-tile_count // grid_size)
    width = slot_count * TILE
    diag_pieces = lax.all_gather(front_work[:width, :width], ("row", "col"), axis=0)
    diag_block = diag_pieces.reshape(grid_size, grid_size, slot_count, TILE, slot_count, TILE)
    diag_block = diag_block.transpose(2, 0, 3, 4, 1, 5).reshape(slot_count * grid_size * TILE, -1)
    diag_block = diag_block[:pivot_count, :pivot_count]
    diag_factor, block_inverses = factor_pivots(diag_block)
    if tile_count & (tile_count - 1):
        eye = jnp.eye(pivot_count, dtype=jnp.float32)
        diag_inverse = jnp.tril(jax.scipy.linalg.solve_triangular(diag_factor, eye, lower=True))
    else:
        diag_inverse = lower_inverse(diag_factor, block_inverses)
    col_pieces = lax.all_gather(front_work[:, :width].T, "col", axis=0)
    panel_rows = pivot_order(col_pieces, slot_count, tile_count)
    row_pieces = lax.all_gather(front_work[:width, :], "row", axis=0)
    panel_cols = pivot_order(row_pieces, slot_count, tile_count)
    both = jnp.concatenate([panel_rows, panel_cols], axis=1)
    solved = jnp.dot(
        diag_inverse, both, precision=lax.Precision.HIGH, preferred_element_type=jnp.float32
    )
    solved_rows = solved[:, :local_count].T
    solved_cols = solved[:, local_count:].T
    within = jnp.arange(local_count, dtype=jnp.int32)
    row_index = within // TILE * grid_size * TILE + my_row * TILE + within % TILE
    col_index = within // TILE * grid_size * TILE + my_col * TILE + within % TILE
    rows_after = (row_index >= pivot_count)[:, None]
    cols_after = (col_index >= pivot_count)[None, :]
    update = jnp.dot(
        jnp.where(rows_after, solved_rows, 0.0),
        jnp.where(cols_after.T, solved_cols, 0.0).T,
        precision=lax.Precision.HIGH,
        preferred_element_type=jnp.float32,
    )
    diag_rows = jnp.take(diag_factor, jnp.minimum(row_index, pivot_count - 1), axis=0)
    full_rows = jnp.where(rows_after, solved_rows, diag_rows)
    pivot_cols = jnp.take(full_rows, jnp.minimum(col_index[:width], pivot_count - 1), axis=1)
    trailing = jnp.where(rows_after & cols_after, front_work - update, 0.0)
    head = jnp.where(cols_after[:, :width], trailing[:, :width], pivot_cols)
    return jnp.concatenate([head, trailing[:, width:]], axis=1)


def assemble_by_einsum(child_done, child_maps, parent_own, grid_size, half_index, my_row, my_col):
    local_tiles = child_done.shape[0] // TILE
    pivot_tiles = CHILD_PIVOTS // TILE
    own_map = lax.dynamic_index_in_dim(child_maps, half_index, 0, keepdims=False)
    update_count = child_maps.shape[1]
    slot_ids = jnp.arange(local_tiles, dtype=jnp.int32)
    update_range = jnp.arange(update_count, dtype=jnp.int32)

    def parent_tile(offset):
        update_ids = slot_ids * grid_size + offset - pivot_tiles
        matches = update_ids[:, None] == update_range[None, :]
        return (jnp.sum(jnp.where(matches, own_map[None, :], 0), axis=1), update_ids >= 0)

    row_target, row_valid = parent_tile(my_row)
    col_target, col_valid = parent_tile(my_col)
    parent_row_tiles = parent_own.shape[0] // TILE
    parent_col_tiles = parent_own.shape[1] // TILE
    row_dest = (
        jnp.arange(parent_row_tiles, dtype=jnp.int32)[None, :] * (2 * grid_size)
        + jnp.arange(2, dtype=jnp.int32)[:, None] * grid_size
        + my_row
    )
    row_place = (
        (row_dest[:, :, None] == row_target[None, None, :]) & row_valid[None, None, :]
    ).astype(jnp.float32)
    col_dest = jnp.arange(parent_col_tiles, dtype=jnp.int32) * grid_size + my_col
    col_place = ((col_dest[:, None] == col_target[None, :]) & col_valid[None, :]).astype(
        jnp.float32
    )
    blocks = child_done.reshape(local_tiles, TILE, local_tiles, TILE)
    rows_moved = jnp.einsum("hak,kilj->hailj", row_place, blocks, precision=lax.Precision.HIGHEST)
    both_moved = jnp.einsum(
        "hailj,bl->haibj", rows_moved, col_place, precision=lax.Precision.HIGHEST
    )
    both_moved = both_moved.reshape(2, parent_own.shape[0], parent_own.shape[1])
    kept_part = lax.dynamic_index_in_dim(both_moved, half_index, 0, keepdims=False)
    sent_part = lax.dynamic_index_in_dim(both_moved, 1 - half_index, 0, keepdims=False)
    received = from_partner(sent_part, "half", 0)
    return parent_own + kept_part + received


def tile_source(targets, slot_total):
    slots = jnp.arange(slot_total, dtype=jnp.int32)
    matches = targets[None, :] == slots[:, None]
    source = jnp.sum(jnp.where(matches, jnp.arange(targets.shape[0], dtype=jnp.int32)[None, :], 0), axis=1)
    return source, jnp.any(matches, axis=1)


def place_tiles(block, child_map, row_source, parent_shape, grid_size, row_groups, my_col):
    col_count = block.shape[2] // TILE
    col_ids = jnp.arange(col_count, dtype=jnp.int32) * grid_size + my_col
    col_targets = jnp.take(child_map, col_ids, axis=0) // grid_size
    col_source, col_valid = tile_source(col_targets, parent_shape[1] // TILE)
    row_ids = row_source
    row_targets = jnp.take(child_map, row_ids, axis=0) // row_groups
    row_from, row_valid = tile_source(row_targets, parent_shape[0] // TILE)
    tiles = block.reshape(block.shape[0], TILE, col_count, TILE)
    tiles = jnp.take(tiles, row_from, axis=0)
    tiles = jnp.take(tiles, col_source, axis=2)
    valid = row_valid[:, None, None, None] & col_valid[None, None, :, None]
    return jnp.where(valid, tiles, 0.0).reshape(parent_shape)


def assemble_by_parity(child_done, child_maps, parent_own, grid_size, half_index, my_row, my_col):
    pivot_tiles = CHILD_PIVOTS // TILE
    first_slot = pivot_tiles // grid_size
    update = child_done[first_slot * TILE :, first_slot * TILE :]
    pair_count = update.shape[0] // (2 * TILE)
    by_parity = update.reshape(pair_count, 2, TILE, update.shape[1])
    kept = lax.dynamic_index_in_dim(by_parity, half_index, 1, keepdims=False)
    sent = lax.dynamic_index_in_dim(by_parity, 1 - half_index, 1, keepdims=False)
    received = from_partner(sent, "half", 0)
    pair_ids = jnp.arange(pair_count, dtype=jnp.int32)
    row_update_ids = (2 * pair_ids + half_index) * grid_size + my_row
    own_map = lax.dynamic_index_in_dim(child_maps, half_index, 0, keepdims=False)
    other_map = lax.dynamic_index_in_dim(child_maps, 1 - half_index, 0, keepdims=False)
    row_groups = 2 * grid_size
    kept_part = place_tiles(kept, own_map, row_update_ids, parent_own.shape, grid_size, row_groups, my_col)
    got_part = place_tiles(received, other_map, row_update_ids, parent_own.shape, grid_size, row_groups, my_col)
    return parent_own + kept_part + got_part


def factor_parent(front_work, grid_size, half_index, my_row, my_col):
    row_groups = 2 * grid_size
    parent_row = half_index * grid_size + my_row
    row_count, col_count = front_work.shape
    column = copy_from(front_work[:, :TILE], "col", 0)
    halves = lax.all_gather(column, "half", axis=0)
    halves = halves.reshape(2, row_count // TILE, TILE, TILE)
    my_row_cols = jnp.swapaxes(halves, 0, 1).reshape(col_count, TILE)
    pairs = [
        (col * grid_size + row, row * grid_size + col)
        for row in range(grid_size)
        for col in range(grid_size)
    ]
    my_cols = lax.ppermute(my_row_cols, ("row", "col"), pairs)
    diag_block = copy_from(my_row_cols[:TILE], "row", 0)
    diag_factor = jnp.tril(jnp.linalg.cholesky(diag_block))
    eye = jnp.eye(TILE, dtype=jnp.float32)
    inverse = jnp.tril(jax.scipy.linalg.solve_triangular(diag_factor, eye, lower=True))
    solved_rows = jnp.dot(column, inverse.T, precision=lax.Precision.HIGHEST)
    solved_cols = jnp.dot(my_cols, inverse.T, precision=lax.Precision.HIGHEST)
    row_within = jnp.arange(row_count, dtype=jnp.int32)
    col_within = jnp.arange(col_count, dtype=jnp.int32)
    row_index = row_within // TILE * row_groups * TILE + parent_row * TILE + row_within % TILE
    col_index = col_within // TILE * grid_size * TILE + my_col * TILE + col_within % TILE
    return finish_front(front_work, solved_rows, solved_cols, diag_factor, row_index, col_index, TILE)


def finish_front(front_work, solved_rows, solved_cols, diag_factor, row_index, col_index, pivot_count):
    width = TILE * (-(-pivot_count // TILE))
    rows_after = (row_index >= pivot_count)[:, None]
    cols_after = (col_index >= pivot_count)[None, :]
    update = jnp.dot(
        jnp.where(rows_after, solved_rows, 0.0),
        jnp.where(cols_after.T, solved_cols, 0.0).T,
        precision=lax.Precision.HIGHEST,
        preferred_element_type=jnp.float32,
    )
    diag_rows = jnp.take(diag_factor, jnp.minimum(row_index, pivot_count - 1), axis=0)
    full_rows = jnp.where(rows_after, solved_rows, diag_rows)
    pivot_cols = jnp.take(full_rows, jnp.minimum(col_index[:width], pivot_count - 1), axis=1)
    trailing = jnp.where(rows_after & cols_after, front_work - update, 0.0)
    head = jnp.where(cols_after[:, :width], trailing[:, :width], pivot_cols)
    return jnp.concatenate([head, trailing[:, width:]], axis=1)


def local(child_fronts, child_maps, parent_own):
    grid_size = lax.axis_size("row")
    half_index = lax.axis_index("half")
    my_row = lax.axis_index("row")
    my_col = lax.axis_index("col")

    child_done = factor_child(child_fronts[0], CHILD_PIVOTS, grid_size, my_row, my_col)
    pivot_tiles = CHILD_PIVOTS // TILE
    first_slot = pivot_tiles // grid_size
    update_slots = child_done.shape[0] // TILE - first_slot
    parity_fits = CYCLE_TILES % (2 * grid_size) == 0 and pivot_tiles % grid_size == 0
    parity_fits = parity_fits and first_slot % 2 == 0 and update_slots % 2 == 0
    if not parity_fits:
        parent_start = assemble_by_einsum(
            child_done, child_maps, parent_own, grid_size, half_index, my_row, my_col
        )
    else:
        parent_start = assemble_by_parity(
            child_done, child_maps, parent_own, grid_size, half_index, my_row, my_col
        )

    parent_done = factor_parent(parent_start, grid_size, half_index, my_row, my_col)
    return (child_done[None], parent_done)


def solution(mesh):
    in_specs = (P("half", "row", "col"), P(), P(("half", "row"), "col"))
    out_specs = (P("half", "row", "col"), P(("half", "row"), "col"))
    return jax.shard_map(local, mesh=mesh, in_specs=in_specs, out_specs=out_specs, check_vma=False)
```

```python
import jax
import jax.numpy as jnp
from jax import lax
from jax.sharding import PartitionSpec as P

TILE = 128
CHILD_PIVOTS = 1024
PARENT_PIVOTS = 128
CYCLE_TILES = 16


def spread(shard, axis, root):
    mine = lax.axis_index(axis) == root
    return lax.psum(jnp.where(mine, shard, jnp.zeros_like(shard)), axis)


def copy_from(shard, axis, root):
    size = lax.axis_size(axis)
    mine = lax.axis_index(axis) == root
    total = jnp.where(mine, shard, jnp.zeros_like(shard))
    for target in range(size):
        if target != root:
            total = total + lax.ppermute(shard, axis, [(root, target)])
    return total


def gather_by_shifts(shard, axis):
    size = lax.axis_size(axis)
    pieces = [shard]
    for shift in range(1, size):
        pairs = [(i, (i + shift) % size) for i in range(size)]
        pieces.append(lax.ppermute(shard, axis, pairs))
    order = (lax.axis_index(axis) - jnp.arange(size, dtype=jnp.int32)) % size
    return jnp.take(jnp.stack(pieces), order, axis=0)


def from_partner(shard, axis, distance):
    return lax.ppermute(shard, axis, [(i, i ^ 1 << distance) for i in range(lax.axis_size(axis))])


def pivot_order(pieces, slot_count, tile_count):
    group_count, rest = pieces.shape[0], pieces.shape[2:]
    shaped = pieces.reshape((group_count, slot_count, TILE) + rest)
    shaped = jnp.moveaxis(shaped, 0, 1).reshape((slot_count * group_count * TILE,) + rest)
    return shaped[: tile_count * TILE]


def factor_pivots(block):
    order = block.shape[0]
    count = order // TILE
    eye = jnp.eye(TILE, dtype=jnp.float32)
    work = block
    columns = []
    inverses = []
    for step in range(count):
        factor = jnp.tril(jnp.linalg.cholesky(work[:TILE, :TILE]))
        inverse = jnp.tril(jax.scipy.linalg.solve_triangular(factor, eye, lower=True))
        panel = jnp.dot(
            work[TILE:, :TILE], inverse.T, precision=lax.Precision.HIGHEST,
            preferred_element_type=jnp.float32,
        )
        work = work[TILE:, TILE:] - jnp.dot(
            panel, panel.T, precision=lax.Precision.HIGHEST, preferred_element_type=jnp.float32
        )
        columns.append(jnp.concatenate([jnp.zeros((step * TILE, TILE), jnp.float32), factor, panel]))
        inverses.append(inverse)
    return jnp.concatenate(columns, axis=1), jnp.stack(inverses)


def lower_inverse(factor, inverse):
    order = factor.shape[0]
    size = TILE
    while size < order:
        pairs = order // size // 2
        halves = inverse.reshape(pairs, 2, size, size)
        first, second = halves[:, 0], halves[:, 1]
        picks = jnp.arange(pairs)
        lower = factor.reshape(pairs, 2, size, pairs, 2, size)[picks, 1, :, picks, 0, :]
        mixed = jnp.einsum("kab,kbc->kac", second, lower, precision=lax.Precision.HIGHEST)
        mixed = -jnp.einsum("kab,kbc->kac", mixed, first, precision=lax.Precision.HIGHEST)
        top = jnp.concatenate([first, jnp.zeros_like(first)], axis=2)
        bottom = jnp.concatenate([mixed, second], axis=2)
        inverse = jnp.concatenate([top, bottom], axis=1)
        size *= 2
    return inverse[0]


def factor_child(front_work, pivot_count, grid_size, my_row, my_col):
    local_count = front_work.shape[0]
    tile_count = pivot_count // TILE
    slot_count = -(-tile_count // grid_size)
    width = slot_count * TILE
    diag_pieces = lax.all_gather(front_work[:width, :width], ("row", "col"), axis=0)
    diag_block = diag_pieces.reshape(grid_size, grid_size, slot_count, TILE, slot_count, TILE)
    diag_block = diag_block.transpose(2, 0, 3, 4, 1, 5).reshape(slot_count * grid_size * TILE, -1)
    diag_block = diag_block[:pivot_count, :pivot_count]
    diag_factor, block_inverses = factor_pivots(diag_block)
    if tile_count & (tile_count - 1):
        eye = jnp.eye(pivot_count, dtype=jnp.float32)
        diag_inverse = jnp.tril(jax.scipy.linalg.solve_triangular(diag_factor, eye, lower=True))
    else:
        diag_inverse = lower_inverse(diag_factor, block_inverses)
    col_pieces = gather_by_shifts(front_work[:, :width].T, "col")
    panel_rows = pivot_order(col_pieces, slot_count, tile_count)
    row_pieces = gather_by_shifts(front_work[:width, :], "row")
    panel_cols = pivot_order(row_pieces, slot_count, tile_count)
    both = jnp.concatenate([panel_rows, panel_cols], axis=1)
    solved = jnp.dot(
        diag_inverse, both, precision=lax.Precision.HIGH, preferred_element_type=jnp.float32
    )
    solved_rows = solved[:, :local_count].T
    solved_cols = solved[:, local_count:].T
    within = jnp.arange(local_count, dtype=jnp.int32)
    row_index = within // TILE * grid_size * TILE + my_row * TILE + within % TILE
    col_index = within // TILE * grid_size * TILE + my_col * TILE + within % TILE
    rows_after = (row_index >= pivot_count)[:, None]
    cols_after = (col_index >= pivot_count)[None, :]
    update = jnp.dot(
        jnp.where(rows_after, solved_rows, 0.0),
        jnp.where(cols_after.T, solved_cols, 0.0).T,
        precision=lax.Precision.HIGH,
        preferred_element_type=jnp.float32,
    )
    diag_rows = jnp.take(diag_factor, jnp.minimum(row_index, pivot_count - 1), axis=0)
    full_rows = jnp.where(rows_after, solved_rows, diag_rows)
    pivot_cols = jnp.take(full_rows, jnp.minimum(col_index[:width], pivot_count - 1), axis=1)
    trailing = jnp.where(rows_after & cols_after, front_work - update, 0.0)
    head = jnp.where(cols_after[:, :width], trailing[:, :width], pivot_cols)
    return jnp.concatenate([head, trailing[:, width:]], axis=1)


def assemble_by_einsum(child_done, child_maps, parent_own, grid_size, half_index, my_row, my_col):
    local_tiles = child_done.shape[0] // TILE
    pivot_tiles = CHILD_PIVOTS // TILE
    own_map = lax.dynamic_index_in_dim(child_maps, half_index, 0, keepdims=False)
    update_count = child_maps.shape[1]
    slot_ids = jnp.arange(local_tiles, dtype=jnp.int32)
    update_range = jnp.arange(update_count, dtype=jnp.int32)

    def parent_tile(offset):
        update_ids = slot_ids * grid_size + offset - pivot_tiles
        matches = update_ids[:, None] == update_range[None, :]
        return (jnp.sum(jnp.where(matches, own_map[None, :], 0), axis=1), update_ids >= 0)

    row_target, row_valid = parent_tile(my_row)
    col_target, col_valid = parent_tile(my_col)
    parent_row_tiles = parent_own.shape[0] // TILE
    parent_col_tiles = parent_own.shape[1] // TILE
    row_dest = (
        jnp.arange(parent_row_tiles, dtype=jnp.int32)[None, :] * (2 * grid_size)
        + jnp.arange(2, dtype=jnp.int32)[:, None] * grid_size
        + my_row
    )
    row_place = (
        (row_dest[:, :, None] == row_target[None, None, :]) & row_valid[None, None, :]
    ).astype(jnp.float32)
    col_dest = jnp.arange(parent_col_tiles, dtype=jnp.int32) * grid_size + my_col
    col_place = ((col_dest[:, None] == col_target[None, :]) & col_valid[None, :]).astype(
        jnp.float32
    )
    blocks = child_done.reshape(local_tiles, TILE, local_tiles, TILE)
    rows_moved = jnp.einsum("hak,kilj->hailj", row_place, blocks, precision=lax.Precision.HIGHEST)
    both_moved = jnp.einsum(
        "hailj,bl->haibj", rows_moved, col_place, precision=lax.Precision.HIGHEST
    )
    both_moved = both_moved.reshape(2, parent_own.shape[0], parent_own.shape[1])
    kept_part = lax.dynamic_index_in_dim(both_moved, half_index, 0, keepdims=False)
    sent_part = lax.dynamic_index_in_dim(both_moved, 1 - half_index, 0, keepdims=False)
    received = from_partner(sent_part, "half", 0)
    return parent_own + kept_part + received


def tile_source(targets, slot_total):
    slots = jnp.arange(slot_total, dtype=jnp.int32)
    matches = targets[None, :] == slots[:, None]
    source = jnp.sum(jnp.where(matches, jnp.arange(targets.shape[0], dtype=jnp.int32)[None, :], 0), axis=1)
    return source, jnp.any(matches, axis=1)


def place_tiles(block, child_map, row_source, parent_shape, grid_size, row_groups, my_col):
    col_count = block.shape[2] // TILE
    col_ids = jnp.arange(col_count, dtype=jnp.int32) * grid_size + my_col
    col_targets = jnp.take(child_map, col_ids, axis=0) // grid_size
    col_source, col_valid = tile_source(col_targets, parent_shape[1] // TILE)
    row_ids = row_source
    row_targets = jnp.take(child_map, row_ids, axis=0) // row_groups
    row_from, row_valid = tile_source(row_targets, parent_shape[0] // TILE)
    tiles = block.reshape(block.shape[0], TILE, col_count, TILE)
    tiles = jnp.take(tiles, row_from, axis=0)
    tiles = jnp.take(tiles, col_source, axis=2)
    valid = row_valid[:, None, None, None] & col_valid[None, None, :, None]
    return jnp.where(valid, tiles, 0.0).reshape(parent_shape)


def assemble_by_parity(child_done, child_maps, parent_own, grid_size, half_index, my_row, my_col):
    pivot_tiles = CHILD_PIVOTS // TILE
    first_slot = pivot_tiles // grid_size
    update = child_done[first_slot * TILE :, first_slot * TILE :]
    pair_count = update.shape[0] // (2 * TILE)
    by_parity = update.reshape(pair_count, 2, TILE, update.shape[1])
    kept = lax.dynamic_index_in_dim(by_parity, half_index, 1, keepdims=False)
    sent = lax.dynamic_index_in_dim(by_parity, 1 - half_index, 1, keepdims=False)
    received = from_partner(sent, "half", 0)
    pair_ids = jnp.arange(pair_count, dtype=jnp.int32)
    row_update_ids = (2 * pair_ids + half_index) * grid_size + my_row
    own_map = lax.dynamic_index_in_dim(child_maps, half_index, 0, keepdims=False)
    other_map = lax.dynamic_index_in_dim(child_maps, 1 - half_index, 0, keepdims=False)
    row_groups = 2 * grid_size
    kept_part = place_tiles(kept, own_map, row_update_ids, parent_own.shape, grid_size, row_groups, my_col)
    got_part = place_tiles(received, other_map, row_update_ids, parent_own.shape, grid_size, row_groups, my_col)
    return parent_own + kept_part + got_part


def factor_parent(front_work, grid_size, half_index, my_row, my_col):
    row_groups = 2 * grid_size
    parent_row = half_index * grid_size + my_row
    row_count, col_count = front_work.shape
    column = copy_from(front_work[:, :TILE], "col", 0)
    halves = lax.all_gather(column, "half", axis=0)
    halves = halves.reshape(2, row_count // TILE, TILE, TILE)
    my_row_cols = jnp.swapaxes(halves, 0, 1).reshape(col_count, TILE)
    pairs = [
        (col * grid_size + row, row * grid_size + col)
        for row in range(grid_size)
        for col in range(grid_size)
    ]
    my_cols = lax.ppermute(my_row_cols, ("row", "col"), pairs)
    diag_block = copy_from(my_row_cols[:TILE], "row", 0)
    diag_factor = jnp.tril(jnp.linalg.cholesky(diag_block))
    eye = jnp.eye(TILE, dtype=jnp.float32)
    inverse = jnp.tril(jax.scipy.linalg.solve_triangular(diag_factor, eye, lower=True))
    solved_rows = jnp.dot(column, inverse.T, precision=lax.Precision.HIGHEST)
    solved_cols = jnp.dot(my_cols, inverse.T, precision=lax.Precision.HIGHEST)
    row_within = jnp.arange(row_count, dtype=jnp.int32)
    col_within = jnp.arange(col_count, dtype=jnp.int32)
    row_index = row_within // TILE * row_groups * TILE + parent_row * TILE + row_within % TILE
    col_index = col_within // TILE * grid_size * TILE + my_col * TILE + col_within % TILE
    return finish_front(front_work, solved_rows, solved_cols, diag_factor, row_index, col_index, TILE)


def finish_front(front_work, solved_rows, solved_cols, diag_factor, row_index, col_index, pivot_count):
    width = TILE * (-(-pivot_count // TILE))
    rows_after = (row_index >= pivot_count)[:, None]
    cols_after = (col_index >= pivot_count)[None, :]
    update = jnp.dot(
        jnp.where(rows_after, solved_rows, 0.0),
        jnp.where(cols_after.T, solved_cols, 0.0).T,
        precision=lax.Precision.HIGHEST,
        preferred_element_type=jnp.float32,
    )
    diag_rows = jnp.take(diag_factor, jnp.minimum(row_index, pivot_count - 1), axis=0)
    full_rows = jnp.where(rows_after, solved_rows, diag_rows)
    pivot_cols = jnp.take(full_rows, jnp.minimum(col_index[:width], pivot_count - 1), axis=1)
    trailing = jnp.where(rows_after & cols_after, front_work - update, 0.0)
    head = jnp.where(cols_after[:, :width], trailing[:, :width], pivot_cols)
    return jnp.concatenate([head, trailing[:, width:]], axis=1)


def local(child_fronts, child_maps, parent_own):
    grid_size = lax.axis_size("row")
    half_index = lax.axis_index("half")
    my_row = lax.axis_index("row")
    my_col = lax.axis_index("col")

    child_done = factor_child(child_fronts[0], CHILD_PIVOTS, grid_size, my_row, my_col)
    pivot_tiles = CHILD_PIVOTS // TILE
    first_slot = pivot_tiles // grid_size
    update_slots = child_done.shape[0] // TILE - first_slot
    parity_fits = CYCLE_TILES % (2 * grid_size) == 0 and pivot_tiles % grid_size == 0
    parity_fits = parity_fits and first_slot % 2 == 0 and update_slots % 2 == 0
    if not parity_fits:
        parent_start = assemble_by_einsum(
            child_done, child_maps, parent_own, grid_size, half_index, my_row, my_col
        )
    else:
        parent_start = assemble_by_parity(
            child_done, child_maps, parent_own, grid_size, half_index, my_row, my_col
        )

    parent_done = factor_parent(parent_start, grid_size, half_index, my_row, my_col)
    return (child_done[None], parent_done)


def solution(mesh):
    in_specs = (P("half", "row", "col"), P(), P(("half", "row"), "col"))
    out_specs = (P("half", "row", "col"), P(("half", "row"), "col"))
    return jax.shard_map(local, mesh=mesh, in_specs=in_specs, out_specs=out_specs, check_vma=False)
```

```python
import jax
import jax.numpy as jnp
from jax import lax
from jax.sharding import PartitionSpec as P

TILE = 128
CHILD_PIVOTS = 1024
PARENT_PIVOTS = 128
CYCLE_TILES = 16


def spread(shard, axis, root):
    mine = lax.axis_index(axis) == root
    return lax.psum(jnp.where(mine, shard, jnp.zeros_like(shard)), axis)


def copy_from(shard, axis, root):
    size = lax.axis_size(axis)
    mine = lax.axis_index(axis) == root
    total = jnp.where(mine, shard, jnp.zeros_like(shard))
    for target in range(size):
        if target != root:
            total = total + lax.ppermute(shard, axis, [(root, target)])
    return total


def from_partner(shard, axis, distance):
    return lax.ppermute(shard, axis, [(i, i ^ 1 << distance) for i in range(lax.axis_size(axis))])


def pivot_order(pieces, slot_count, tile_count):
    group_count, rest = pieces.shape[0], pieces.shape[2:]
    shaped = pieces.reshape((group_count, slot_count, TILE) + rest)
    shaped = jnp.moveaxis(shaped, 0, 1).reshape((slot_count * group_count * TILE,) + rest)
    return shaped[: tile_count * TILE]


def factor_pivots(block):
    order = block.shape[0]
    count = order // TILE
    eye = jnp.eye(TILE, dtype=jnp.float32)
    work = block
    columns = []
    inverses = []
    for step in range(count):
        factor = jnp.tril(jnp.linalg.cholesky(work[:TILE, :TILE]))
        inverse = jnp.tril(jax.scipy.linalg.solve_triangular(factor, eye, lower=True))
        panel = jnp.dot(
            work[TILE:, :TILE], inverse.T, precision=lax.Precision.HIGHEST,
            preferred_element_type=jnp.float32,
        )
        work = work[TILE:, TILE:] - jnp.dot(
            panel, panel.T, precision=lax.Precision.HIGHEST, preferred_element_type=jnp.float32
        )
        columns.append(jnp.concatenate([jnp.zeros((step * TILE, TILE), jnp.float32), factor, panel]))
        inverses.append(inverse)
    return jnp.concatenate(columns, axis=1), jnp.stack(inverses)


def lower_inverse(factor, inverse):
    order = factor.shape[0]
    size = TILE
    while size < order:
        pairs = order // size // 2
        halves = inverse.reshape(pairs, 2, size, size)
        first, second = halves[:, 0], halves[:, 1]
        picks = jnp.arange(pairs)
        lower = factor.reshape(pairs, 2, size, pairs, 2, size)[picks, 1, :, picks, 0, :]
        mixed = jnp.einsum("kab,kbc->kac", second, lower, precision=lax.Precision.HIGHEST)
        mixed = -jnp.einsum("kab,kbc->kac", mixed, first, precision=lax.Precision.HIGHEST)
        top = jnp.concatenate([first, jnp.zeros_like(first)], axis=2)
        bottom = jnp.concatenate([mixed, second], axis=2)
        inverse = jnp.concatenate([top, bottom], axis=1)
        size *= 2
    return inverse[0]


def factor_child(front_work, pivot_count, grid_size, my_row, my_col):
    local_count = front_work.shape[0]
    tile_count = pivot_count // TILE
    slot_count = -(-tile_count // grid_size)
    width = slot_count * TILE
    diag_pieces = lax.all_gather(front_work[:width, :width], ("row", "col"), axis=0)
    diag_block = diag_pieces.reshape(grid_size, grid_size, slot_count, TILE, slot_count, TILE)
    diag_block = diag_block.transpose(2, 0, 3, 4, 1, 5).reshape(slot_count * grid_size * TILE, -1)
    diag_block = diag_block[:pivot_count, :pivot_count]
    diag_factor, block_inverses = factor_pivots(diag_block)
    if tile_count & (tile_count - 1):
        eye = jnp.eye(pivot_count, dtype=jnp.float32)
        diag_inverse = jnp.tril(jax.scipy.linalg.solve_triangular(diag_factor, eye, lower=True))
    else:
        diag_inverse = lower_inverse(diag_factor, block_inverses)
    col_pieces = lax.all_gather(front_work[:, :width].T, "col", axis=0)
    panel_rows = pivot_order(col_pieces, slot_count, tile_count)
    row_pieces = lax.all_gather(front_work[:width, :], "row", axis=0)
    panel_cols = pivot_order(row_pieces, slot_count, tile_count)
    both = jnp.concatenate([panel_rows, panel_cols], axis=1)
    solved = jnp.dot(
        diag_inverse, both, precision=lax.Precision.HIGH, preferred_element_type=jnp.float32
    )
    solved_rows = solved[:, :local_count].T
    solved_cols = solved[:, local_count:].T
    within = jnp.arange(local_count, dtype=jnp.int32)
    row_index = within // TILE * grid_size * TILE + my_row * TILE + within % TILE
    col_index = within // TILE * grid_size * TILE + my_col * TILE + within % TILE
    rows_after = (row_index >= pivot_count)[:, None]
    cols_after = (col_index >= pivot_count)[None, :]
    update = jnp.dot(
        jnp.where(rows_after, solved_rows, 0.0),
        jnp.where(cols_after.T, solved_cols, 0.0).T,
        precision=lax.Precision.HIGH,
        preferred_element_type=jnp.float32,
    )
    diag_rows = jnp.take(diag_factor, jnp.minimum(row_index, pivot_count - 1), axis=0)
    full_rows = jnp.where(rows_after, solved_rows, diag_rows)
    pivot_cols = jnp.take(full_rows, jnp.minimum(col_index[:width], pivot_count - 1), axis=1)
    trailing = jnp.where(rows_after & cols_after, front_work - update, 0.0)
    head = jnp.where(cols_after[:, :width], trailing[:, :width], pivot_cols)
    return jnp.concatenate([head, trailing[:, width:]], axis=1)


def assemble_by_einsum(child_done, child_maps, parent_own, grid_size, half_index, my_row, my_col):
    local_tiles = child_done.shape[0] // TILE
    pivot_tiles = CHILD_PIVOTS // TILE
    own_map = lax.dynamic_index_in_dim(child_maps, half_index, 0, keepdims=False)
    update_count = child_maps.shape[1]
    slot_ids = jnp.arange(local_tiles, dtype=jnp.int32)
    update_range = jnp.arange(update_count, dtype=jnp.int32)

    def parent_tile(offset):
        update_ids = slot_ids * grid_size + offset - pivot_tiles
        matches = update_ids[:, None] == update_range[None, :]
        return (jnp.sum(jnp.where(matches, own_map[None, :], 0), axis=1), update_ids >= 0)

    row_target, row_valid = parent_tile(my_row)
    col_target, col_valid = parent_tile(my_col)
    parent_row_tiles = parent_own.shape[0] // TILE
    parent_col_tiles = parent_own.shape[1] // TILE
    row_dest = (
        jnp.arange(parent_row_tiles, dtype=jnp.int32)[None, :] * (2 * grid_size)
        + jnp.arange(2, dtype=jnp.int32)[:, None] * grid_size
        + my_row
    )
    row_place = (
        (row_dest[:, :, None] == row_target[None, None, :]) & row_valid[None, None, :]
    ).astype(jnp.float32)
    col_dest = jnp.arange(parent_col_tiles, dtype=jnp.int32) * grid_size + my_col
    col_place = ((col_dest[:, None] == col_target[None, :]) & col_valid[None, :]).astype(
        jnp.float32
    )
    blocks = child_done.reshape(local_tiles, TILE, local_tiles, TILE)
    rows_moved = jnp.einsum("hak,kilj->hailj", row_place, blocks, precision=lax.Precision.HIGHEST)
    both_moved = jnp.einsum(
        "hailj,bl->haibj", rows_moved, col_place, precision=lax.Precision.HIGHEST
    )
    both_moved = both_moved.reshape(2, parent_own.shape[0], parent_own.shape[1])
    kept_part = lax.dynamic_index_in_dim(both_moved, half_index, 0, keepdims=False)
    sent_part = lax.dynamic_index_in_dim(both_moved, 1 - half_index, 0, keepdims=False)
    received = from_partner(sent_part, "half", 0)
    return parent_own + kept_part + received


def tile_source(targets, slot_total):
    slots = jnp.arange(slot_total, dtype=jnp.int32)
    matches = targets[None, :] == slots[:, None]
    source = jnp.sum(jnp.where(matches, jnp.arange(targets.shape[0], dtype=jnp.int32)[None, :], 0), axis=1)
    return source, jnp.any(matches, axis=1)


def place_tiles(block, child_map, row_source, parent_shape, grid_size, row_groups, my_col):
    col_count = block.shape[2] // TILE
    col_ids = jnp.arange(col_count, dtype=jnp.int32) * grid_size + my_col
    col_targets = jnp.take(child_map, col_ids, axis=0) // grid_size
    col_source, col_valid = tile_source(col_targets, parent_shape[1] // TILE)
    row_ids = row_source
    row_targets = jnp.take(child_map, row_ids, axis=0) // row_groups
    row_from, row_valid = tile_source(row_targets, parent_shape[0] // TILE)
    tiles = block.reshape(block.shape[0], TILE, col_count, TILE)
    tiles = jnp.take(tiles, row_from, axis=0)
    tiles = jnp.take(tiles, col_source, axis=2)
    valid = row_valid[:, None, None, None] & col_valid[None, None, :, None]
    return jnp.where(valid, tiles, 0.0).reshape(parent_shape)


def assemble_by_parity(child_done, child_maps, parent_own, grid_size, half_index, my_row, my_col):
    pivot_tiles = CHILD_PIVOTS // TILE
    first_slot = pivot_tiles // grid_size
    update = child_done[first_slot * TILE :, first_slot * TILE :]
    pair_count = update.shape[0] // (2 * TILE)
    by_parity = update.reshape(pair_count, 2, TILE, update.shape[1])
    kept = lax.dynamic_index_in_dim(by_parity, half_index, 1, keepdims=False)
    sent = lax.dynamic_index_in_dim(by_parity, 1 - half_index, 1, keepdims=False)
    received = from_partner(sent, "half", 0)
    pair_ids = jnp.arange(pair_count, dtype=jnp.int32)
    row_update_ids = (2 * pair_ids + half_index) * grid_size + my_row
    own_map = lax.dynamic_index_in_dim(child_maps, half_index, 0, keepdims=False)
    other_map = lax.dynamic_index_in_dim(child_maps, 1 - half_index, 0, keepdims=False)
    row_groups = 2 * grid_size
    kept_part = place_tiles(kept, own_map, row_update_ids, parent_own.shape, grid_size, row_groups, my_col)
    got_part = place_tiles(received, other_map, row_update_ids, parent_own.shape, grid_size, row_groups, my_col)
    return parent_own + kept_part + got_part


def factor_parent(front_work, grid_size, half_index, my_row, my_col):
    row_groups = 2 * grid_size
    parent_row = half_index * grid_size + my_row
    row_count, col_count = front_work.shape
    column = copy_from(front_work[:, :TILE], "col", 0)
    partner = from_partner(column, "half", 0)
    first = half_index == 0
    halves = jnp.stack([jnp.where(first, column, partner), jnp.where(first, partner, column)])
    halves = halves.reshape(2, row_count // TILE, TILE, TILE)
    my_row_cols = jnp.swapaxes(halves, 0, 1).reshape(col_count, TILE)
    pairs = [
        (col * grid_size + row, row * grid_size + col)
        for row in range(grid_size)
        for col in range(grid_size)
    ]
    my_cols = lax.ppermute(my_row_cols, ("row", "col"), pairs)
    diag_block = copy_from(my_row_cols[:TILE], "row", 0)
    diag_factor = jnp.tril(jnp.linalg.cholesky(diag_block))
    eye = jnp.eye(TILE, dtype=jnp.float32)
    inverse = jnp.tril(jax.scipy.linalg.solve_triangular(diag_factor, eye, lower=True))
    solved_rows = jnp.dot(column, inverse.T, precision=lax.Precision.HIGHEST)
    solved_cols = jnp.dot(my_cols, inverse.T, precision=lax.Precision.HIGHEST)
    row_within = jnp.arange(row_count, dtype=jnp.int32)
    col_within = jnp.arange(col_count, dtype=jnp.int32)
    row_index = row_within // TILE * row_groups * TILE + parent_row * TILE + row_within % TILE
    col_index = col_within // TILE * grid_size * TILE + my_col * TILE + col_within % TILE
    return finish_front(front_work, solved_rows, solved_cols, diag_factor, row_index, col_index, TILE)


def finish_front(front_work, solved_rows, solved_cols, diag_factor, row_index, col_index, pivot_count):
    width = TILE * (-(-pivot_count // TILE))
    rows_after = (row_index >= pivot_count)[:, None]
    cols_after = (col_index >= pivot_count)[None, :]
    update = jnp.dot(
        jnp.where(rows_after, solved_rows, 0.0),
        jnp.where(cols_after.T, solved_cols, 0.0).T,
        precision=lax.Precision.HIGHEST,
        preferred_element_type=jnp.float32,
    )
    diag_rows = jnp.take(diag_factor, jnp.minimum(row_index, pivot_count - 1), axis=0)
    full_rows = jnp.where(rows_after, solved_rows, diag_rows)
    pivot_cols = jnp.take(full_rows, jnp.minimum(col_index[:width], pivot_count - 1), axis=1)
    trailing = jnp.where(rows_after & cols_after, front_work - update, 0.0)
    head = jnp.where(cols_after[:, :width], trailing[:, :width], pivot_cols)
    return jnp.concatenate([head, trailing[:, width:]], axis=1)


def local(child_fronts, child_maps, parent_own):
    grid_size = lax.axis_size("row")
    half_index = lax.axis_index("half")
    my_row = lax.axis_index("row")
    my_col = lax.axis_index("col")

    child_done = factor_child(child_fronts[0], CHILD_PIVOTS, grid_size, my_row, my_col)
    pivot_tiles = CHILD_PIVOTS // TILE
    first_slot = pivot_tiles // grid_size
    update_slots = child_done.shape[0] // TILE - first_slot
    parity_fits = CYCLE_TILES % (2 * grid_size) == 0 and pivot_tiles % grid_size == 0
    parity_fits = parity_fits and first_slot % 2 == 0 and update_slots % 2 == 0
    if not parity_fits:
        parent_start = assemble_by_einsum(
            child_done, child_maps, parent_own, grid_size, half_index, my_row, my_col
        )
    else:
        parent_start = assemble_by_parity(
            child_done, child_maps, parent_own, grid_size, half_index, my_row, my_col
        )

    parent_done = factor_parent(parent_start, grid_size, half_index, my_row, my_col)
    return (child_done[None], parent_done)


def solution(mesh):
    in_specs = (P("half", "row", "col"), P(), P(("half", "row"), "col"))
    out_specs = (P("half", "row", "col"), P(("half", "row"), "col"))
    return jax.shard_map(local, mesh=mesh, in_specs=in_specs, out_specs=out_specs, check_vma=False)
```

```python
import jax
import jax.numpy as jnp
from jax import lax
from jax.sharding import PartitionSpec as P

TILE = 128
CHILD_PIVOTS = 1024
PARENT_PIVOTS = 128
CYCLE_TILES = 16


def spread(shard, axis, root):
    mine = lax.axis_index(axis) == root
    return lax.psum(jnp.where(mine, shard, jnp.zeros_like(shard)), axis)


def copy_from(shard, axis, root):
    size = lax.axis_size(axis)
    mine = lax.axis_index(axis) == root
    total = jnp.where(mine, shard, jnp.zeros_like(shard))
    for target in range(size):
        if target != root:
            total = total + lax.ppermute(shard, axis, [(root, target)])
    return total


def from_partner(shard, axis, distance):
    return lax.ppermute(shard, axis, [(i, i ^ 1 << distance) for i in range(lax.axis_size(axis))])


def pivot_order(pieces, slot_count, tile_count):
    group_count, rest = pieces.shape[0], pieces.shape[2:]
    shaped = pieces.reshape((group_count, slot_count, TILE) + rest)
    shaped = jnp.moveaxis(shaped, 0, 1).reshape((slot_count * group_count * TILE,) + rest)
    return shaped[: tile_count * TILE]


def factor_pivots(block):
    order = block.shape[0]
    count = order // TILE
    eye = jnp.eye(TILE, dtype=jnp.float32)
    work = block
    columns = []
    inverses = []
    for step in range(count):
        factor = jnp.tril(jnp.linalg.cholesky(work[:TILE, :TILE]))
        inverse = jnp.tril(jax.scipy.linalg.solve_triangular(factor, eye, lower=True))
        panel = jnp.dot(
            work[TILE:, :TILE], inverse.T, precision=lax.Precision.HIGHEST,
            preferred_element_type=jnp.float32,
        )
        work = work[TILE:, TILE:] - jnp.dot(
            panel, panel.T, precision=lax.Precision.HIGHEST, preferred_element_type=jnp.float32
        )
        columns.append(jnp.concatenate([jnp.zeros((step * TILE, TILE), jnp.float32), factor, panel]))
        inverses.append(inverse)
    return jnp.concatenate(columns, axis=1), jnp.stack(inverses)


def lower_inverse(factor, inverse):
    order = factor.shape[0]
    size = TILE
    while size < order:
        pairs = order // size // 2
        halves = inverse.reshape(pairs, 2, size, size)
        first, second = halves[:, 0], halves[:, 1]
        picks = jnp.arange(pairs)
        lower = factor.reshape(pairs, 2, size, pairs, 2, size)[picks, 1, :, picks, 0, :]
        mixed = jnp.einsum("kab,kbc->kac", second, lower, precision=lax.Precision.HIGHEST)
        mixed = -jnp.einsum("kab,kbc->kac", mixed, first, precision=lax.Precision.HIGHEST)
        top = jnp.concatenate([first, jnp.zeros_like(first)], axis=2)
        bottom = jnp.concatenate([mixed, second], axis=2)
        inverse = jnp.concatenate([top, bottom], axis=1)
        size *= 2
    return inverse[0]


def factor_child(front_work, pivot_count, grid_size, my_row, my_col):
    local_count = front_work.shape[0]
    tile_count = pivot_count // TILE
    slot_count = -(-tile_count // grid_size)
    width = slot_count * TILE
    diag_pieces = lax.all_gather(front_work[:width, :width], ("row", "col"), axis=0)
    diag_block = diag_pieces.reshape(grid_size, grid_size, slot_count, TILE, slot_count, TILE)
    diag_block = diag_block.transpose(2, 0, 3, 4, 1, 5).reshape(slot_count * grid_size * TILE, -1)
    diag_block = diag_block[:pivot_count, :pivot_count]
    diag_factor, block_inverses = factor_pivots(diag_block)
    if tile_count & (tile_count - 1):
        eye = jnp.eye(pivot_count, dtype=jnp.float32)
        diag_inverse = jnp.tril(jax.scipy.linalg.solve_triangular(diag_factor, eye, lower=True))
    else:
        diag_inverse = lower_inverse(diag_factor, block_inverses)
    skip = width if tile_count % grid_size == 0 else 0
    kept_count = local_count - skip
    col_pieces = lax.all_gather(front_work[skip:, :width].T, "col", axis=0)
    panel_rows = pivot_order(col_pieces, slot_count, tile_count)
    row_pieces = lax.all_gather(front_work[:width, skip:], "row", axis=0)
    panel_cols = pivot_order(row_pieces, slot_count, tile_count)
    both = jnp.concatenate([panel_rows, panel_cols], axis=1)
    solved = jnp.dot(
        diag_inverse, both, precision=lax.Precision.HIGH, preferred_element_type=jnp.float32
    )
    lead = jnp.zeros((skip, pivot_count), jnp.float32)
    solved_rows = jnp.concatenate([lead, solved[:, :kept_count].T])
    solved_cols = jnp.concatenate([lead, solved[:, kept_count:].T])
    within = jnp.arange(local_count, dtype=jnp.int32)
    row_index = within // TILE * grid_size * TILE + my_row * TILE + within % TILE
    col_index = within // TILE * grid_size * TILE + my_col * TILE + within % TILE
    rows_after = (row_index >= pivot_count)[:, None]
    cols_after = (col_index >= pivot_count)[None, :]
    update = jnp.dot(
        jnp.where(rows_after, solved_rows, 0.0),
        jnp.where(cols_after.T, solved_cols, 0.0).T,
        precision=lax.Precision.HIGH,
        preferred_element_type=jnp.float32,
    )
    diag_rows = jnp.take(diag_factor, jnp.minimum(row_index, pivot_count - 1), axis=0)
    full_rows = jnp.where(rows_after, solved_rows, diag_rows)
    pivot_cols = jnp.take(full_rows, jnp.minimum(col_index[:width], pivot_count - 1), axis=1)
    trailing = jnp.where(rows_after & cols_after, front_work - update, 0.0)
    head = jnp.where(cols_after[:, :width], trailing[:, :width], pivot_cols)
    return jnp.concatenate([head, trailing[:, width:]], axis=1)


def assemble_by_einsum(child_done, child_maps, parent_own, grid_size, half_index, my_row, my_col):
    local_tiles = child_done.shape[0] // TILE
    pivot_tiles = CHILD_PIVOTS // TILE
    own_map = lax.dynamic_index_in_dim(child_maps, half_index, 0, keepdims=False)
    update_count = child_maps.shape[1]
    slot_ids = jnp.arange(local_tiles, dtype=jnp.int32)
    update_range = jnp.arange(update_count, dtype=jnp.int32)

    def parent_tile(offset):
        update_ids = slot_ids * grid_size + offset - pivot_tiles
        matches = update_ids[:, None] == update_range[None, :]
        return (jnp.sum(jnp.where(matches, own_map[None, :], 0), axis=1), update_ids >= 0)

    row_target, row_valid = parent_tile(my_row)
    col_target, col_valid = parent_tile(my_col)
    parent_row_tiles = parent_own.shape[0] // TILE
    parent_col_tiles = parent_own.shape[1] // TILE
    row_dest = (
        jnp.arange(parent_row_tiles, dtype=jnp.int32)[None, :] * (2 * grid_size)
        + jnp.arange(2, dtype=jnp.int32)[:, None] * grid_size
        + my_row
    )
    row_place = (
        (row_dest[:, :, None] == row_target[None, None, :]) & row_valid[None, None, :]
    ).astype(jnp.float32)
    col_dest = jnp.arange(parent_col_tiles, dtype=jnp.int32) * grid_size + my_col
    col_place = ((col_dest[:, None] == col_target[None, :]) & col_valid[None, :]).astype(
        jnp.float32
    )
    blocks = child_done.reshape(local_tiles, TILE, local_tiles, TILE)
    rows_moved = jnp.einsum("hak,kilj->hailj", row_place, blocks, precision=lax.Precision.HIGHEST)
    both_moved = jnp.einsum(
        "hailj,bl->haibj", rows_moved, col_place, precision=lax.Precision.HIGHEST
    )
    both_moved = both_moved.reshape(2, parent_own.shape[0], parent_own.shape[1])
    kept_part = lax.dynamic_index_in_dim(both_moved, half_index, 0, keepdims=False)
    sent_part = lax.dynamic_index_in_dim(both_moved, 1 - half_index, 0, keepdims=False)
    received = from_partner(sent_part, "half", 0)
    return parent_own + kept_part + received


def tile_source(targets, slot_total):
    slots = jnp.arange(slot_total, dtype=jnp.int32)
    matches = targets[None, :] == slots[:, None]
    source = jnp.sum(jnp.where(matches, jnp.arange(targets.shape[0], dtype=jnp.int32)[None, :], 0), axis=1)
    return source, jnp.any(matches, axis=1)


def place_tiles(block, child_map, row_source, parent_shape, grid_size, row_groups, my_col):
    col_count = block.shape[2] // TILE
    col_ids = jnp.arange(col_count, dtype=jnp.int32) * grid_size + my_col
    col_targets = jnp.take(child_map, col_ids, axis=0) // grid_size
    col_source, col_valid = tile_source(col_targets, parent_shape[1] // TILE)
    row_ids = row_source
    row_targets = jnp.take(child_map, row_ids, axis=0) // row_groups
    row_from, row_valid = tile_source(row_targets, parent_shape[0] // TILE)
    tiles = block.reshape(block.shape[0], TILE, col_count, TILE)
    tiles = jnp.take(tiles, row_from, axis=0)
    tiles = jnp.take(tiles, col_source, axis=2)
    valid = row_valid[:, None, None, None] & col_valid[None, None, :, None]
    return jnp.where(valid, tiles, 0.0).reshape(parent_shape)


def assemble_by_parity(child_done, child_maps, parent_own, grid_size, half_index, my_row, my_col):
    pivot_tiles = CHILD_PIVOTS // TILE
    first_slot = pivot_tiles // grid_size
    update = child_done[first_slot * TILE :, first_slot * TILE :]
    pair_count = update.shape[0] // (2 * TILE)
    by_parity = update.reshape(pair_count, 2, TILE, update.shape[1])
    kept = lax.dynamic_index_in_dim(by_parity, half_index, 1, keepdims=False)
    sent = lax.dynamic_index_in_dim(by_parity, 1 - half_index, 1, keepdims=False)
    received = from_partner(sent, "half", 0)
    pair_ids = jnp.arange(pair_count, dtype=jnp.int32)
    row_update_ids = (2 * pair_ids + half_index) * grid_size + my_row
    own_map = lax.dynamic_index_in_dim(child_maps, half_index, 0, keepdims=False)
    other_map = lax.dynamic_index_in_dim(child_maps, 1 - half_index, 0, keepdims=False)
    row_groups = 2 * grid_size
    kept_part = place_tiles(kept, own_map, row_update_ids, parent_own.shape, grid_size, row_groups, my_col)
    got_part = place_tiles(received, other_map, row_update_ids, parent_own.shape, grid_size, row_groups, my_col)
    return parent_own + kept_part + got_part


def factor_parent(front_work, grid_size, half_index, my_row, my_col):
    row_groups = 2 * grid_size
    parent_row = half_index * grid_size + my_row
    row_count, col_count = front_work.shape
    column = copy_from(front_work[:, :TILE], "col", 0)
    partner = from_partner(column, "half", 0)
    first = half_index == 0
    halves = jnp.stack([jnp.where(first, column, partner), jnp.where(first, partner, column)])
    halves = halves.reshape(2, row_count // TILE, TILE, TILE)
    my_row_cols = jnp.swapaxes(halves, 0, 1).reshape(col_count, TILE)
    pairs = [
        (col * grid_size + row, row * grid_size + col)
        for row in range(grid_size)
        for col in range(grid_size)
    ]
    my_cols = lax.ppermute(my_row_cols, ("row", "col"), pairs)
    diag_block = copy_from(my_row_cols[:TILE], "row", 0)
    diag_factor = jnp.tril(jnp.linalg.cholesky(diag_block))
    eye = jnp.eye(TILE, dtype=jnp.float32)
    inverse = jnp.tril(jax.scipy.linalg.solve_triangular(diag_factor, eye, lower=True))
    solved_rows = jnp.dot(column, inverse.T, precision=lax.Precision.HIGHEST)
    solved_cols = jnp.dot(my_cols, inverse.T, precision=lax.Precision.HIGHEST)
    row_within = jnp.arange(row_count, dtype=jnp.int32)
    col_within = jnp.arange(col_count, dtype=jnp.int32)
    row_index = row_within // TILE * row_groups * TILE + parent_row * TILE + row_within % TILE
    col_index = col_within // TILE * grid_size * TILE + my_col * TILE + col_within % TILE
    return finish_front(front_work, solved_rows, solved_cols, diag_factor, row_index, col_index, TILE)


def finish_front(front_work, solved_rows, solved_cols, diag_factor, row_index, col_index, pivot_count):
    width = TILE * (-(-pivot_count // TILE))
    rows_after = (row_index >= pivot_count)[:, None]
    cols_after = (col_index >= pivot_count)[None, :]
    update = jnp.dot(
        jnp.where(rows_after, solved_rows, 0.0),
        jnp.where(cols_after.T, solved_cols, 0.0).T,
        precision=lax.Precision.HIGHEST,
        preferred_element_type=jnp.float32,
    )
    diag_rows = jnp.take(diag_factor, jnp.minimum(row_index, pivot_count - 1), axis=0)
    full_rows = jnp.where(rows_after, solved_rows, diag_rows)
    pivot_cols = jnp.take(full_rows, jnp.minimum(col_index[:width], pivot_count - 1), axis=1)
    trailing = jnp.where(rows_after & cols_after, front_work - update, 0.0)
    head = jnp.where(cols_after[:, :width], trailing[:, :width], pivot_cols)
    return jnp.concatenate([head, trailing[:, width:]], axis=1)


def local(child_fronts, child_maps, parent_own):
    grid_size = lax.axis_size("row")
    half_index = lax.axis_index("half")
    my_row = lax.axis_index("row")
    my_col = lax.axis_index("col")

    child_done = factor_child(child_fronts[0], CHILD_PIVOTS, grid_size, my_row, my_col)
    pivot_tiles = CHILD_PIVOTS // TILE
    first_slot = pivot_tiles // grid_size
    update_slots = child_done.shape[0] // TILE - first_slot
    parity_fits = CYCLE_TILES % (2 * grid_size) == 0 and pivot_tiles % grid_size == 0
    parity_fits = parity_fits and first_slot % 2 == 0 and update_slots % 2 == 0
    if not parity_fits:
        parent_start = assemble_by_einsum(
            child_done, child_maps, parent_own, grid_size, half_index, my_row, my_col
        )
    else:
        parent_start = assemble_by_parity(
            child_done, child_maps, parent_own, grid_size, half_index, my_row, my_col
        )

    parent_done = factor_parent(parent_start, grid_size, half_index, my_row, my_col)
    return (child_done[None], parent_done)


def solution(mesh):
    in_specs = (P("half", "row", "col"), P(), P(("half", "row"), "col"))
    out_specs = (P("half", "row", "col"), P(("half", "row"), "col"))
    return jax.shard_map(local, mesh=mesh, in_specs=in_specs, out_specs=out_specs, check_vma=False)
```

```python
import jax
import jax.numpy as jnp
from jax import lax
from jax.sharding import PartitionSpec as P

TILE = 128
CHILD_PIVOTS = 1024
PARENT_PIVOTS = 128
CYCLE_TILES = 16


def spread(shard, axis, root):
    mine = lax.axis_index(axis) == root
    return lax.psum(jnp.where(mine, shard, jnp.zeros_like(shard)), axis)


def copy_from(shard, axis, root):
    size = lax.axis_size(axis)
    mine = lax.axis_index(axis) == root
    total = jnp.where(mine, shard, jnp.zeros_like(shard))
    for target in range(size):
        if target != root:
            total = total + lax.ppermute(shard, axis, [(root, target)])
    return total


def from_partner(shard, axis, distance):
    return lax.ppermute(shard, axis, [(i, i ^ 1 << distance) for i in range(lax.axis_size(axis))])


def pivot_order(pieces, slot_count, tile_count):
    group_count, rest = pieces.shape[0], pieces.shape[2:]
    shaped = pieces.reshape((group_count, slot_count, TILE) + rest)
    shaped = jnp.moveaxis(shaped, 0, 1).reshape((slot_count * group_count * TILE,) + rest)
    return shaped[: tile_count * TILE]


def factor_pivots(block):
    order = block.shape[0]
    count = order // TILE
    eye = jnp.eye(TILE, dtype=jnp.float32)
    work = block
    columns = []
    inverses = []
    for step in range(count):
        factor = jnp.tril(jnp.linalg.cholesky(work[:TILE, :TILE]))
        inverse = jnp.tril(jax.scipy.linalg.solve_triangular(factor, eye, lower=True))
        panel = jnp.dot(
            work[TILE:, :TILE], inverse.T, precision=lax.Precision.HIGHEST,
            preferred_element_type=jnp.float32,
        )
        work = work[TILE:, TILE:] - jnp.dot(
            panel, panel.T, precision=lax.Precision.HIGHEST, preferred_element_type=jnp.float32
        )
        columns.append(jnp.concatenate([jnp.zeros((step * TILE, TILE), jnp.float32), factor, panel]))
        inverses.append(inverse)
    return jnp.concatenate(columns, axis=1), jnp.stack(inverses)


def lower_inverse(factor, inverse):
    order = factor.shape[0]
    size = TILE
    while size < order:
        pairs = order // size // 2
        halves = inverse.reshape(pairs, 2, size, size)
        first, second = halves[:, 0], halves[:, 1]
        lower = jnp.stack(
            [
                factor[(2 * pair + 1) * size : (2 * pair + 2) * size, 2 * pair * size : (2 * pair + 1) * size]
                for pair in range(pairs)
            ]
        )
        mixed = jnp.einsum("kab,kbc->kac", second, lower, precision=lax.Precision.HIGHEST)
        mixed = -jnp.einsum("kab,kbc->kac", mixed, first, precision=lax.Precision.HIGHEST)
        top = jnp.concatenate([first, jnp.zeros_like(first)], axis=2)
        bottom = jnp.concatenate([mixed, second], axis=2)
        inverse = jnp.concatenate([top, bottom], axis=1)
        size *= 2
    return inverse[0]


def factor_child(front_work, pivot_count, grid_size, my_row, my_col):
    local_count = front_work.shape[0]
    tile_count = pivot_count // TILE
    slot_count = -(-tile_count // grid_size)
    width = slot_count * TILE
    diag_pieces = lax.all_gather(front_work[:width, :width], ("row", "col"), axis=0)
    diag_block = diag_pieces.reshape(grid_size, grid_size, slot_count, TILE, slot_count, TILE)
    diag_block = diag_block.transpose(2, 0, 3, 4, 1, 5).reshape(slot_count * grid_size * TILE, -1)
    diag_block = diag_block[:pivot_count, :pivot_count]
    diag_factor, block_inverses = factor_pivots(diag_block)
    if tile_count & (tile_count - 1):
        eye = jnp.eye(pivot_count, dtype=jnp.float32)
        diag_inverse = jnp.tril(jax.scipy.linalg.solve_triangular(diag_factor, eye, lower=True))
    else:
        diag_inverse = lower_inverse(diag_factor, block_inverses)
    skip = width if tile_count % grid_size == 0 else 0
    kept_count = local_count - skip
    col_pieces = lax.all_gather(front_work[skip:, :width].T, "col", axis=0)
    panel_rows = pivot_order(col_pieces, slot_count, tile_count)
    row_pieces = lax.all_gather(front_work[:width, skip:], "row", axis=0)
    panel_cols = pivot_order(row_pieces, slot_count, tile_count)
    if slot_count * grid_size == tile_count:
        gathered_inverse = diag_inverse.reshape(pivot_count, slot_count, grid_size, TILE)
        gathered_inverse = gathered_inverse.swapaxes(1, 2).reshape(pivot_count, pivot_count)
        solved_by_rows = jnp.dot(
            gathered_inverse, col_pieces.reshape(pivot_count, kept_count),
            precision=lax.Precision.HIGH, preferred_element_type=jnp.float32,
        )
        solved_by_cols = jnp.dot(
            gathered_inverse, row_pieces.reshape(pivot_count, kept_count),
            precision=lax.Precision.HIGH, preferred_element_type=jnp.float32,
        )
    else:
        both = jnp.concatenate([panel_rows, panel_cols], axis=1)
        solved = jnp.dot(
            diag_inverse, both, precision=lax.Precision.HIGH, preferred_element_type=jnp.float32
        )
        solved_by_rows = solved[:, :kept_count]
        solved_by_cols = solved[:, kept_count:]
    lead = jnp.zeros((skip, pivot_count), jnp.float32)
    solved_rows = jnp.concatenate([lead, solved_by_rows.T])
    solved_cols = jnp.concatenate([lead, solved_by_cols.T])
    within = jnp.arange(local_count, dtype=jnp.int32)
    row_index = within // TILE * grid_size * TILE + my_row * TILE + within % TILE
    col_index = within // TILE * grid_size * TILE + my_col * TILE + within % TILE
    rows_after = (row_index >= pivot_count)[:, None]
    cols_after = (col_index >= pivot_count)[None, :]
    update = jnp.dot(
        jnp.where(rows_after, solved_rows, 0.0),
        jnp.where(cols_after.T, solved_cols, 0.0).T,
        precision=lax.Precision.HIGH,
        preferred_element_type=jnp.float32,
    )
    diag_rows = jnp.take(diag_factor, jnp.minimum(row_index, pivot_count - 1), axis=0)
    full_rows = jnp.where(rows_after, solved_rows, diag_rows)
    pivot_cols = jnp.take(full_rows, jnp.minimum(col_index[:width], pivot_count - 1), axis=1)
    trailing = jnp.where(rows_after & cols_after, front_work - update, 0.0)
    head = jnp.where(cols_after[:, :width], trailing[:, :width], pivot_cols)
    return jnp.concatenate([head, trailing[:, width:]], axis=1)


def assemble_by_einsum(child_done, child_maps, parent_own, grid_size, half_index, my_row, my_col):
    local_tiles = child_done.shape[0] // TILE
    pivot_tiles = CHILD_PIVOTS // TILE
    own_map = lax.dynamic_index_in_dim(child_maps, half_index, 0, keepdims=False)
    update_count = child_maps.shape[1]
    slot_ids = jnp.arange(local_tiles, dtype=jnp.int32)
    update_range = jnp.arange(update_count, dtype=jnp.int32)

    def parent_tile(offset):
        update_ids = slot_ids * grid_size + offset - pivot_tiles
        matches = update_ids[:, None] == update_range[None, :]
        return (jnp.sum(jnp.where(matches, own_map[None, :], 0), axis=1), update_ids >= 0)

    row_target, row_valid = parent_tile(my_row)
    col_target, col_valid = parent_tile(my_col)
    parent_row_tiles = parent_own.shape[0] // TILE
    parent_col_tiles = parent_own.shape[1] // TILE
    row_dest = (
        jnp.arange(parent_row_tiles, dtype=jnp.int32)[None, :] * (2 * grid_size)
        + jnp.arange(2, dtype=jnp.int32)[:, None] * grid_size
        + my_row
    )
    row_place = (
        (row_dest[:, :, None] == row_target[None, None, :]) & row_valid[None, None, :]
    ).astype(jnp.float32)
    col_dest = jnp.arange(parent_col_tiles, dtype=jnp.int32) * grid_size + my_col
    col_place = ((col_dest[:, None] == col_target[None, :]) & col_valid[None, :]).astype(
        jnp.float32
    )
    blocks = child_done.reshape(local_tiles, TILE, local_tiles, TILE)
    rows_moved = jnp.einsum("hak,kilj->hailj", row_place, blocks, precision=lax.Precision.HIGHEST)
    both_moved = jnp.einsum(
        "hailj,bl->haibj", rows_moved, col_place, precision=lax.Precision.HIGHEST
    )
    both_moved = both_moved.reshape(2, parent_own.shape[0], parent_own.shape[1])
    kept_part = lax.dynamic_index_in_dim(both_moved, half_index, 0, keepdims=False)
    sent_part = lax.dynamic_index_in_dim(both_moved, 1 - half_index, 0, keepdims=False)
    received = from_partner(sent_part, "half", 0)
    return parent_own + kept_part + received


def tile_source(targets, slot_total):
    slots = jnp.arange(slot_total, dtype=jnp.int32)
    matches = targets[None, :] == slots[:, None]
    source = jnp.sum(jnp.where(matches, jnp.arange(targets.shape[0], dtype=jnp.int32)[None, :], 0), axis=1)
    return source, jnp.any(matches, axis=1)


def place_tiles(block, child_map, row_source, parent_shape, grid_size, row_groups, my_col):
    col_count = block.shape[2] // TILE
    col_ids = jnp.arange(col_count, dtype=jnp.int32) * grid_size + my_col
    col_targets = jnp.take(child_map, col_ids, axis=0) // grid_size
    col_source, col_valid = tile_source(col_targets, parent_shape[1] // TILE)
    row_ids = row_source
    row_targets = jnp.take(child_map, row_ids, axis=0) // row_groups
    row_from, row_valid = tile_source(row_targets, parent_shape[0] // TILE)
    tiles = block.reshape(block.shape[0], TILE, col_count, TILE)
    tiles = jnp.take(tiles, row_from, axis=0)
    tiles = jnp.take(tiles, col_source, axis=2)
    valid = row_valid[:, None, None, None] & col_valid[None, None, :, None]
    return jnp.where(valid, tiles, 0.0).reshape(parent_shape)


def assemble_by_parity(child_done, child_maps, parent_own, grid_size, half_index, my_row, my_col):
    pivot_tiles = CHILD_PIVOTS // TILE
    first_slot = pivot_tiles // grid_size
    update = child_done[first_slot * TILE :, first_slot * TILE :]
    pair_count = update.shape[0] // (2 * TILE)
    by_parity = update.reshape(pair_count, 2, TILE, update.shape[1])
    kept = lax.dynamic_index_in_dim(by_parity, half_index, 1, keepdims=False)
    sent = lax.dynamic_index_in_dim(by_parity, 1 - half_index, 1, keepdims=False)
    received = from_partner(sent, "half", 0)
    pair_ids = jnp.arange(pair_count, dtype=jnp.int32)
    row_update_ids = (2 * pair_ids + half_index) * grid_size + my_row
    own_map = lax.dynamic_index_in_dim(child_maps, half_index, 0, keepdims=False)
    other_map = lax.dynamic_index_in_dim(child_maps, 1 - half_index, 0, keepdims=False)
    row_groups = 2 * grid_size
    kept_part = place_tiles(kept, own_map, row_update_ids, parent_own.shape, grid_size, row_groups, my_col)
    got_part = place_tiles(received, other_map, row_update_ids, parent_own.shape, grid_size, row_groups, my_col)
    return parent_own + kept_part + got_part


def factor_parent(front_work, grid_size, half_index, my_row, my_col):
    row_groups = 2 * grid_size
    parent_row = half_index * grid_size + my_row
    row_count, col_count = front_work.shape
    column = copy_from(front_work[:, :TILE], "col", 0)
    partner = from_partner(column, "half", 0)
    first = half_index == 0
    halves = jnp.stack([jnp.where(first, column, partner), jnp.where(first, partner, column)])
    halves = halves.reshape(2, row_count // TILE, TILE, TILE)
    my_row_cols = jnp.swapaxes(halves, 0, 1).reshape(col_count, TILE)
    pairs = [
        (col * grid_size + row, row * grid_size + col)
        for row in range(grid_size)
        for col in range(grid_size)
    ]
    my_cols = lax.ppermute(my_row_cols, ("row", "col"), pairs)
    diag_block = copy_from(my_row_cols[:TILE], "row", 0)
    diag_factor = jnp.tril(jnp.linalg.cholesky(diag_block))
    eye = jnp.eye(TILE, dtype=jnp.float32)
    inverse = jnp.tril(jax.scipy.linalg.solve_triangular(diag_factor, eye, lower=True))
    solved_rows = jnp.dot(column, inverse.T, precision=lax.Precision.HIGHEST)
    solved_cols = jnp.dot(my_cols, inverse.T, precision=lax.Precision.HIGHEST)
    row_within = jnp.arange(row_count, dtype=jnp.int32)
    col_within = jnp.arange(col_count, dtype=jnp.int32)
    row_index = row_within // TILE * row_groups * TILE + parent_row * TILE + row_within % TILE
    col_index = col_within // TILE * grid_size * TILE + my_col * TILE + col_within % TILE
    return finish_front(front_work, solved_rows, solved_cols, diag_factor, row_index, col_index, TILE)


def finish_front(front_work, solved_rows, solved_cols, diag_factor, row_index, col_index, pivot_count):
    width = TILE * (-(-pivot_count // TILE))
    rows_after = (row_index >= pivot_count)[:, None]
    cols_after = (col_index >= pivot_count)[None, :]
    update = jnp.dot(
        jnp.where(rows_after, solved_rows, 0.0),
        jnp.where(cols_after.T, solved_cols, 0.0).T,
        precision=lax.Precision.HIGHEST,
        preferred_element_type=jnp.float32,
    )
    diag_rows = jnp.take(diag_factor, jnp.minimum(row_index, pivot_count - 1), axis=0)
    full_rows = jnp.where(rows_after, solved_rows, diag_rows)
    pivot_cols = jnp.take(full_rows, jnp.minimum(col_index[:width], pivot_count - 1), axis=1)
    trailing = jnp.where(rows_after & cols_after, front_work - update, 0.0)
    head = jnp.where(cols_after[:, :width], trailing[:, :width], pivot_cols)
    return jnp.concatenate([head, trailing[:, width:]], axis=1)


def local(child_fronts, child_maps, parent_own):
    grid_size = lax.axis_size("row")
    half_index = lax.axis_index("half")
    my_row = lax.axis_index("row")
    my_col = lax.axis_index("col")

    child_done = factor_child(child_fronts[0], CHILD_PIVOTS, grid_size, my_row, my_col)
    pivot_tiles = CHILD_PIVOTS // TILE
    first_slot = pivot_tiles // grid_size
    update_slots = child_done.shape[0] // TILE - first_slot
    parity_fits = CYCLE_TILES % (2 * grid_size) == 0 and pivot_tiles % grid_size == 0
    parity_fits = parity_fits and first_slot % 2 == 0 and update_slots % 2 == 0
    if not parity_fits:
        parent_start = assemble_by_einsum(
            child_done, child_maps, parent_own, grid_size, half_index, my_row, my_col
        )
    else:
        parent_start = assemble_by_parity(
            child_done, child_maps, parent_own, grid_size, half_index, my_row, my_col
        )

    parent_done = factor_parent(parent_start, grid_size, half_index, my_row, my_col)
    return (child_done[None], parent_done)


def solution(mesh):
    in_specs = (P("half", "row", "col"), P(), P(("half", "row"), "col"))
    out_specs = (P("half", "row", "col"), P(("half", "row"), "col"))
    return jax.shard_map(local, mesh=mesh, in_specs=in_specs, out_specs=out_specs, check_vma=False)
```

```python
import jax
import jax.numpy as jnp
from jax import lax
from jax.sharding import PartitionSpec as P

TILE = 128
CHILD_PIVOTS = 1024
PARENT_PIVOTS = 128
CYCLE_TILES = 16


def spread(shard, axis, root):
    mine = lax.axis_index(axis) == root
    return lax.psum(jnp.where(mine, shard, jnp.zeros_like(shard)), axis)


def copy_from(shard, axis, root):
    size = lax.axis_size(axis)
    mine = lax.axis_index(axis) == root
    total = jnp.where(mine, shard, jnp.zeros_like(shard))
    for target in range(size):
        if target != root:
            total = total + lax.ppermute(shard, axis, [(root, target)])
    return total


def from_partner(shard, axis, distance):
    return lax.ppermute(shard, axis, [(i, i ^ 1 << distance) for i in range(lax.axis_size(axis))])


def pivot_order(pieces, slot_count, tile_count):
    group_count, rest = pieces.shape[0], pieces.shape[2:]
    shaped = pieces.reshape((group_count, slot_count, TILE) + rest)
    shaped = jnp.moveaxis(shaped, 0, 1).reshape((slot_count * group_count * TILE,) + rest)
    return shaped[: tile_count * TILE]


def factor_pivots(block):
    order = block.shape[0]
    count = order // TILE
    eye = jnp.eye(TILE, dtype=jnp.float32)
    work = block
    columns = []
    inverses = []
    for step in range(count):
        factor = jnp.tril(jnp.linalg.cholesky(work[:TILE, :TILE]))
        inverse = jnp.tril(jax.scipy.linalg.solve_triangular(factor, eye, lower=True))
        panel = jnp.dot(
            work[TILE:, :TILE], inverse.T, precision=lax.Precision.HIGH,
            preferred_element_type=jnp.float32,
        )
        work = work[TILE:, TILE:] - jnp.dot(
            panel, panel.T, precision=lax.Precision.HIGH, preferred_element_type=jnp.float32
        )
        columns.append(jnp.concatenate([jnp.zeros((step * TILE, TILE), jnp.float32), factor, panel]))
        inverses.append(inverse)
    return jnp.concatenate(columns, axis=1), jnp.stack(inverses)


def lower_inverse(factor, inverse):
    order = factor.shape[0]
    size = TILE
    while size < order:
        pairs = order // size // 2
        halves = inverse.reshape(pairs, 2, size, size)
        first, second = halves[:, 0], halves[:, 1]
        lower = jnp.stack(
            [
                factor[(2 * pair + 1) * size : (2 * pair + 2) * size, 2 * pair * size : (2 * pair + 1) * size]
                for pair in range(pairs)
            ]
        )
        mixed = jnp.einsum("kab,kbc->kac", second, lower, precision=lax.Precision.HIGH)
        mixed = -jnp.einsum("kab,kbc->kac", mixed, first, precision=lax.Precision.HIGH)
        top = jnp.concatenate([first, jnp.zeros_like(first)], axis=2)
        bottom = jnp.concatenate([mixed, second], axis=2)
        inverse = jnp.concatenate([top, bottom], axis=1)
        size *= 2
    return inverse[0]


def factor_child(front_work, pivot_count, grid_size, my_row, my_col):
    local_count = front_work.shape[0]
    tile_count = pivot_count // TILE
    slot_count = -(-tile_count // grid_size)
    width = slot_count * TILE
    diag_pieces = lax.all_gather(front_work[:width, :width], ("row", "col"), axis=0)
    diag_block = diag_pieces.reshape(grid_size, grid_size, slot_count, TILE, slot_count, TILE)
    diag_block = diag_block.transpose(2, 0, 3, 4, 1, 5).reshape(slot_count * grid_size * TILE, -1)
    diag_block = diag_block[:pivot_count, :pivot_count]
    diag_factor, block_inverses = factor_pivots(diag_block)
    if tile_count & (tile_count - 1):
        eye = jnp.eye(pivot_count, dtype=jnp.float32)
        diag_inverse = jnp.tril(jax.scipy.linalg.solve_triangular(diag_factor, eye, lower=True))
    else:
        diag_inverse = lower_inverse(diag_factor, block_inverses)
    skip = width if tile_count % grid_size == 0 else 0
    kept_count = local_count - skip
    col_pieces = lax.all_gather(front_work[skip:, :width].T, "col", axis=0)
    panel_rows = pivot_order(col_pieces, slot_count, tile_count)
    row_pieces = lax.all_gather(front_work[:width, skip:], "row", axis=0)
    panel_cols = pivot_order(row_pieces, slot_count, tile_count)
    if slot_count * grid_size == tile_count:
        gathered_inverse = diag_inverse.reshape(pivot_count, slot_count, grid_size, TILE)
        gathered_inverse = gathered_inverse.swapaxes(1, 2).reshape(pivot_count, pivot_count)
        solved_by_rows = jnp.dot(
            gathered_inverse, col_pieces.reshape(pivot_count, kept_count),
            precision=lax.Precision.HIGH, preferred_element_type=jnp.float32,
        )
        solved_by_cols = jnp.dot(
            gathered_inverse, row_pieces.reshape(pivot_count, kept_count),
            precision=lax.Precision.HIGH, preferred_element_type=jnp.float32,
        )
    else:
        both = jnp.concatenate([panel_rows, panel_cols], axis=1)
        solved = jnp.dot(
            diag_inverse, both, precision=lax.Precision.HIGH, preferred_element_type=jnp.float32
        )
        solved_by_rows = solved[:, :kept_count]
        solved_by_cols = solved[:, kept_count:]
    lead = jnp.zeros((skip, pivot_count), jnp.float32)
    solved_rows = jnp.concatenate([lead, solved_by_rows.T])
    solved_cols = jnp.concatenate([lead, solved_by_cols.T])
    within = jnp.arange(local_count, dtype=jnp.int32)
    row_index = within // TILE * grid_size * TILE + my_row * TILE + within % TILE
    col_index = within // TILE * grid_size * TILE + my_col * TILE + within % TILE
    rows_after = (row_index >= pivot_count)[:, None]
    cols_after = (col_index >= pivot_count)[None, :]
    update = jnp.dot(
        jnp.where(rows_after, solved_rows, 0.0),
        jnp.where(cols_after.T, solved_cols, 0.0).T,
        precision=lax.Precision.HIGH,
        preferred_element_type=jnp.float32,
    )
    diag_rows = jnp.take(diag_factor, jnp.minimum(row_index, pivot_count - 1), axis=0)
    full_rows = jnp.where(rows_after, solved_rows, diag_rows)
    pivot_cols = jnp.take(full_rows, jnp.minimum(col_index[:width], pivot_count - 1), axis=1)
    trailing = jnp.where(rows_after & cols_after, front_work - update, 0.0)
    head = jnp.where(cols_after[:, :width], trailing[:, :width], pivot_cols)
    return jnp.concatenate([head, trailing[:, width:]], axis=1)


def assemble_by_einsum(child_done, child_maps, parent_own, grid_size, half_index, my_row, my_col):
    local_tiles = child_done.shape[0] // TILE
    pivot_tiles = CHILD_PIVOTS // TILE
    own_map = lax.dynamic_index_in_dim(child_maps, half_index, 0, keepdims=False)
    update_count = child_maps.shape[1]
    slot_ids = jnp.arange(local_tiles, dtype=jnp.int32)
    update_range = jnp.arange(update_count, dtype=jnp.int32)

    def parent_tile(offset):
        update_ids = slot_ids * grid_size + offset - pivot_tiles
        matches = update_ids[:, None] == update_range[None, :]
        return (jnp.sum(jnp.where(matches, own_map[None, :], 0), axis=1), update_ids >= 0)

    row_target, row_valid = parent_tile(my_row)
    col_target, col_valid = parent_tile(my_col)
    parent_row_tiles = parent_own.shape[0] // TILE
    parent_col_tiles = parent_own.shape[1] // TILE
    row_dest = (
        jnp.arange(parent_row_tiles, dtype=jnp.int32)[None, :] * (2 * grid_size)
        + jnp.arange(2, dtype=jnp.int32)[:, None] * grid_size
        + my_row
    )
    row_place = (
        (row_dest[:, :, None] == row_target[None, None, :]) & row_valid[None, None, :]
    ).astype(jnp.float32)
    col_dest = jnp.arange(parent_col_tiles, dtype=jnp.int32) * grid_size + my_col
    col_place = ((col_dest[:, None] == col_target[None, :]) & col_valid[None, :]).astype(
        jnp.float32
    )
    blocks = child_done.reshape(local_tiles, TILE, local_tiles, TILE)
    rows_moved = jnp.einsum("hak,kilj->hailj", row_place, blocks, precision=lax.Precision.HIGHEST)
    both_moved = jnp.einsum(
        "hailj,bl->haibj", rows_moved, col_place, precision=lax.Precision.HIGHEST
    )
    both_moved = both_moved.reshape(2, parent_own.shape[0], parent_own.shape[1])
    kept_part = lax.dynamic_index_in_dim(both_moved, half_index, 0, keepdims=False)
    sent_part = lax.dynamic_index_in_dim(both_moved, 1 - half_index, 0, keepdims=False)
    received = from_partner(sent_part, "half", 0)
    return parent_own + kept_part + received


def tile_source(targets, slot_total):
    slots = jnp.arange(slot_total, dtype=jnp.int32)
    matches = targets[None, :] == slots[:, None]
    source = jnp.sum(jnp.where(matches, jnp.arange(targets.shape[0], dtype=jnp.int32)[None, :], 0), axis=1)
    return source, jnp.any(matches, axis=1)


def place_tiles(block, child_map, row_source, parent_shape, grid_size, row_groups, my_col):
    col_count = block.shape[2] // TILE
    col_ids = jnp.arange(col_count, dtype=jnp.int32) * grid_size + my_col
    col_targets = jnp.take(child_map, col_ids, axis=0) // grid_size
    col_source, col_valid = tile_source(col_targets, parent_shape[1] // TILE)
    row_ids = row_source
    row_targets = jnp.take(child_map, row_ids, axis=0) // row_groups
    row_from, row_valid = tile_source(row_targets, parent_shape[0] // TILE)
    tiles = block.reshape(block.shape[0], TILE, col_count, TILE)
    tiles = jnp.take(tiles, row_from, axis=0)
    tiles = jnp.take(tiles, col_source, axis=2)
    valid = row_valid[:, None, None, None] & col_valid[None, None, :, None]
    return jnp.where(valid, tiles, 0.0).reshape(parent_shape)


def assemble_by_parity(child_done, child_maps, parent_own, grid_size, half_index, my_row, my_col):
    pivot_tiles = CHILD_PIVOTS // TILE
    first_slot = pivot_tiles // grid_size
    update = child_done[first_slot * TILE :, first_slot * TILE :]
    pair_count = update.shape[0] // (2 * TILE)
    by_parity = update.reshape(pair_count, 2, TILE, update.shape[1])
    kept = lax.dynamic_index_in_dim(by_parity, half_index, 1, keepdims=False)
    sent = lax.dynamic_index_in_dim(by_parity, 1 - half_index, 1, keepdims=False)
    received = from_partner(sent, "half", 0)
    pair_ids = jnp.arange(pair_count, dtype=jnp.int32)
    row_update_ids = (2 * pair_ids + half_index) * grid_size + my_row
    own_map = lax.dynamic_index_in_dim(child_maps, half_index, 0, keepdims=False)
    other_map = lax.dynamic_index_in_dim(child_maps, 1 - half_index, 0, keepdims=False)
    row_groups = 2 * grid_size
    kept_part = place_tiles(kept, own_map, row_update_ids, parent_own.shape, grid_size, row_groups, my_col)
    got_part = place_tiles(received, other_map, row_update_ids, parent_own.shape, grid_size, row_groups, my_col)
    return parent_own + kept_part + got_part


def factor_parent(front_work, grid_size, half_index, my_row, my_col):
    row_groups = 2 * grid_size
    parent_row = half_index * grid_size + my_row
    row_count, col_count = front_work.shape
    column = copy_from(front_work[:, :TILE], "col", 0)
    partner = from_partner(column, "half", 0)
    first = half_index == 0
    halves = jnp.stack([jnp.where(first, column, partner), jnp.where(first, partner, column)])
    halves = halves.reshape(2, row_count // TILE, TILE, TILE)
    my_row_cols = jnp.swapaxes(halves, 0, 1).reshape(col_count, TILE)
    pairs = [
        (col * grid_size + row, row * grid_size + col)
        for row in range(grid_size)
        for col in range(grid_size)
    ]
    my_cols = lax.ppermute(my_row_cols, ("row", "col"), pairs)
    diag_block = copy_from(my_row_cols[:TILE], "row", 0)
    diag_factor = jnp.tril(jnp.linalg.cholesky(diag_block))
    eye = jnp.eye(TILE, dtype=jnp.float32)
    inverse = jnp.tril(jax.scipy.linalg.solve_triangular(diag_factor, eye, lower=True))
    solved_rows = jnp.dot(column, inverse.T, precision=lax.Precision.HIGH)
    solved_cols = jnp.dot(my_cols, inverse.T, precision=lax.Precision.HIGH)
    row_within = jnp.arange(row_count, dtype=jnp.int32)
    col_within = jnp.arange(col_count, dtype=jnp.int32)
    row_index = row_within // TILE * row_groups * TILE + parent_row * TILE + row_within % TILE
    col_index = col_within // TILE * grid_size * TILE + my_col * TILE + col_within % TILE
    return finish_front(front_work, solved_rows, solved_cols, diag_factor, row_index, col_index, TILE)


def finish_front(front_work, solved_rows, solved_cols, diag_factor, row_index, col_index, pivot_count):
    width = TILE * (-(-pivot_count // TILE))
    rows_after = (row_index >= pivot_count)[:, None]
    cols_after = (col_index >= pivot_count)[None, :]
    update = jnp.dot(
        jnp.where(rows_after, solved_rows, 0.0),
        jnp.where(cols_after.T, solved_cols, 0.0).T,
        precision=lax.Precision.HIGH,
        preferred_element_type=jnp.float32,
    )
    diag_rows = jnp.take(diag_factor, jnp.minimum(row_index, pivot_count - 1), axis=0)
    full_rows = jnp.where(rows_after, solved_rows, diag_rows)
    pivot_cols = jnp.take(full_rows, jnp.minimum(col_index[:width], pivot_count - 1), axis=1)
    trailing = jnp.where(rows_after & cols_after, front_work - update, 0.0)
    head = jnp.where(cols_after[:, :width], trailing[:, :width], pivot_cols)
    return jnp.concatenate([head, trailing[:, width:]], axis=1)


def local(child_fronts, child_maps, parent_own):
    grid_size = lax.axis_size("row")
    half_index = lax.axis_index("half")
    my_row = lax.axis_index("row")
    my_col = lax.axis_index("col")

    child_done = factor_child(child_fronts[0], CHILD_PIVOTS, grid_size, my_row, my_col)
    pivot_tiles = CHILD_PIVOTS // TILE
    first_slot = pivot_tiles // grid_size
    update_slots = child_done.shape[0] // TILE - first_slot
    parity_fits = CYCLE_TILES % (2 * grid_size) == 0 and pivot_tiles % grid_size == 0
    parity_fits = parity_fits and first_slot % 2 == 0 and update_slots % 2 == 0
    if not parity_fits:
        parent_start = assemble_by_einsum(
            child_done, child_maps, parent_own, grid_size, half_index, my_row, my_col
        )
    else:
        parent_start = assemble_by_parity(
            child_done, child_maps, parent_own, grid_size, half_index, my_row, my_col
        )

    parent_done = factor_parent(parent_start, grid_size, half_index, my_row, my_col)
    return (child_done[None], parent_done)


def solution(mesh):
    in_specs = (P("half", "row", "col"), P(), P(("half", "row"), "col"))
    out_specs = (P("half", "row", "col"), P(("half", "row"), "col"))
    return jax.shard_map(local, mesh=mesh, in_specs=in_specs, out_specs=out_specs, check_vma=False)
```

```python
import jax
import jax.numpy as jnp
from jax import lax
from jax.sharding import PartitionSpec as P

TILE = 128
CHILD_PIVOTS = 1024
PARENT_PIVOTS = 128
CYCLE_TILES = 16


def spread(shard, axis, root):
    mine = lax.axis_index(axis) == root
    return lax.psum(jnp.where(mine, shard, jnp.zeros_like(shard)), axis)


def copy_from(shard, axis, root):
    size = lax.axis_size(axis)
    mine = lax.axis_index(axis) == root
    total = jnp.where(mine, shard, jnp.zeros_like(shard))
    for target in range(size):
        if target != root:
            total = total + lax.ppermute(shard, axis, [(root, target)])
    return total


def from_partner(shard, axis, distance):
    return lax.ppermute(shard, axis, [(i, i ^ 1 << distance) for i in range(lax.axis_size(axis))])


def pivot_order(pieces, slot_count, tile_count):
    group_count, rest = pieces.shape[0], pieces.shape[2:]
    shaped = pieces.reshape((group_count, slot_count, TILE) + rest)
    shaped = jnp.moveaxis(shaped, 0, 1).reshape((slot_count * group_count * TILE,) + rest)
    return shaped[: tile_count * TILE]


def factor_pivots(block):
    order = block.shape[0]
    count = order // TILE
    eye = jnp.eye(TILE, dtype=jnp.float32)
    work = block
    columns = []
    inverses = []
    for step in range(count):
        factor = jnp.tril(jnp.linalg.cholesky(work[:TILE, :TILE]))
        inverse = jnp.tril(jax.scipy.linalg.solve_triangular(factor, eye, lower=True))
        panel = jnp.dot(
            work[TILE:, :TILE], inverse.T, precision=lax.Precision.HIGH,
            preferred_element_type=jnp.float32,
        )
        work = work[TILE:, TILE:] - jnp.dot(
            panel, panel.T, precision=lax.Precision.HIGH, preferred_element_type=jnp.float32
        )
        columns.append(jnp.concatenate([jnp.zeros((step * TILE, TILE), jnp.float32), factor, panel]))
        inverses.append(inverse)
    return jnp.concatenate(columns, axis=1), jnp.stack(inverses)


def lower_inverse(factor, inverse):
    order = factor.shape[0]
    size = TILE
    while size < order:
        pairs = order // size // 2
        halves = inverse.reshape(pairs, 2, size, size)
        first, second = halves[:, 0], halves[:, 1]
        lower = jnp.stack(
            [
                factor[(2 * pair + 1) * size : (2 * pair + 2) * size, 2 * pair * size : (2 * pair + 1) * size]
                for pair in range(pairs)
            ]
        )
        mixed = jnp.einsum("kab,kbc->kac", second, lower, precision=lax.Precision.HIGH)
        mixed = -jnp.einsum("kab,kbc->kac", mixed, first, precision=lax.Precision.HIGH)
        top = jnp.concatenate([first, jnp.zeros_like(first)], axis=2)
        bottom = jnp.concatenate([mixed, second], axis=2)
        inverse = jnp.concatenate([top, bottom], axis=1)
        size *= 2
    return inverse[0]


def factor_child(front_work, pivot_count, grid_size, my_row, my_col):
    local_count = front_work.shape[0]
    tile_count = pivot_count // TILE
    slot_count = -(-tile_count // grid_size)
    width = slot_count * TILE
    diag_pieces = lax.all_gather(front_work[:width, :width], ("row", "col"), axis=0)
    diag_block = diag_pieces.reshape(grid_size, grid_size, slot_count, TILE, slot_count, TILE)
    diag_block = diag_block.transpose(2, 0, 3, 4, 1, 5).reshape(slot_count * grid_size * TILE, -1)
    diag_block = diag_block[:pivot_count, :pivot_count]
    diag_factor, block_inverses = factor_pivots(diag_block)
    if tile_count & (tile_count - 1):
        eye = jnp.eye(pivot_count, dtype=jnp.float32)
        diag_inverse = jnp.tril(jax.scipy.linalg.solve_triangular(diag_factor, eye, lower=True))
    else:
        diag_inverse = lower_inverse(diag_factor, block_inverses)
    skip = width if tile_count % grid_size == 0 else 0
    kept_count = local_count - skip
    col_pieces = lax.all_gather(front_work[skip:, :width].T, "col", axis=0)
    panel_rows = pivot_order(col_pieces, slot_count, tile_count)
    row_pieces = lax.all_gather(front_work[:width, skip:], "row", axis=0)
    panel_cols = pivot_order(row_pieces, slot_count, tile_count)
    if slot_count * grid_size == tile_count:
        gathered_inverse = diag_inverse.reshape(pivot_count, slot_count, grid_size, TILE)
        gathered_inverse = gathered_inverse.swapaxes(1, 2).reshape(pivot_count, pivot_count)
        solved_by_rows = jnp.dot(
            gathered_inverse, col_pieces.reshape(pivot_count, kept_count),
            precision=lax.Precision.HIGH, preferred_element_type=jnp.float32,
        )
        solved_by_cols = jnp.dot(
            gathered_inverse, row_pieces.reshape(pivot_count, kept_count),
            precision=lax.Precision.HIGH, preferred_element_type=jnp.float32,
        )
    else:
        both = jnp.concatenate([panel_rows, panel_cols], axis=1)
        solved = jnp.dot(
            diag_inverse, both, precision=lax.Precision.HIGH, preferred_element_type=jnp.float32
        )
        solved_by_rows = solved[:, :kept_count]
        solved_by_cols = solved[:, kept_count:]
    lead = jnp.zeros((skip, pivot_count), jnp.float32)
    solved_rows = jnp.concatenate([lead, solved_by_rows.T])
    solved_cols = jnp.concatenate([lead, solved_by_cols.T])
    within = jnp.arange(local_count, dtype=jnp.int32)
    row_index = within // TILE * grid_size * TILE + my_row * TILE + within % TILE
    col_index = within // TILE * grid_size * TILE + my_col * TILE + within % TILE
    rows_after = (row_index >= pivot_count)[:, None]
    cols_after = (col_index >= pivot_count)[None, :]
    diag_rows = jnp.take(diag_factor, jnp.minimum(row_index, pivot_count - 1), axis=0)
    full_rows = jnp.where(rows_after, solved_rows, diag_rows)
    pivot_cols = jnp.take(full_rows, jnp.minimum(col_index[:width], pivot_count - 1), axis=1)
    if skip:
        core = front_work[skip:, skip:] - jnp.dot(
            solved_by_rows.T, solved_by_cols, precision=lax.Precision.HIGH,
            preferred_element_type=jnp.float32,
        )
        right = jnp.concatenate([jnp.zeros((skip, kept_count), jnp.float32), core])
        return jnp.concatenate([pivot_cols, right], axis=1)
    update = jnp.dot(
        jnp.where(rows_after, solved_rows, 0.0),
        jnp.where(cols_after.T, solved_cols, 0.0).T,
        precision=lax.Precision.HIGH,
        preferred_element_type=jnp.float32,
    )
    trailing = jnp.where(rows_after & cols_after, front_work - update, 0.0)
    head = jnp.where(cols_after[:, :width], trailing[:, :width], pivot_cols)
    return jnp.concatenate([head, trailing[:, width:]], axis=1)


def assemble_by_einsum(child_done, child_maps, parent_own, grid_size, half_index, my_row, my_col):
    local_tiles = child_done.shape[0] // TILE
    pivot_tiles = CHILD_PIVOTS // TILE
    own_map = lax.dynamic_index_in_dim(child_maps, half_index, 0, keepdims=False)
    update_count = child_maps.shape[1]
    slot_ids = jnp.arange(local_tiles, dtype=jnp.int32)
    update_range = jnp.arange(update_count, dtype=jnp.int32)

    def parent_tile(offset):
        update_ids = slot_ids * grid_size + offset - pivot_tiles
        matches = update_ids[:, None] == update_range[None, :]
        return (jnp.sum(jnp.where(matches, own_map[None, :], 0), axis=1), update_ids >= 0)

    row_target, row_valid = parent_tile(my_row)
    col_target, col_valid = parent_tile(my_col)
    parent_row_tiles = parent_own.shape[0] // TILE
    parent_col_tiles = parent_own.shape[1] // TILE
    row_dest = (
        jnp.arange(parent_row_tiles, dtype=jnp.int32)[None, :] * (2 * grid_size)
        + jnp.arange(2, dtype=jnp.int32)[:, None] * grid_size
        + my_row
    )
    row_place = (
        (row_dest[:, :, None] == row_target[None, None, :]) & row_valid[None, None, :]
    ).astype(jnp.float32)
    col_dest = jnp.arange(parent_col_tiles, dtype=jnp.int32) * grid_size + my_col
    col_place = ((col_dest[:, None] == col_target[None, :]) & col_valid[None, :]).astype(
        jnp.float32
    )
    blocks = child_done.reshape(local_tiles, TILE, local_tiles, TILE)
    rows_moved = jnp.einsum("hak,kilj->hailj", row_place, blocks, precision=lax.Precision.HIGHEST)
    both_moved = jnp.einsum(
        "hailj,bl->haibj", rows_moved, col_place, precision=lax.Precision.HIGHEST
    )
    both_moved = both_moved.reshape(2, parent_own.shape[0], parent_own.shape[1])
    kept_part = lax.dynamic_index_in_dim(both_moved, half_index, 0, keepdims=False)
    sent_part = lax.dynamic_index_in_dim(both_moved, 1 - half_index, 0, keepdims=False)
    received = from_partner(sent_part, "half", 0)
    return parent_own + kept_part + received


def tile_source(targets, slot_total):
    slots = jnp.arange(slot_total, dtype=jnp.int32)
    matches = targets[None, :] == slots[:, None]
    source = jnp.sum(jnp.where(matches, jnp.arange(targets.shape[0], dtype=jnp.int32)[None, :], 0), axis=1)
    return source, jnp.any(matches, axis=1)


def place_tiles(block, child_map, row_source, parent_shape, grid_size, row_groups, my_col):
    col_count = block.shape[2] // TILE
    col_ids = jnp.arange(col_count, dtype=jnp.int32) * grid_size + my_col
    col_targets = jnp.take(child_map, col_ids, axis=0) // grid_size
    col_source, col_valid = tile_source(col_targets, parent_shape[1] // TILE)
    row_ids = row_source
    row_targets = jnp.take(child_map, row_ids, axis=0) // row_groups
    row_from, row_valid = tile_source(row_targets, parent_shape[0] // TILE)
    tiles = block.reshape(block.shape[0], TILE, col_count, TILE)
    tiles = jnp.take(tiles, row_from, axis=0)
    tiles = jnp.take(tiles, col_source, axis=2)
    valid = row_valid[:, None, None, None] & col_valid[None, None, :, None]
    return jnp.where(valid, tiles, 0.0).reshape(parent_shape)


def assemble_by_parity(child_done, child_maps, parent_own, grid_size, half_index, my_row, my_col):
    pivot_tiles = CHILD_PIVOTS // TILE
    first_slot = pivot_tiles // grid_size
    update = child_done[first_slot * TILE :, first_slot * TILE :]
    pair_count = update.shape[0] // (2 * TILE)
    by_parity = update.reshape(pair_count, 2, TILE, update.shape[1])
    kept = lax.dynamic_index_in_dim(by_parity, half_index, 1, keepdims=False)
    sent = lax.dynamic_index_in_dim(by_parity, 1 - half_index, 1, keepdims=False)
    received = from_partner(sent, "half", 0)
    pair_ids = jnp.arange(pair_count, dtype=jnp.int32)
    row_update_ids = (2 * pair_ids + half_index) * grid_size + my_row
    own_map = lax.dynamic_index_in_dim(child_maps, half_index, 0, keepdims=False)
    other_map = lax.dynamic_index_in_dim(child_maps, 1 - half_index, 0, keepdims=False)
    row_groups = 2 * grid_size
    kept_part = place_tiles(kept, own_map, row_update_ids, parent_own.shape, grid_size, row_groups, my_col)
    got_part = place_tiles(received, other_map, row_update_ids, parent_own.shape, grid_size, row_groups, my_col)
    return parent_own + kept_part + got_part


def factor_parent(front_work, grid_size, half_index, my_row, my_col):
    row_groups = 2 * grid_size
    parent_row = half_index * grid_size + my_row
    row_count, col_count = front_work.shape
    column = copy_from(front_work[:, :TILE], "col", 0)
    partner = from_partner(column, "half", 0)
    first = half_index == 0
    halves = jnp.stack([jnp.where(first, column, partner), jnp.where(first, partner, column)])
    halves = halves.reshape(2, row_count // TILE, TILE, TILE)
    my_row_cols = jnp.swapaxes(halves, 0, 1).reshape(col_count, TILE)
    pairs = [
        (col * grid_size + row, row * grid_size + col)
        for row in range(grid_size)
        for col in range(grid_size)
    ]
    my_cols = lax.ppermute(my_row_cols, ("row", "col"), pairs)
    diag_block = copy_from(my_row_cols[:TILE], "row", 0)
    diag_factor = jnp.tril(jnp.linalg.cholesky(diag_block))
    eye = jnp.eye(TILE, dtype=jnp.float32)
    inverse = jnp.tril(jax.scipy.linalg.solve_triangular(diag_factor, eye, lower=True))
    solved_rows = jnp.dot(column, inverse.T, precision=lax.Precision.HIGH)
    solved_cols = jnp.dot(my_cols, inverse.T, precision=lax.Precision.HIGH)
    row_within = jnp.arange(row_count, dtype=jnp.int32)
    col_within = jnp.arange(col_count, dtype=jnp.int32)
    row_index = row_within // TILE * row_groups * TILE + parent_row * TILE + row_within % TILE
    col_index = col_within // TILE * grid_size * TILE + my_col * TILE + col_within % TILE
    return finish_front(front_work, solved_rows, solved_cols, diag_factor, row_index, col_index, TILE)


def finish_front(front_work, solved_rows, solved_cols, diag_factor, row_index, col_index, pivot_count):
    width = TILE * (-(-pivot_count // TILE))
    rows_after = (row_index >= pivot_count)[:, None]
    cols_after = (col_index >= pivot_count)[None, :]
    update = jnp.dot(
        jnp.where(rows_after, solved_rows, 0.0),
        jnp.where(cols_after.T, solved_cols, 0.0).T,
        precision=lax.Precision.HIGH,
        preferred_element_type=jnp.float32,
    )
    diag_rows = jnp.take(diag_factor, jnp.minimum(row_index, pivot_count - 1), axis=0)
    full_rows = jnp.where(rows_after, solved_rows, diag_rows)
    pivot_cols = jnp.take(full_rows, jnp.minimum(col_index[:width], pivot_count - 1), axis=1)
    trailing = jnp.where(rows_after & cols_after, front_work - update, 0.0)
    head = jnp.where(cols_after[:, :width], trailing[:, :width], pivot_cols)
    return jnp.concatenate([head, trailing[:, width:]], axis=1)


def local(child_fronts, child_maps, parent_own):
    grid_size = lax.axis_size("row")
    half_index = lax.axis_index("half")
    my_row = lax.axis_index("row")
    my_col = lax.axis_index("col")

    child_done = factor_child(child_fronts[0], CHILD_PIVOTS, grid_size, my_row, my_col)
    pivot_tiles = CHILD_PIVOTS // TILE
    first_slot = pivot_tiles // grid_size
    update_slots = child_done.shape[0] // TILE - first_slot
    parity_fits = CYCLE_TILES % (2 * grid_size) == 0 and pivot_tiles % grid_size == 0
    parity_fits = parity_fits and first_slot % 2 == 0 and update_slots % 2 == 0
    if not parity_fits:
        parent_start = assemble_by_einsum(
            child_done, child_maps, parent_own, grid_size, half_index, my_row, my_col
        )
    else:
        parent_start = assemble_by_parity(
            child_done, child_maps, parent_own, grid_size, half_index, my_row, my_col
        )

    parent_done = factor_parent(parent_start, grid_size, half_index, my_row, my_col)
    return (child_done[None], parent_done)


def solution(mesh):
    in_specs = (P("half", "row", "col"), P(), P(("half", "row"), "col"))
    out_specs = (P("half", "row", "col"), P(("half", "row"), "col"))
    return jax.shard_map(local, mesh=mesh, in_specs=in_specs, out_specs=out_specs, check_vma=False)
```

```python
import jax
import jax.numpy as jnp
from jax import lax
from jax.sharding import PartitionSpec as P

TILE = 128
CHILD_PIVOTS = 1024
PARENT_PIVOTS = 128
CYCLE_TILES = 16


def spread(shard, axis, root):
    mine = lax.axis_index(axis) == root
    return lax.psum(jnp.where(mine, shard, jnp.zeros_like(shard)), axis)


def copy_from(shard, axis, root):
    size = lax.axis_size(axis)
    mine = lax.axis_index(axis) == root
    total = jnp.where(mine, shard, jnp.zeros_like(shard))
    for target in range(size):
        if target != root:
            total = total + lax.ppermute(shard, axis, [(root, target)])
    return total


def from_partner(shard, axis, distance):
    return lax.ppermute(shard, axis, [(i, i ^ 1 << distance) for i in range(lax.axis_size(axis))])


def pivot_order(pieces, slot_count, tile_count):
    group_count, rest = pieces.shape[0], pieces.shape[2:]
    shaped = pieces.reshape((group_count, slot_count, TILE) + rest)
    shaped = jnp.moveaxis(shaped, 0, 1).reshape((slot_count * group_count * TILE,) + rest)
    return shaped[: tile_count * TILE]


def factor_pivots(block):
    order = block.shape[0]
    count = order // TILE
    eye = jnp.eye(TILE, dtype=jnp.float32)
    work = block
    columns = []
    inverses = []
    for step in range(count):
        factor = jnp.tril(jnp.linalg.cholesky(work[:TILE, :TILE]))
        inverse = jnp.tril(jax.scipy.linalg.solve_triangular(factor, eye, lower=True))
        panel = jnp.dot(
            work[TILE:, :TILE], inverse.T, precision=lax.Precision.HIGH,
            preferred_element_type=jnp.float32,
        )
        work = work[TILE:, TILE:] - jnp.dot(
            panel, panel.T, precision=lax.Precision.HIGH, preferred_element_type=jnp.float32
        )
        columns.append(jnp.concatenate([jnp.zeros((step * TILE, TILE), jnp.float32), factor, panel]))
        inverses.append(inverse)
    return jnp.concatenate(columns, axis=1), jnp.stack(inverses)


def lower_inverse(factor, inverse):
    order = factor.shape[0]
    size = TILE
    while size < order:
        pairs = order // size // 2
        halves = inverse.reshape(pairs, 2, size, size)
        first, second = halves[:, 0], halves[:, 1]
        lower = jnp.stack(
            [
                factor[(2 * pair + 1) * size : (2 * pair + 2) * size, 2 * pair * size : (2 * pair + 1) * size]
                for pair in range(pairs)
            ]
        )
        mixed = jnp.einsum("kab,kbc->kac", second, lower, precision=lax.Precision.HIGH)
        mixed = -jnp.einsum("kab,kbc->kac", mixed, first, precision=lax.Precision.HIGH)
        top = jnp.concatenate([first, jnp.zeros_like(first)], axis=2)
        bottom = jnp.concatenate([mixed, second], axis=2)
        inverse = jnp.concatenate([top, bottom], axis=1)
        size *= 2
    return inverse[0]


def factor_child(front_work, pivot_count, grid_size, my_row, my_col):
    local_count = front_work.shape[0]
    tile_count = pivot_count // TILE
    slot_count = -(-tile_count // grid_size)
    width = slot_count * TILE
    diag_pieces = lax.all_gather(front_work[:width, :width], ("row", "col"), axis=0)
    diag_block = diag_pieces.reshape(grid_size, grid_size, slot_count, TILE, slot_count, TILE)
    diag_block = diag_block.transpose(2, 0, 3, 4, 1, 5).reshape(slot_count * grid_size * TILE, -1)
    diag_block = diag_block[:pivot_count, :pivot_count]
    diag_factor, block_inverses = factor_pivots(diag_block)
    if tile_count & (tile_count - 1):
        eye = jnp.eye(pivot_count, dtype=jnp.float32)
        diag_inverse = jnp.tril(jax.scipy.linalg.solve_triangular(diag_factor, eye, lower=True))
    else:
        diag_inverse = lower_inverse(diag_factor, block_inverses)
    skip = width if tile_count % grid_size == 0 else 0
    kept_count = local_count - skip
    col_pieces = lax.all_gather(front_work[skip:, :width].T, "col", axis=0)
    panel_rows = pivot_order(col_pieces, slot_count, tile_count)
    row_pieces = lax.all_gather(front_work[:width, skip:], "row", axis=0)
    panel_cols = pivot_order(row_pieces, slot_count, tile_count)
    if slot_count * grid_size == tile_count:
        gathered_inverse = diag_inverse.reshape(pivot_count, slot_count, grid_size, TILE)
        gathered_inverse = gathered_inverse.swapaxes(1, 2).reshape(pivot_count, pivot_count)
        solved_by_rows = jnp.dot(
            gathered_inverse, col_pieces.reshape(pivot_count, kept_count),
            precision=lax.Precision.HIGH, preferred_element_type=jnp.float32,
        )
        solved_by_cols = jnp.dot(
            gathered_inverse, row_pieces.reshape(pivot_count, kept_count),
            precision=lax.Precision.HIGH, preferred_element_type=jnp.float32,
        )
    else:
        both = jnp.concatenate([panel_rows, panel_cols], axis=1)
        solved = jnp.dot(
            diag_inverse, both, precision=lax.Precision.HIGH, preferred_element_type=jnp.float32
        )
        solved_by_rows = solved[:, :kept_count]
        solved_by_cols = solved[:, kept_count:]
    lead = jnp.zeros((skip, pivot_count), jnp.float32)
    solved_rows = jnp.concatenate([lead, solved_by_rows.T])
    solved_cols = jnp.concatenate([lead, solved_by_cols.T])
    within = jnp.arange(local_count, dtype=jnp.int32)
    row_index = within // TILE * grid_size * TILE + my_row * TILE + within % TILE
    col_index = within // TILE * grid_size * TILE + my_col * TILE + within % TILE
    rows_after = (row_index >= pivot_count)[:, None]
    cols_after = (col_index >= pivot_count)[None, :]
    if skip:
        col_pick = jnp.minimum(col_index[:width], pivot_count - 1)
        top_rows = jnp.take(diag_factor, jnp.minimum(row_index[:skip], pivot_count - 1), axis=0)
        top = jnp.take(top_rows, col_pick, axis=1)
        below = jnp.take(solved_by_rows, col_pick, axis=0).T
        pivot_cols = jnp.concatenate([top, below])
        core = front_work[skip:, skip:] - jnp.dot(
            solved_by_rows.T, solved_by_cols, precision=lax.Precision.HIGH,
            preferred_element_type=jnp.float32,
        )
        right = jnp.concatenate([jnp.zeros((skip, kept_count), jnp.float32), core])
        return jnp.concatenate([pivot_cols, right], axis=1)
    diag_rows = jnp.take(diag_factor, jnp.minimum(row_index, pivot_count - 1), axis=0)
    full_rows = jnp.where(rows_after, solved_rows, diag_rows)
    pivot_cols = jnp.take(full_rows, jnp.minimum(col_index[:width], pivot_count - 1), axis=1)
    update = jnp.dot(
        jnp.where(rows_after, solved_rows, 0.0),
        jnp.where(cols_after.T, solved_cols, 0.0).T,
        precision=lax.Precision.HIGH,
        preferred_element_type=jnp.float32,
    )
    trailing = jnp.where(rows_after & cols_after, front_work - update, 0.0)
    head = jnp.where(cols_after[:, :width], trailing[:, :width], pivot_cols)
    return jnp.concatenate([head, trailing[:, width:]], axis=1)


def assemble_by_einsum(child_done, child_maps, parent_own, grid_size, half_index, my_row, my_col):
    local_tiles = child_done.shape[0] // TILE
    pivot_tiles = CHILD_PIVOTS // TILE
    own_map = lax.dynamic_index_in_dim(child_maps, half_index, 0, keepdims=False)
    update_count = child_maps.shape[1]
    slot_ids = jnp.arange(local_tiles, dtype=jnp.int32)
    update_range = jnp.arange(update_count, dtype=jnp.int32)

    def parent_tile(offset):
        update_ids = slot_ids * grid_size + offset - pivot_tiles
        matches = update_ids[:, None] == update_range[None, :]
        return (jnp.sum(jnp.where(matches, own_map[None, :], 0), axis=1), update_ids >= 0)

    row_target, row_valid = parent_tile(my_row)
    col_target, col_valid = parent_tile(my_col)
    parent_row_tiles = parent_own.shape[0] // TILE
    parent_col_tiles = parent_own.shape[1] // TILE
    row_dest = (
        jnp.arange(parent_row_tiles, dtype=jnp.int32)[None, :] * (2 * grid_size)
        + jnp.arange(2, dtype=jnp.int32)[:, None] * grid_size
        + my_row
    )
    row_place = (
        (row_dest[:, :, None] == row_target[None, None, :]) & row_valid[None, None, :]
    ).astype(jnp.float32)
    col_dest = jnp.arange(parent_col_tiles, dtype=jnp.int32) * grid_size + my_col
    col_place = ((col_dest[:, None] == col_target[None, :]) & col_valid[None, :]).astype(
        jnp.float32
    )
    blocks = child_done.reshape(local_tiles, TILE, local_tiles, TILE)
    rows_moved = jnp.einsum("hak,kilj->hailj", row_place, blocks, precision=lax.Precision.HIGHEST)
    both_moved = jnp.einsum(
        "hailj,bl->haibj", rows_moved, col_place, precision=lax.Precision.HIGHEST
    )
    both_moved = both_moved.reshape(2, parent_own.shape[0], parent_own.shape[1])
    kept_part = lax.dynamic_index_in_dim(both_moved, half_index, 0, keepdims=False)
    sent_part = lax.dynamic_index_in_dim(both_moved, 1 - half_index, 0, keepdims=False)
    received = from_partner(sent_part, "half", 0)
    return parent_own + kept_part + received


def tile_source(targets, slot_total):
    slots = jnp.arange(slot_total, dtype=jnp.int32)
    matches = targets[None, :] == slots[:, None]
    source = jnp.sum(jnp.where(matches, jnp.arange(targets.shape[0], dtype=jnp.int32)[None, :], 0), axis=1)
    return source, jnp.any(matches, axis=1)


def place_tiles(block, child_map, row_source, parent_shape, grid_size, row_groups, my_col):
    col_count = block.shape[2] // TILE
    col_ids = jnp.arange(col_count, dtype=jnp.int32) * grid_size + my_col
    col_targets = jnp.take(child_map, col_ids, axis=0) // grid_size
    col_source, col_valid = tile_source(col_targets, parent_shape[1] // TILE)
    row_ids = row_source
    row_targets = jnp.take(child_map, row_ids, axis=0) // row_groups
    row_from, row_valid = tile_source(row_targets, parent_shape[0] // TILE)
    tiles = block.reshape(block.shape[0], TILE, col_count, TILE)
    tiles = jnp.take(tiles, row_from, axis=0)
    tiles = jnp.take(tiles, col_source, axis=2)
    valid = row_valid[:, None, None, None] & col_valid[None, None, :, None]
    return jnp.where(valid, tiles, 0.0).reshape(parent_shape)


def assemble_by_parity(child_done, child_maps, parent_own, grid_size, half_index, my_row, my_col):
    pivot_tiles = CHILD_PIVOTS // TILE
    first_slot = pivot_tiles // grid_size
    update = child_done[first_slot * TILE :, first_slot * TILE :]
    pair_count = update.shape[0] // (2 * TILE)
    by_parity = update.reshape(pair_count, 2, TILE, update.shape[1])
    kept = lax.dynamic_index_in_dim(by_parity, half_index, 1, keepdims=False)
    sent = lax.dynamic_index_in_dim(by_parity, 1 - half_index, 1, keepdims=False)
    received = from_partner(sent, "half", 0)
    pair_ids = jnp.arange(pair_count, dtype=jnp.int32)
    row_update_ids = (2 * pair_ids + half_index) * grid_size + my_row
    own_map = lax.dynamic_index_in_dim(child_maps, half_index, 0, keepdims=False)
    other_map = lax.dynamic_index_in_dim(child_maps, 1 - half_index, 0, keepdims=False)
    row_groups = 2 * grid_size
    kept_part = place_tiles(kept, own_map, row_update_ids, parent_own.shape, grid_size, row_groups, my_col)
    got_part = place_tiles(received, other_map, row_update_ids, parent_own.shape, grid_size, row_groups, my_col)
    return parent_own + kept_part + got_part


def factor_parent(front_work, grid_size, half_index, my_row, my_col):
    row_groups = 2 * grid_size
    parent_row = half_index * grid_size + my_row
    row_count, col_count = front_work.shape
    column = copy_from(front_work[:, :TILE], "col", 0)
    partner = from_partner(column, "half", 0)
    first = half_index == 0
    halves = jnp.stack([jnp.where(first, column, partner), jnp.where(first, partner, column)])
    halves = halves.reshape(2, row_count // TILE, TILE, TILE)
    my_row_cols = jnp.swapaxes(halves, 0, 1).reshape(col_count, TILE)
    pairs = [
        (col * grid_size + row, row * grid_size + col)
        for row in range(grid_size)
        for col in range(grid_size)
    ]
    my_cols = lax.ppermute(my_row_cols, ("row", "col"), pairs)
    diag_block = copy_from(my_row_cols[:TILE], "row", 0)
    diag_factor = jnp.tril(jnp.linalg.cholesky(diag_block))
    eye = jnp.eye(TILE, dtype=jnp.float32)
    inverse = jnp.tril(jax.scipy.linalg.solve_triangular(diag_factor, eye, lower=True))
    solved_rows = jnp.dot(column, inverse.T, precision=lax.Precision.HIGH)
    solved_cols = jnp.dot(my_cols, inverse.T, precision=lax.Precision.HIGH)
    row_within = jnp.arange(row_count, dtype=jnp.int32)
    col_within = jnp.arange(col_count, dtype=jnp.int32)
    row_index = row_within // TILE * row_groups * TILE + parent_row * TILE + row_within % TILE
    col_index = col_within // TILE * grid_size * TILE + my_col * TILE + col_within % TILE
    return finish_front(front_work, solved_rows, solved_cols, diag_factor, row_index, col_index, TILE)


def finish_front(front_work, solved_rows, solved_cols, diag_factor, row_index, col_index, pivot_count):
    width = TILE * (-(-pivot_count // TILE))
    rows_after = (row_index >= pivot_count)[:, None]
    cols_after = (col_index >= pivot_count)[None, :]
    update = jnp.dot(
        jnp.where(rows_after, solved_rows, 0.0),
        jnp.where(cols_after.T, solved_cols, 0.0).T,
        precision=lax.Precision.HIGH,
        preferred_element_type=jnp.float32,
    )
    diag_rows = jnp.take(diag_factor, jnp.minimum(row_index, pivot_count - 1), axis=0)
    full_rows = jnp.where(rows_after, solved_rows, diag_rows)
    pivot_cols = jnp.take(full_rows, jnp.minimum(col_index[:width], pivot_count - 1), axis=1)
    trailing = jnp.where(rows_after & cols_after, front_work - update, 0.0)
    head = jnp.where(cols_after[:, :width], trailing[:, :width], pivot_cols)
    return jnp.concatenate([head, trailing[:, width:]], axis=1)


def local(child_fronts, child_maps, parent_own):
    grid_size = lax.axis_size("row")
    half_index = lax.axis_index("half")
    my_row = lax.axis_index("row")
    my_col = lax.axis_index("col")

    child_done = factor_child(child_fronts[0], CHILD_PIVOTS, grid_size, my_row, my_col)
    pivot_tiles = CHILD_PIVOTS // TILE
    first_slot = pivot_tiles // grid_size
    update_slots = child_done.shape[0] // TILE - first_slot
    parity_fits = CYCLE_TILES % (2 * grid_size) == 0 and pivot_tiles % grid_size == 0
    parity_fits = parity_fits and first_slot % 2 == 0 and update_slots % 2 == 0
    if not parity_fits:
        parent_start = assemble_by_einsum(
            child_done, child_maps, parent_own, grid_size, half_index, my_row, my_col
        )
    else:
        parent_start = assemble_by_parity(
            child_done, child_maps, parent_own, grid_size, half_index, my_row, my_col
        )

    parent_done = factor_parent(parent_start, grid_size, half_index, my_row, my_col)
    return (child_done[None], parent_done)


def solution(mesh):
    in_specs = (P("half", "row", "col"), P(), P(("half", "row"), "col"))
    out_specs = (P("half", "row", "col"), P(("half", "row"), "col"))
    return jax.shard_map(local, mesh=mesh, in_specs=in_specs, out_specs=out_specs, check_vma=False)
```
